32 devices in a mesh: ctx: 8 (over z, core), head: 4 (over y, x).
Axes of the slice: x: 2, y: 2, z: 4, core: 2. Of those that a mesh axis runs over, the one named last changes fastest.
Arguments:
- queries: bfloat16 [4096, 4096], P('ctx', 'head'), may hold values from -6 to 6
- keys: bfloat16 [4096, 4096], P('ctx', 'head'), may hold values from -6 to 6
- values: bfloat16 [4096, 4096], P('ctx', 'head'), may hold values from -6 to 6
- output_grad: bfloat16 [4096, 4096], P('ctx', 'head'), may hold values from -0.09375 to 0.09375
- out_weight: bfloat16 [4096, 4096], P('head'), may hold values from -0.09375 to 0.09375
Outputs:
- grad_queries: bfloat16 [4096, 4096], P('ctx', 'head')
- grad_keys: bfloat16 [4096, 4096], P('ctx', 'head')
- grad_values: bfloat16 [4096, 4096], P('ctx', 'head')
The draws below stay inside these ranges and needn't reach their ends.
All inputs are finite; a program needn't handle non-finite values.
Results may differ from the reference program's by a relative error of at most 0.01.
Values may be sent and summed in bfloat16 or wider, within the bound.
No kernel may reach another device: no remote copies, remote signals or barrier semaphores. Data moves between devices by JAX's collectives and lax.ppermute only.
A program may use at most 64 MiB of HBM per device.

```python
import jax
import jax.numpy as jnp
from jax import lax

D = 4096
H = 32
DH = 128
TOK_DEV = 512
TOKENS = 4096


def block_scale(rng, dims, cuts, low, high):
    loudness = 1.0
    for position, parts in cuts:
        steps = jax.random.uniform(jax.random.fold_in(jax.random.fold_in(rng, 6), position), (parts,), jnp.float32, low / len(cuts), high / len(cuts))
        loudness = loudness * jnp.repeat(jnp.exp(steps), dims[position] // parts).reshape((-1,) + (1,) * (len(dims) - 1 - position))
    return loudness


def centred(key, extent, width, limit, cuts=(), dtype=jnp.bfloat16):
    array = jax.random.normal(key, extent, jnp.float32) * width
    if len(cuts) > 0:
        array = block_scale(key, extent, cuts, -0.22, 0.18) * array
    return jnp.clip(array, min=-limit, max=limit).astype(dtype)


def setup_inputs(seed: int = 0) -> dict:
    streams_of = jax.random.split(jax.random.key(seed), 6)
    return {
        "queries": centred(streams_of[0], (TOKENS, H * DH), 1.0, 6.0, ((0, 8), (1, 4))),
        "keys": centred(streams_of[1], (TOKENS, H * DH), 1.0, 6.0, ((0, 8), (1, 4))),
        "values": centred(streams_of[2], (TOKENS, H * DH), 1.0, 6.0, ((0, 8), (1, 4))),
        "output_grad": centred(streams_of[3], (TOKENS, D), (TOKENS ** -0.5), 0.09375, ((0, 8), (1, 4))),
        "out_weight": centred(streams_of[4], (H * DH, D), D ** -0.5, 0.09375, ((0, 4),)),
    }


def rounded(x):
    return lax.optimization_barrier(x.astype(jnp.bfloat16)).astype(jnp.float32)


def reference(queries, keys, values, output_grad, out_weight):
    scale_factor = DH ** -0.5
    highest = lax.Precision.HIGHEST
    grad_heads = jnp.dot(output_grad, out_weight.T, preferred_element_type=jnp.float32).astype(jnp.bfloat16)
    block_len = min(TOK_DEV, 512)
    count = TOKENS // block_len

    def split(x):
        return x.reshape(count, block_len, H, DH).astype(jnp.float32)

    q_blocks = split(queries)
    k_blocks = split(keys)
    v_blocks = split(values)
    g_blocks = split(grad_heads)
    rows = jnp.arange(block_len)
    causal = (rows[:, None] >= rows[None, :])[None]
    zeros = jnp.zeros((H, DH, DH), jnp.float32)

    def forward(state, blocks):
        qb, kb, vb, gb = blocks
        scores = jnp.einsum('the,she->hts', gb, vb, precision=highest) * scale_factor
        scores = rounded(jnp.where(causal, scores, 0.0))
        grad_q = jnp.einsum('hts,shd->thd', scores, kb, precision=highest)
        grad_q = grad_q + scale_factor * jnp.einsum('the,hde->thd', gb, state, precision=highest)
        state = state + jnp.einsum('shd,she->hde', kb, vb, precision=highest)
        return state, grad_q.astype(jnp.bfloat16)

    def backward(state, blocks):
        qb, kb, vb, gb = blocks
        score_grad = jnp.einsum('the,she->hts', gb, vb, precision=highest) * scale_factor
        score_grad = rounded(jnp.where(causal, score_grad, 0.0))
        score_fwd = jnp.einsum('thd,shd->hts', qb, kb, precision=highest) * scale_factor
        score_fwd = rounded(jnp.where(causal, score_fwd, 0.0))
        grad_k = jnp.einsum('hts,thd->shd', score_grad, qb, precision=highest)
        grad_k = grad_k + scale_factor * jnp.einsum('she,hde->shd', vb, state, precision=highest)
        grad_v = jnp.einsum('hts,the->she', score_fwd, gb, precision=highest)
        grad_v = grad_v + scale_factor * jnp.einsum('shd,hde->she', kb, state, precision=highest)
        state = state + jnp.einsum('thd,the->hde', qb, gb, precision=highest)
        return state, (grad_k.astype(jnp.bfloat16), grad_v.astype(jnp.bfloat16))

    inputs = (q_blocks, k_blocks, v_blocks, g_blocks)
    _, grad_q = lax.scan(forward, zeros, inputs)
    _, (grad_k, grad_v) = lax.scan(backward, zeros, inputs, reverse=True)
    shape = (TOKENS, H * DH)
    return grad_q.reshape(shape), grad_k.reshape(shape), grad_v.reshape(shape)
```

```python
import jax
import jax.numpy as jnp
from jax import lax
from jax.sharding import PartitionSpec as P

DH = 128


def flip_pairs(n, bit):
    return [(a, a ^ bit) for a in range(n)]


def project(og, out_weight, head_size):
    cols = og.shape[1]

    def weight_cols(source, lo, width):
        return lax.dynamic_slice_in_dim(out_weight, source * cols + lo, width, axis=1)

    def mm(a, b):
        return lax.dot_general(
            a, b, (((1,), (1,)), ((), ())), preferred_element_type=jnp.float32
        )

    if head_size != 4:
        full = lax.all_gather(og, "head", axis=1, tiled=True)
        return mm(full, out_weight)
    me = lax.axis_index("head")
    half = cols // 2
    from_x = lax.ppermute(og, "head", flip_pairs(4, 1))
    from_y = lax.ppermute(og, "head", flip_pairs(4, 2))
    diag_a = lax.ppermute(from_x[:, :half], "head", flip_pairs(4, 2))
    diag_b = lax.ppermute(from_y[:, half:], "head", flip_pairs(4, 1))
    acc = mm(og, weight_cols(me, 0, cols))
    acc = acc + mm(from_x, weight_cols(me ^ 1, 0, cols))
    acc = acc + mm(from_y, weight_cols(me ^ 2, 0, cols))
    acc = acc + mm(diag_a, weight_cols(me ^ 3, 0, half))
    acc = acc + mm(diag_b, weight_cols(me ^ 3, half, half))
    return acc


def ctx_exclusive(state, ctx_size, reverse):
    p = lax.axis_index("ctx")
    core = p % 2
    chips = ctx_size // 2
    rounded = state.astype(jnp.bfloat16)
    partner = lax.ppermute(rounded, "ctx", flip_pairs(ctx_size, 1))
    chip_sum = rounded.astype(jnp.float32) + partner.astype(jnp.float32)
    half = state.shape[1] // 2
    mine = lax.dynamic_slice_in_dim(chip_sum, core * half, half, axis=1)
    run = mine
    others = jnp.zeros_like(mine)
    step = 1
    while step < chips:
        if reverse:
            pairs = [(2 * (z + step) + c, 2 * z + c) for z in range(chips - step) for c in range(2)]
        else:
            pairs = [(2 * z + c, 2 * (z + step) + c) for z in range(chips - step) for c in range(2)]
        got = lax.ppermute(run.astype(jnp.bfloat16), "ctx", pairs).astype(jnp.float32)
        run = run + got
        others = others + got
        step *= 2
    theirs = lax.ppermute(others, "ctx", flip_pairs(ctx_size, 1))
    lower = jnp.where(core == 0, others, theirs)
    upper = jnp.where(core == 0, theirs, others)
    chips_side = jnp.concatenate([lower, upper], axis=1)
    same_chip = (core == 0) if reverse else (core == 1)
    return chips_side + jnp.where(same_chip, partner.astype(jnp.float32), 0.0)


def make_shards(ctx_size, head_size):
    def shards(queries, keys, values, output_grad, out_weight):
        row_count = queries.shape[0]
        width = queries.shape[1]
        heads = width // DH
        block_len = min(row_count, 512)
        blocks = row_count // block_len
        scale_factor = DH ** (-0.5)
        highest = lax.Precision.HIGHEST
        shape = (blocks, block_len, heads, DH)
        q_blocks = queries.reshape(shape)
        k_blocks = keys.reshape(shape)
        v_blocks = values.reshape(shape)
        kv_blocks = jnp.einsum(
            "nshd,nshe->nhde", k_blocks, v_blocks, preferred_element_type=jnp.float32
        )
        kv_running = jnp.cumsum(kv_blocks, axis=0)
        kv_before = ctx_exclusive(kv_running[-1], ctx_size, False)
        kv_entry = kv_before[None] + kv_running - kv_blocks
        rows = jnp.arange(block_len)
        causal = (rows[:, None] >= rows[None, :])[None, None]
        score_fwd = (
            jnp.einsum("nthd,nshd->nhts", q_blocks, k_blocks, preferred_element_type=jnp.float32)
            * scale_factor
        )
        score_fwd = jnp.where(causal, score_fwd, 0.0).astype(jnp.bfloat16)

        grad_heads = project(output_grad, out_weight, head_size).astype(jnp.bfloat16)
        g_blocks = grad_heads.reshape(shape)
        qg_blocks = jnp.einsum(
            "nthd,nthe->nhde", q_blocks, g_blocks, preferred_element_type=jnp.float32
        )
        qg_running = jnp.flip(jnp.cumsum(jnp.flip(qg_blocks, 0), axis=0), 0)
        qg_after = ctx_exclusive(qg_running[0], ctx_size, True)
        qg_entry = qg_after[None] + qg_running - qg_blocks

        score_grad = (
            jnp.einsum("nthe,nshe->nhts", g_blocks, v_blocks, preferred_element_type=jnp.float32)
            * scale_factor
        )
        score_grad = jnp.where(causal, score_grad, 0.0).astype(jnp.bfloat16)
        grad_q = jnp.einsum("nhts,nshd->nthd", score_grad, k_blocks, preferred_element_type=jnp.float32)
        grad_q = grad_q + scale_factor * jnp.einsum(
            "nthe,nhde->nthd", g_blocks.astype(jnp.float32), kv_entry, precision=highest
        )
        grad_k = jnp.einsum("nhts,nthd->nshd", score_grad, q_blocks, preferred_element_type=jnp.float32)
        grad_k = grad_k + scale_factor * jnp.einsum(
            "nshe,nhde->nshd", v_blocks.astype(jnp.float32), qg_entry, precision=highest
        )
        grad_v = jnp.einsum("nhts,nthe->nshe", score_fwd, g_blocks, preferred_element_type=jnp.float32)
        grad_v = grad_v + scale_factor * jnp.einsum(
            "nshd,nhde->nshe", k_blocks.astype(jnp.float32), qg_entry, precision=highest
        )
        flat = (row_count, width)
        return (
            grad_q.reshape(flat).astype(jnp.bfloat16),
            grad_k.reshape(flat).astype(jnp.bfloat16),
            grad_v.reshape(flat).astype(jnp.bfloat16),
        )

    return shards


def solution(mesh):
    return jax.shard_map(
        make_shards(mesh.shape["ctx"], mesh.shape["head"]),
        mesh=mesh,
        in_specs=(
            P("ctx", "head"),
            P("ctx", "head"),
            P("ctx", "head"),
            P("ctx", "head"),
            P("head", None),
        ),
        out_specs=(P("ctx", "head"), P("ctx", "head"), P("ctx", "head")),
        check_vma=False,
    )
```

```python
import jax
import jax.numpy as jnp
from jax import lax
from jax.sharding import PartitionSpec as P

DH = 128


def flip_pairs(n, bit):
    return [(a, a ^ bit) for a in range(n)]


def project(og, out_weight, head_size, tied):
    cols = og.shape[1]

    def weight_cols(source, lo, width):
        return lax.dynamic_slice_in_dim(out_weight, source * cols + lo, width, axis=1)

    def mm(a, b):
        return lax.dot_general(
            a, b, (((1,), (1,)), ((), ())), preferred_element_type=jnp.float32
        )

    if head_size != 4:
        full = lax.all_gather(og, "head", axis=1, tiled=True)
        full, tied = lax.optimization_barrier((full, tied))
        return mm(full, out_weight), tied
    me = lax.axis_index("head")
    half = cols // 2
    from_x = lax.ppermute(og, "head", flip_pairs(4, 1))
    from_y = lax.ppermute(og, "head", flip_pairs(4, 2))
    from_x, from_y, tied = lax.optimization_barrier((from_x, from_y, tied))
    diag_a = lax.ppermute(from_x[:, :half], "head", flip_pairs(4, 2))
    diag_b = lax.ppermute(from_y[:, half:], "head", flip_pairs(4, 1))
    acc = mm(og, weight_cols(me, 0, cols))
    acc = acc + mm(from_x, weight_cols(me ^ 1, 0, cols))
    acc = acc + mm(from_y, weight_cols(me ^ 2, 0, cols))
    acc = acc + mm(diag_a, weight_cols(me ^ 3, 0, half))
    acc = acc + mm(diag_b, weight_cols(me ^ 3, half, half))
    return acc, tied


def ctx_exclusive(state, ctx_size, reverse):
    p = lax.axis_index("ctx")
    core = p % 2
    chips = ctx_size // 2
    rounded = state.astype(jnp.bfloat16)
    partner = lax.ppermute(rounded, "ctx", flip_pairs(ctx_size, 1))
    chip_sum = rounded.astype(jnp.float32) + partner.astype(jnp.float32)
    half = state.shape[1] // 2
    mine = lax.dynamic_slice_in_dim(chip_sum, core * half, half, axis=1)
    others = jnp.zeros_like(mine)
    if chips <= 4:
        sent = mine.astype(jnp.bfloat16)
        for step in range(1, chips):
            if reverse:
                pairs = [(2 * (z + step) + c, 2 * z + c) for z in range(chips - step) for c in range(2)]
            else:
                pairs = [(2 * z + c, 2 * (z + step) + c) for z in range(chips - step) for c in range(2)]
            others = others + lax.ppermute(sent, "ctx", pairs).astype(jnp.float32)
    else:
        run = mine
        step = 1
        while step < chips:
            if reverse:
                pairs = [(2 * (z + step) + c, 2 * z + c) for z in range(chips - step) for c in range(2)]
            else:
                pairs = [(2 * z + c, 2 * (z + step) + c) for z in range(chips - step) for c in range(2)]
            got = lax.ppermute(run.astype(jnp.bfloat16), "ctx", pairs).astype(jnp.float32)
            run = run + got
            others = others + got
            step *= 2
    theirs = lax.ppermute(others, "ctx", flip_pairs(ctx_size, 1))
    lower = jnp.where(core == 0, others, theirs)
    upper = jnp.where(core == 0, theirs, others)
    chips_side = jnp.concatenate([lower, upper], axis=1)
    same_chip = (core == 0) if reverse else (core == 1)
    return chips_side + jnp.where(same_chip, partner.astype(jnp.float32), 0.0)


def state_mm(spec, x, state):
    high = state.astype(jnp.bfloat16)
    low = (state - high.astype(jnp.float32)).astype(jnp.bfloat16)
    return jnp.einsum(spec, x, high, preferred_element_type=jnp.float32) + jnp.einsum(
        spec, x, low, preferred_element_type=jnp.float32
    )


def make_shards(ctx_size, head_size):
    def shards(queries, keys, values, output_grad, out_weight):
        row_count = queries.shape[0]
        width = queries.shape[1]
        heads = width // DH
        block_len = min(row_count, 512)
        blocks = row_count // block_len
        scale_factor = DH ** (-0.5)
        shape = (blocks, block_len, heads, DH)
        q_blocks = queries.reshape(shape)
        k_blocks = keys.reshape(shape)
        v_blocks = values.reshape(shape)
        grad_heads, (k_tied, v_tied) = project(output_grad, out_weight, head_size, (keys, values))
        grad_heads = grad_heads.astype(jnp.bfloat16)
        kv_blocks = jnp.einsum(
            "nshd,nshe->nhde", k_tied.reshape(shape), v_tied.reshape(shape),
            preferred_element_type=jnp.float32,
        )
        kv_running = jnp.cumsum(kv_blocks, axis=0)
        kv_before = ctx_exclusive(kv_running[-1], ctx_size, False)
        kv_entry = kv_before[None] + kv_running - kv_blocks
        rows = jnp.arange(block_len)
        causal = (rows[:, None] >= rows[None, :])[None, None]
        score_fwd = (
            jnp.einsum("nthd,nshd->nhts", q_blocks, k_blocks, preferred_element_type=jnp.float32)
            * scale_factor
        )
        score_fwd = jnp.where(causal, score_fwd, 0.0).astype(jnp.bfloat16)

        g_blocks = grad_heads.reshape(shape)
        qg_blocks = jnp.einsum(
            "nthd,nthe->nhde", q_blocks, g_blocks, preferred_element_type=jnp.float32
        )
        qg_running = jnp.flip(jnp.cumsum(jnp.flip(qg_blocks, 0), axis=0), 0)
        qg_after = ctx_exclusive(qg_running[0], ctx_size, True)
        qg_entry = qg_after[None] + qg_running - qg_blocks

        score_grad = (
            jnp.einsum("nthe,nshe->nhts", g_blocks, v_blocks, preferred_element_type=jnp.float32)
            * scale_factor
        )
        score_grad = jnp.where(causal, score_grad, 0.0).astype(jnp.bfloat16)
        grad_q = jnp.einsum("nhts,nshd->nthd", score_grad, k_blocks, preferred_element_type=jnp.float32)
        grad_q = grad_q + state_mm("nthe,nhde->nthd", g_blocks, scale_factor * kv_entry)
        grad_k = jnp.einsum("nhts,nthd->nshd", score_grad, q_blocks, preferred_element_type=jnp.float32)
        grad_k = grad_k + state_mm("nshe,nhde->nshd", v_blocks, scale_factor * qg_entry)
        grad_v = jnp.einsum("nhts,nthe->nshe", score_fwd, g_blocks, preferred_element_type=jnp.float32)
        grad_v = grad_v + state_mm("nshd,nhde->nshe", k_blocks, scale_factor * qg_entry)
        flat = (row_count, width)
        return (
            grad_q.reshape(flat).astype(jnp.bfloat16),
            grad_k.reshape(flat).astype(jnp.bfloat16),
            grad_v.reshape(flat).astype(jnp.bfloat16),
        )

    return shards


def solution(mesh):
    return jax.shard_map(
        make_shards(mesh.shape["ctx"], mesh.shape["head"]),
        mesh=mesh,
        in_specs=(
            P("ctx", "head"),
            P("ctx", "head"),
            P("ctx", "head"),
            P("ctx", "head"),
            P("head", None),
        ),
        out_specs=(P("ctx", "head"), P("ctx", "head"), P("ctx", "head")),
        check_vma=False,
    )
```

```python
import jax
import jax.numpy as jnp
from jax import lax
from jax.sharding import PartitionSpec as P

DH = 128


def flip_pairs(n, bit):
    return [(a, a ^ bit) for a in range(n)]


def project(og, out_weight, ctx_size, head_size, tied):
    cols = og.shape[1]

    def weight_cols(source, lo, width):
        return lax.dynamic_slice_in_dim(out_weight, source * cols + lo, width, axis=1)

    def mm(a, b):
        return lax.dot_general(
            a, b, (((1,), (1,)), ((), ())), preferred_element_type=jnp.float32
        )

    if head_size != 4:
        full = lax.all_gather(og, "head", axis=1, tiled=True)
        full, tied = lax.optimization_barrier((full, tied))
        return mm(full, out_weight), tied
    me = lax.axis_index("head")
    core = lax.axis_index("ctx") % 2
    from_x = lax.ppermute(og, "head", flip_pairs(4, 1))
    from_y = lax.ppermute(og, "head", flip_pairs(4, 2))
    relayed = jnp.where(core == 0, from_x, from_y)
    devices = [(p, j) for p in range(ctx_size) for j in range(4)]
    route = [(p * 4 + j, p * 4 + (j ^ (2 if p % 2 == 0 else 1))) for p, j in devices]
    diag = lax.ppermute(relayed, ("ctx", "head"), route)
    diag, tied = lax.optimization_barrier((diag, tied))
    acc = mm(og, weight_cols(me, 0, cols))
    acc = acc + mm(from_x, weight_cols(me ^ 1, 0, cols))
    acc = acc + mm(from_y, weight_cols(me ^ 2, 0, cols))
    acc = acc + mm(diag, weight_cols(me ^ 3, 0, cols))
    return acc, tied


def ctx_exclusive(state, ctx_size, reverse):
    p = lax.axis_index("ctx")
    core = p % 2
    chips = ctx_size // 2
    rounded = state.astype(jnp.bfloat16)
    partner = lax.ppermute(rounded, "ctx", flip_pairs(ctx_size, 1))
    chip_sum = rounded.astype(jnp.float32) + partner.astype(jnp.float32)
    half = state.shape[1] // 2
    mine = lax.dynamic_slice_in_dim(chip_sum, core * half, half, axis=1)
    others = jnp.zeros_like(mine)
    if chips <= 4:
        sent = mine.astype(jnp.bfloat16)
        for step in range(1, chips):
            if reverse:
                pairs = [(2 * (z + step) + c, 2 * z + c) for z in range(chips - step) for c in range(2)]
            else:
                pairs = [(2 * z + c, 2 * (z + step) + c) for z in range(chips - step) for c in range(2)]
            others = others + lax.ppermute(sent, "ctx", pairs).astype(jnp.float32)
    else:
        run = mine
        step = 1
        while step < chips:
            if reverse:
                pairs = [(2 * (z + step) + c, 2 * z + c) for z in range(chips - step) for c in range(2)]
            else:
                pairs = [(2 * z + c, 2 * (z + step) + c) for z in range(chips - step) for c in range(2)]
            got = lax.ppermute(run.astype(jnp.bfloat16), "ctx", pairs).astype(jnp.float32)
            run = run + got
            others = others + got
            step *= 2
    theirs = lax.ppermute(others, "ctx", flip_pairs(ctx_size, 1))
    lower = jnp.where(core == 0, others, theirs)
    upper = jnp.where(core == 0, theirs, others)
    chips_side = jnp.concatenate([lower, upper], axis=1)
    same_chip = (core == 0) if reverse else (core == 1)
    return chips_side + jnp.where(same_chip, partner.astype(jnp.float32), 0.0)


def state_mm(spec, x, state):
    high = state.astype(jnp.bfloat16)
    low = (state - high.astype(jnp.float32)).astype(jnp.bfloat16)
    return jnp.einsum(spec, x, high, preferred_element_type=jnp.float32) + jnp.einsum(
        spec, x, low, preferred_element_type=jnp.float32
    )


def make_shards(ctx_size, head_size):
    def shards(queries, keys, values, output_grad, out_weight):
        row_count = queries.shape[0]
        width = queries.shape[1]
        heads = width // DH
        block_len = min(row_count, 512)
        blocks = row_count // block_len
        scale_factor = DH ** (-0.5)
        shape = (blocks, block_len, heads, DH)
        q_blocks = queries.reshape(shape)
        k_blocks = keys.reshape(shape)
        v_blocks = values.reshape(shape)
        grad_heads, (k_tied, v_tied) = project(output_grad, out_weight, ctx_size, head_size, (keys, values))
        grad_heads = grad_heads.astype(jnp.bfloat16)
        kv_blocks = jnp.einsum(
            "nshd,nshe->nhde", k_tied.reshape(shape), v_tied.reshape(shape),
            preferred_element_type=jnp.float32,
        )
        kv_running = jnp.cumsum(kv_blocks, axis=0)
        kv_before = ctx_exclusive(kv_running[-1], ctx_size, False)
        kv_entry = kv_before[None] + kv_running - kv_blocks
        rows = jnp.arange(block_len)
        causal = (rows[:, None] >= rows[None, :])[None, None]
        score_fwd = (
            jnp.einsum("nthd,nshd->nhts", q_blocks, k_blocks, preferred_element_type=jnp.float32)
            * scale_factor
        )
        score_fwd = jnp.where(causal, score_fwd, 0.0).astype(jnp.bfloat16)

        g_blocks = grad_heads.reshape(shape)
        qg_blocks = jnp.einsum(
            "nthd,nthe->nhde", q_blocks, g_blocks, preferred_element_type=jnp.float32
        )
        qg_running = jnp.flip(jnp.cumsum(jnp.flip(qg_blocks, 0), axis=0), 0)
        qg_after = ctx_exclusive(qg_running[0], ctx_size, True)
        qg_entry = qg_after[None] + qg_running - qg_blocks

        score_grad = (
            jnp.einsum("nthe,nshe->nhts", g_blocks, v_blocks, preferred_element_type=jnp.float32)
            * scale_factor
        )
        score_grad = jnp.where(causal, score_grad, 0.0).astype(jnp.bfloat16)
        grad_q = jnp.einsum("nhts,nshd->nthd", score_grad, k_blocks, preferred_element_type=jnp.float32)
        grad_q = grad_q + state_mm("nthe,nhde->nthd", g_blocks, scale_factor * kv_entry)
        grad_k = jnp.einsum("nhts,nthd->nshd", score_grad, q_blocks, preferred_element_type=jnp.float32)
        grad_k = grad_k + state_mm("nshe,nhde->nshd", v_blocks, scale_factor * qg_entry)
        grad_v = jnp.einsum("nhts,nthe->nshe", score_fwd, g_blocks, preferred_element_type=jnp.float32)
        grad_v = grad_v + state_mm("nshd,nhde->nshe", k_blocks, scale_factor * qg_entry)
        flat = (row_count, width)
        return (
            grad_q.reshape(flat).astype(jnp.bfloat16),
            grad_k.reshape(flat).astype(jnp.bfloat16),
            grad_v.reshape(flat).astype(jnp.bfloat16),
        )

    return shards


def solution(mesh):
    return jax.shard_map(
        make_shards(mesh.shape["ctx"], mesh.shape["head"]),
        mesh=mesh,
        in_specs=(
            P("ctx", "head"),
            P("ctx", "head"),
            P("ctx", "head"),
            P("ctx", "head"),
            P("head", None),
        ),
        out_specs=(P("ctx", "head"), P("ctx", "head"), P("ctx", "head")),
        check_vma=False,
    )
```

```python
import jax
import jax.numpy as jnp
from jax import lax
from jax.experimental import pallas as pl
from jax.sharding import PartitionSpec as P

DH = 128


def flip_pairs(n, bit):
    return [(a, a ^ bit) for a in range(n)]


def project(og, out_weight, ctx_size, head_size, tied):
    cols = og.shape[1]

    def weight_cols(source, lo, width):
        return lax.dynamic_slice_in_dim(out_weight, source * cols + lo, width, axis=1)

    def mm(a, b):
        return lax.dot_general(
            a, b, (((1,), (1,)), ((), ())), preferred_element_type=jnp.float32
        )

    if head_size != 4:
        full = lax.all_gather(og, "head", axis=1, tiled=True)
        full, tied = lax.optimization_barrier((full, tied))
        return mm(full, out_weight), tied
    me = lax.axis_index("head")
    core = lax.axis_index("ctx") % 2
    from_x = lax.ppermute(og, "head", flip_pairs(4, 1))
    from_y = lax.ppermute(og, "head", flip_pairs(4, 2))
    relayed = jnp.where(core == 0, from_x, from_y)
    devices = [(p, j) for p in range(ctx_size) for j in range(4)]
    route = [(p * 4 + j, p * 4 + (j ^ (2 if p % 2 == 0 else 1))) for p, j in devices]
    diag = lax.ppermute(relayed, ("ctx", "head"), route)
    diag, tied = lax.optimization_barrier((diag, tied))
    acc = mm(og, weight_cols(me, 0, cols))
    acc = acc + mm(from_x, weight_cols(me ^ 1, 0, cols))
    acc = acc + mm(from_y, weight_cols(me ^ 2, 0, cols))
    acc = acc + mm(diag, weight_cols(me ^ 3, 0, cols))
    return acc, tied


def ctx_exclusive(state, ctx_size, reverse):
    p = lax.axis_index("ctx")
    core = p % 2
    chips = ctx_size // 2
    rounded = state.astype(jnp.bfloat16)
    partner = lax.ppermute(rounded, "ctx", flip_pairs(ctx_size, 1))
    chip_sum = rounded.astype(jnp.float32) + partner.astype(jnp.float32)
    half = state.shape[1] // 2
    mine = lax.dynamic_slice_in_dim(chip_sum, core * half, half, axis=1)
    others = jnp.zeros_like(mine)
    if chips <= 4:
        sent = mine.astype(jnp.bfloat16)
        for step in range(1, chips):
            if reverse:
                pairs = [(2 * (z + step) + c, 2 * z + c) for z in range(chips - step) for c in range(2)]
            else:
                pairs = [(2 * z + c, 2 * (z + step) + c) for z in range(chips - step) for c in range(2)]
            others = others + lax.ppermute(sent, "ctx", pairs).astype(jnp.float32)
    else:
        run = mine
        step = 1
        while step < chips:
            if reverse:
                pairs = [(2 * (z + step) + c, 2 * z + c) for z in range(chips - step) for c in range(2)]
            else:
                pairs = [(2 * z + c, 2 * (z + step) + c) for z in range(chips - step) for c in range(2)]
            got = lax.ppermute(run.astype(jnp.bfloat16), "ctx", pairs).astype(jnp.float32)
            run = run + got
            others = others + got
            step *= 2
    theirs = lax.ppermute(others, "ctx", flip_pairs(ctx_size, 1))
    lower = jnp.where(core == 0, others, theirs)
    upper = jnp.where(core == 0, theirs, others)
    chips_side = jnp.concatenate([lower, upper], axis=1)
    same_chip = (core == 0) if reverse else (core == 1)
    return chips_side + jnp.where(same_chip, partner.astype(jnp.float32), 0.0)


NT = (((1,), (1,)), ((), ()))


def split_state(state):
    high = state.astype(jnp.bfloat16)
    low = (state - high.astype(jnp.float32)).astype(jnp.bfloat16)
    return high, low


def scores_kernel(scale, q_ref, k_ref, v_ref, g_ref, kv_ref, gq_ref, gk_ref, gv_ref):
    q, k, v, g = q_ref[...], k_ref[...], v_ref[...], g_ref[...]
    length = q.shape[0]
    row = lax.broadcasted_iota(jnp.int32, (length, length), 0)
    col = lax.broadcasted_iota(jnp.int32, (length, length), 1)

    def score(a, b, keep):
        s = lax.dot_general(a, b, NT, preferred_element_type=jnp.float32) * scale
        return jnp.where(keep, s, 0.0).astype(jnp.bfloat16)

    score_grad = score(g, v, row >= col)
    score_grad_t = score(v, g, row <= col)
    score_fwd_t = score(k, q, row <= col)
    high, low = split_state(kv_ref[0, 0])
    gq = jnp.dot(score_grad, k, preferred_element_type=jnp.float32)
    gq = gq + lax.dot_general(g, high, NT, preferred_element_type=jnp.float32)
    gq = gq + lax.dot_general(g, low, NT, preferred_element_type=jnp.float32)
    gq_ref[...] = gq.astype(jnp.bfloat16)
    gk_ref[...] = jnp.dot(score_grad_t, q, preferred_element_type=jnp.float32)
    gv_ref[...] = jnp.dot(score_fwd_t, g, preferred_element_type=jnp.float32)


def state_kernel(k_ref, v_ref, qg_ref, gkp_ref, gvp_ref, gk_ref, gv_ref):
    k, v = k_ref[...], v_ref[...]
    high, low = split_state(qg_ref[0, 0])
    gk = gkp_ref[...] + lax.dot_general(v, high, NT, preferred_element_type=jnp.float32)
    gk = gk + lax.dot_general(v, low, NT, preferred_element_type=jnp.float32)
    gv = gvp_ref[...] + jnp.dot(k, high, preferred_element_type=jnp.float32)
    gv = gv + jnp.dot(k, low, preferred_element_type=jnp.float32)
    gk_ref[...] = gk.astype(jnp.bfloat16)
    gv_ref[...] = gv.astype(jnp.bfloat16)


def specs(blocks, block_len, heads):
    tok = pl.BlockSpec((block_len, DH), lambda n, h: (n, h))
    st = pl.BlockSpec((1, 1, DH, DH), lambda n, h: (n, h, 0, 0))
    return tok, st


def attention_part(q, k, v, g, kv_scaled, blocks, block_len, heads, scale):
    tok, st = specs(blocks, block_len, heads)
    rows, width = q.shape
    steps = blocks * heads
    flops = steps * (6 * 2 * block_len * block_len * DH + 2 * 2 * block_len * DH * DH)
    return pl.pallas_call(
        lambda *refs: scores_kernel(scale, *refs),
        grid=(blocks, heads),
        in_specs=[tok, tok, tok, tok, st],
        out_specs=[tok, tok, tok],
        out_shape=[
            jax.ShapeDtypeStruct((rows, width), jnp.bfloat16),
            jax.ShapeDtypeStruct((rows, width), jnp.float32),
            jax.ShapeDtypeStruct((rows, width), jnp.float32),
        ],
        cost_estimate=pl.CostEstimate(
            flops=flops, transcendentals=0, bytes_accessed=rows * width * 18
        ),
        name="attention_part",
    )(q, k, v, g, kv_scaled)


def state_part(k, v, qg_scaled, gk_part, gv_part, blocks, block_len, heads):
    tok, st = specs(blocks, block_len, heads)
    rows, width = k.shape
    steps = blocks * heads
    return pl.pallas_call(
        state_kernel,
        grid=(blocks, heads),
        in_specs=[tok, tok, st, tok, tok],
        out_specs=[tok, tok],
        out_shape=[
            jax.ShapeDtypeStruct((rows, width), jnp.bfloat16),
            jax.ShapeDtypeStruct((rows, width), jnp.bfloat16),
        ],
        cost_estimate=pl.CostEstimate(
            flops=steps * 4 * 2 * block_len * DH * DH,
            transcendentals=0,
            bytes_accessed=rows * width * 16,
        ),
        name="state_part",
    )(k, v, qg_scaled, gk_part, gv_part)


def make_shards(ctx_size, head_size):
    def shards(queries, keys, values, output_grad, out_weight):
        row_count = queries.shape[0]
        width = queries.shape[1]
        heads = width // DH
        block_len = min(row_count, 512)
        blocks = row_count // block_len
        scale_factor = DH ** (-0.5)
        shape = (blocks, block_len, heads, DH)
        q_blocks = queries.reshape(shape)
        k_blocks = keys.reshape(shape)
        v_blocks = values.reshape(shape)
        grad_heads, (k_tied, v_tied) = project(output_grad, out_weight, ctx_size, head_size, (keys, values))
        grad_heads = grad_heads.astype(jnp.bfloat16)
        kv_blocks = jnp.einsum(
            "nshd,nshe->nhde", k_tied.reshape(shape), v_tied.reshape(shape),
            preferred_element_type=jnp.float32,
        )
        kv_running = jnp.cumsum(kv_blocks, axis=0)
        kv_before = ctx_exclusive(kv_running[-1], ctx_size, False)
        kv_entry = kv_before[None] + kv_running - kv_blocks
        gq, gk_part, gv_part = attention_part(
            queries, keys, values, grad_heads, scale_factor * kv_entry,
            blocks, block_len, heads, scale_factor,
        )
        g_blocks = grad_heads.reshape(shape)
        qg_blocks = jnp.einsum(
            "nthd,nthe->nhde", q_blocks, g_blocks, preferred_element_type=jnp.float32
        )
        qg_running = jnp.flip(jnp.cumsum(jnp.flip(qg_blocks, 0), axis=0), 0)
        qg_after = ctx_exclusive(qg_running[0], ctx_size, True)
        qg_entry = qg_after[None] + qg_running - qg_blocks
        gk, gv = state_part(
            keys, values, scale_factor * qg_entry, gk_part, gv_part, blocks, block_len, heads
        )
        return gq, gk, gv

    return shards


def solution(mesh):
    return jax.shard_map(
        make_shards(mesh.shape["ctx"], mesh.shape["head"]),
        mesh=mesh,
        in_specs=(
            P("ctx", "head"),
            P("ctx", "head"),
            P("ctx", "head"),
            P("ctx", "head"),
            P("head", None),
        ),
        out_specs=(P("ctx", "head"), P("ctx", "head"), P("ctx", "head")),
        check_vma=False,
    )
```

```python
import jax
import jax.numpy as jnp
from jax import lax
from jax.experimental import pallas as pl
from jax.sharding import PartitionSpec as P

DH = 128


def flip_pairs(n, bit):
    return [(a, a ^ bit) for a in range(n)]


def project(og, out_weight, ctx_size, head_size, tied):
    cols = og.shape[1]

    def weight_cols(source, lo, width):
        return lax.dynamic_slice_in_dim(out_weight, source * cols + lo, width, axis=1)

    def mm(a, b):
        return lax.dot_general(
            a, b, (((1,), (1,)), ((), ())), preferred_element_type=jnp.float32
        )

    if head_size != 4:
        full = lax.all_gather(og, "head", axis=1, tiled=True)
        full, tied = lax.optimization_barrier((full, tied))
        return mm(full, out_weight), tied
    me = lax.axis_index("head")
    core = lax.axis_index("ctx") % 2
    from_x = lax.ppermute(og, "head", flip_pairs(4, 1))
    from_y = lax.ppermute(og, "head", flip_pairs(4, 2))
    relayed = jnp.where(core == 0, from_x, from_y)
    devices = [(p, j) for p in range(ctx_size) for j in range(4)]
    route = [(p * 4 + j, p * 4 + (j ^ (2 if p % 2 == 0 else 1))) for p, j in devices]
    diag = lax.ppermute(relayed, ("ctx", "head"), route)
    diag, tied = lax.optimization_barrier((diag, tied))
    acc = mm(og, weight_cols(me, 0, cols))
    acc = acc + mm(from_x, weight_cols(me ^ 1, 0, cols))
    acc = acc + mm(from_y, weight_cols(me ^ 2, 0, cols))
    acc = acc + mm(diag, weight_cols(me ^ 3, 0, cols))
    return acc, tied


def ctx_exclusive(state, ctx_size, reverse):
    p = lax.axis_index("ctx")
    core = p % 2
    chips = ctx_size // 2
    rounded = state.astype(jnp.bfloat16)
    partner = lax.ppermute(rounded, "ctx", flip_pairs(ctx_size, 1))
    chip_sum = rounded.astype(jnp.float32) + partner.astype(jnp.float32)
    half = state.shape[1] // 2
    mine = lax.dynamic_slice_in_dim(chip_sum, core * half, half, axis=1)
    others = jnp.zeros_like(mine)
    if chips <= 4:
        sent = mine.astype(jnp.bfloat16)
        for step in range(1, chips):
            if reverse:
                pairs = [(2 * (z + step) + c, 2 * z + c) for z in range(chips - step) for c in range(2)]
            else:
                pairs = [(2 * z + c, 2 * (z + step) + c) for z in range(chips - step) for c in range(2)]
            others = others + lax.ppermute(sent, "ctx", pairs).astype(jnp.float32)
    else:
        run = mine
        step = 1
        while step < chips:
            if reverse:
                pairs = [(2 * (z + step) + c, 2 * z + c) for z in range(chips - step) for c in range(2)]
            else:
                pairs = [(2 * z + c, 2 * (z + step) + c) for z in range(chips - step) for c in range(2)]
            got = lax.ppermute(run.astype(jnp.bfloat16), "ctx", pairs).astype(jnp.float32)
            run = run + got
            others = others + got
            step *= 2
    theirs = lax.ppermute(others, "ctx", flip_pairs(ctx_size, 1))
    lower = jnp.where(core == 0, others, theirs)
    upper = jnp.where(core == 0, theirs, others)
    chips_side = jnp.concatenate([lower, upper], axis=1)
    same_chip = (core == 0) if reverse else (core == 1)
    return chips_side + jnp.where(same_chip, partner.astype(jnp.float32), 0.0)


NT = (((1,), (1,)), ((), ()))


def split_state(state):
    high = state.astype(jnp.bfloat16)
    low = (state - high.astype(jnp.float32)).astype(jnp.bfloat16)
    return high, low


def scores_kernel(scale, q_ref, k_ref, v_ref, g_ref, gq_ref, gk_ref, gv_ref):
    q, k, v, g = q_ref[...], k_ref[...], v_ref[...], g_ref[...]
    length = q.shape[0]
    row = lax.broadcasted_iota(jnp.int32, (length, length), 0)
    col = lax.broadcasted_iota(jnp.int32, (length, length), 1)

    def score(a, b, keep):
        s = lax.dot_general(a, b, NT, preferred_element_type=jnp.float32) * scale
        return jnp.where(keep, s, 0.0).astype(jnp.bfloat16)

    score_grad = score(g, v, row >= col)
    gq_ref[...] = jnp.dot(score_grad, k, preferred_element_type=jnp.float32)
    score_grad_t = score(v, g, row <= col)
    gk_ref[...] = jnp.dot(score_grad_t, q, preferred_element_type=jnp.float32)
    score_fwd_t = score(k, q, row <= col)
    gv_ref[...] = jnp.dot(score_fwd_t, g, preferred_element_type=jnp.float32)


def state_kernel(per_step, k_ref, v_ref, g_ref, kv_ref, qg_ref, gqp_ref, gkp_ref, gvp_ref,
                 gq_ref, gk_ref, gv_ref):
    for i in range(per_step):
        cols = pl.ds(i * DH, DH)
        k, v, g = k_ref[:, cols], v_ref[:, cols], g_ref[:, cols]
        kv_high, kv_low = split_state(kv_ref[0, i])
        qg_high, qg_low = split_state(qg_ref[0, i])
        gq = gqp_ref[:, cols] + lax.dot_general(g, kv_high, NT, preferred_element_type=jnp.float32)
        gq = gq + lax.dot_general(g, kv_low, NT, preferred_element_type=jnp.float32)
        gk = gkp_ref[:, cols] + lax.dot_general(v, qg_high, NT, preferred_element_type=jnp.float32)
        gk = gk + lax.dot_general(v, qg_low, NT, preferred_element_type=jnp.float32)
        gv = gvp_ref[:, cols] + jnp.dot(k, qg_high, preferred_element_type=jnp.float32)
        gv = gv + jnp.dot(k, qg_low, preferred_element_type=jnp.float32)
        gq_ref[:, cols] = gq.astype(jnp.bfloat16)
        gk_ref[:, cols] = gk.astype(jnp.bfloat16)
        gv_ref[:, cols] = gv.astype(jnp.bfloat16)


def attention_part(q, k, v, g, blocks, block_len, heads, scale):
    tok = pl.BlockSpec((block_len, DH), lambda n, h: (n, h))
    rows, width = q.shape
    part = jax.ShapeDtypeStruct((rows, width), jnp.float32)
    return pl.pallas_call(
        lambda *refs: scores_kernel(scale, *refs),
        grid=(blocks, heads),
        in_specs=[tok, tok, tok, tok],
        out_specs=[tok, tok, tok],
        out_shape=[part, part, part],
        cost_estimate=pl.CostEstimate(
            flops=blocks * heads * 6 * 2 * block_len * block_len * DH,
            transcendentals=0,
            bytes_accessed=rows * width * 20,
        ),
        name="attention_part",
    )(q, k, v, g)


def state_part(k, v, g, kv_scaled, qg_scaled, parts, blocks, block_len, heads):
    per_step = 2 if heads % 2 == 0 else 1
    tok = pl.BlockSpec((block_len, DH * per_step), lambda n, h: (n, h))
    st = pl.BlockSpec((1, per_step, DH, DH), lambda n, h: (n, h, 0, 0))
    rows, width = k.shape
    out = jax.ShapeDtypeStruct((rows, width), jnp.bfloat16)
    return pl.pallas_call(
        lambda *refs: state_kernel(per_step, *refs),
        grid=(blocks, heads // per_step),
        in_specs=[tok, tok, tok, st, st, tok, tok, tok],
        out_specs=[tok, tok, tok],
        out_shape=[out, out, out],
        cost_estimate=pl.CostEstimate(
            flops=blocks * heads * 6 * 2 * block_len * DH * DH,
            transcendentals=0,
            bytes_accessed=rows * width * 24,
        ),
        name="state_part",
    )(k, v, g, kv_scaled, qg_scaled, *parts)


def make_shards(ctx_size, head_size):
    def shards(queries, keys, values, output_grad, out_weight):
        row_count = queries.shape[0]
        width = queries.shape[1]
        heads = width // DH
        block_len = min(row_count, 512)
        blocks = row_count // block_len
        scale_factor = DH ** (-0.5)
        shape = (blocks, block_len, heads, DH)
        q_blocks = queries.reshape(shape)
        k_blocks = keys.reshape(shape)
        v_blocks = values.reshape(shape)
        grad_heads, (k_tied, v_tied) = project(output_grad, out_weight, ctx_size, head_size, (keys, values))
        grad_heads = grad_heads.astype(jnp.bfloat16)
        kv_blocks = jnp.einsum(
            "nshd,nshe->nhde", k_tied.reshape(shape), v_tied.reshape(shape),
            preferred_element_type=jnp.float32,
        )
        kv_running = jnp.cumsum(kv_blocks, axis=0)
        kv_before = ctx_exclusive(kv_running[-1], ctx_size, False)
        kv_entry = kv_before[None] + kv_running - kv_blocks
        parts = attention_part(queries, keys, values, grad_heads, blocks, block_len, heads, scale_factor)
        g_blocks = grad_heads.reshape(shape)
        qg_blocks = jnp.einsum(
            "nthd,nthe->nhde", q_blocks, g_blocks, preferred_element_type=jnp.float32
        )
        qg_running = jnp.flip(jnp.cumsum(jnp.flip(qg_blocks, 0), axis=0), 0)
        qg_after = ctx_exclusive(qg_running[0], ctx_size, True)
        qg_entry = qg_after[None] + qg_running - qg_blocks
        return state_part(
            keys, values, grad_heads, scale_factor * kv_entry, scale_factor * qg_entry,
            parts, blocks, block_len, heads,
        )

    return shards


def solution(mesh):
    return jax.shard_map(
        make_shards(mesh.shape["ctx"], mesh.shape["head"]),
        mesh=mesh,
        in_specs=(
            P("ctx", "head"),
            P("ctx", "head"),
            P("ctx", "head"),
            P("ctx", "head"),
            P("head", None),
        ),
        out_specs=(P("ctx", "head"), P("ctx", "head"), P("ctx", "head")),
        check_vma=False,
    )
```

```python
import jax
import jax.numpy as jnp
from jax import lax
from jax.experimental import pallas as pl
from jax.sharding import PartitionSpec as P

DH = 128


def flip_pairs(n, bit):
    return [(a, a ^ bit) for a in range(n)]


def project(og, out_weight, ctx_size, head_size, tied):
    cols = og.shape[1]

    def weight_cols(source, lo, width):
        return lax.dynamic_slice_in_dim(out_weight, source * cols + lo, width, axis=1)

    def mm(a, b):
        return lax.dot_general(
            a, b, (((1,), (1,)), ((), ())), preferred_element_type=jnp.float32
        )

    if head_size != 4:
        full = lax.all_gather(og, "head", axis=1, tiled=True)
        full, tied = lax.optimization_barrier((full, tied))
        return mm(full, out_weight), tied
    me = lax.axis_index("head")
    core = lax.axis_index("ctx") % 2
    from_x = lax.ppermute(og, "head", flip_pairs(4, 1))
    from_y = lax.ppermute(og, "head", flip_pairs(4, 2))
    relayed = jnp.where(core == 0, from_x, from_y)
    devices = [(p, j) for p in range(ctx_size) for j in range(4)]
    route = [(p * 4 + j, p * 4 + (j ^ (2 if p % 2 == 0 else 1))) for p, j in devices]
    diag = lax.ppermute(relayed, ("ctx", "head"), route)
    diag, tied = lax.optimization_barrier((diag, tied))
    acc = mm(og, weight_cols(me, 0, cols))
    acc = acc + mm(from_x, weight_cols(me ^ 1, 0, cols))
    acc = acc + mm(from_y, weight_cols(me ^ 2, 0, cols))
    acc = acc + mm(diag, weight_cols(me ^ 3, 0, cols))
    return acc, tied


def exchange_prepare(state, ctx_size):
    core = lax.axis_index("ctx") % 2
    rounded = state.astype(jnp.bfloat16)
    partner = lax.ppermute(rounded, "ctx", flip_pairs(ctx_size, 1))
    chip_sum = rounded.astype(jnp.float32) + partner.astype(jnp.float32)
    half = state.shape[1] // 2
    mine = lax.dynamic_slice_in_dim(chip_sum, core * half, half, axis=1)
    return partner, mine


def exchange_send(mine, ctx_size, reverse):
    chips = ctx_size // 2

    def pairs(step):
        if reverse:
            return [(2 * (z + step) + c, 2 * z + c) for z in range(chips - step) for c in range(2)]
        return [(2 * z + c, 2 * (z + step) + c) for z in range(chips - step) for c in range(2)]

    others = jnp.zeros_like(mine)
    if chips <= 4:
        sent = mine.astype(jnp.bfloat16)
        for step in range(1, chips):
            others = others + lax.ppermute(sent, "ctx", pairs(step)).astype(jnp.float32)
        return others
    run = mine
    step = 1
    while step < chips:
        got = lax.ppermute(run.astype(jnp.bfloat16), "ctx", pairs(step)).astype(jnp.float32)
        run = run + got
        others = others + got
        step *= 2
    return others


def exchange_finish(others, partner, ctx_size, reverse):
    core = lax.axis_index("ctx") % 2
    theirs = lax.ppermute(others, "ctx", flip_pairs(ctx_size, 1))
    lower = jnp.where(core == 0, others, theirs)
    upper = jnp.where(core == 0, theirs, others)
    chips_side = jnp.concatenate([lower, upper], axis=1)
    same_chip = (core == 0) if reverse else (core == 1)
    return chips_side + jnp.where(same_chip, partner.astype(jnp.float32), 0.0)


NT = (((1,), (1,)), ((), ()))


def split_state(state):
    high = state.astype(jnp.bfloat16)
    low = (state - high.astype(jnp.float32)).astype(jnp.bfloat16)
    return high, low


def scores_kernel(scale, chunk, q_ref, k_ref, v_ref, g_ref, gq_ref, gk_ref, gv_ref):
    length = q_ref.shape[0]
    count = length // chunk
    row = lax.broadcasted_iota(jnp.int32, (chunk, chunk), 0)
    col = lax.broadcasted_iota(jnp.int32, (chunk, chunk), 1)

    def piece(ref, i):
        return ref[pl.ds(i * chunk, chunk), :]

    def score(a, b, keep):
        s = lax.dot_general(a, b, NT, preferred_element_type=jnp.float32) * scale
        if keep is not None:
            s = jnp.where(keep, s, 0.0)
        return s.astype(jnp.bfloat16)

    for i in range(count):
        rows = pl.ds(i * chunk, chunk)
        g_i = piece(g_ref, i)
        gq = None
        for j in range(i + 1):
            sg = score(g_i, piece(v_ref, j), row >= col if j == i else None)
            term = jnp.dot(sg, piece(k_ref, j), preferred_element_type=jnp.float32)
            gq = term if gq is None else gq + term
        gq_ref[rows, :] = gq.astype(gq_ref.dtype)
        v_i, k_i = piece(v_ref, i), piece(k_ref, i)
        gk = None
        gv = None
        for j in range(i, count):
            keep = row <= col if j == i else None
            sgt = score(v_i, piece(g_ref, j), keep)
            sft = score(k_i, piece(q_ref, j), keep)
            term_k = jnp.dot(sgt, piece(q_ref, j), preferred_element_type=jnp.float32)
            term_v = jnp.dot(sft, piece(g_ref, j), preferred_element_type=jnp.float32)
            gk = term_k if gk is None else gk + term_k
            gv = term_v if gv is None else gv + term_v
        gk_ref[rows, :] = gk.astype(gk_ref.dtype)
        gv_ref[rows, :] = gv.astype(gv_ref.dtype)


def state_kernel(per_step, k_ref, v_ref, g_ref, kv_ref, qg_ref, gqp_ref, gkp_ref, gvp_ref,
                 gq_ref, gk_ref, gv_ref):
    for i in range(per_step):
        cols = pl.ds(i * DH, DH)
        k, v, g = k_ref[:, cols], v_ref[:, cols], g_ref[:, cols]
        kv_high, kv_low = split_state(kv_ref[0, i])
        qg_high, qg_low = split_state(qg_ref[0, i])
        gq = gqp_ref[:, cols] + lax.dot_general(g, kv_high, NT, preferred_element_type=jnp.float32)
        gq = gq + lax.dot_general(g, kv_low, NT, preferred_element_type=jnp.float32)
        gk = gkp_ref[:, cols] + lax.dot_general(v, qg_high, NT, preferred_element_type=jnp.float32)
        gk = gk + lax.dot_general(v, qg_low, NT, preferred_element_type=jnp.float32)
        gv = gvp_ref[:, cols] + jnp.dot(k, qg_high, preferred_element_type=jnp.float32)
        gv = gv + jnp.dot(k, qg_low, preferred_element_type=jnp.float32)
        gq_ref[:, cols] = gq.astype(jnp.bfloat16)
        gk_ref[:, cols] = gk.astype(jnp.bfloat16)
        gv_ref[:, cols] = gv.astype(jnp.bfloat16)


def attention_part(q, k, v, g, blocks, block_len, heads, scale):
    tok = pl.BlockSpec((block_len, DH), lambda n, h: (n, h))
    rows, width = q.shape
    part = jax.ShapeDtypeStruct((rows, width), jnp.bfloat16)
    chunk = 256 if block_len % 256 == 0 else block_len
    return pl.pallas_call(
        lambda *refs: scores_kernel(scale, chunk, *refs),
        grid=(blocks, heads),
        in_specs=[tok, tok, tok, tok],
        out_specs=[tok, tok, tok],
        out_shape=[part, part, part],
        cost_estimate=pl.CostEstimate(
            flops=blocks * heads * 6 * 2 * block_len * block_len * DH,
            transcendentals=0,
            bytes_accessed=rows * width * 14,
        ),
        name="attention_part",
    )(q, k, v, g)


def state_part(k, v, g, kv_scaled, qg_scaled, parts, blocks, block_len, heads):
    per_step = 2 if heads % 2 == 0 else 1
    tok = pl.BlockSpec((block_len, DH * per_step), lambda n, h: (n, h))
    st = pl.BlockSpec((1, per_step, DH, DH), lambda n, h: (n, h, 0, 0))
    rows, width = k.shape
    out = jax.ShapeDtypeStruct((rows, width), jnp.bfloat16)
    return pl.pallas_call(
        lambda *refs: state_kernel(per_step, *refs),
        grid=(blocks, heads // per_step),
        in_specs=[tok, tok, tok, st, st, tok, tok, tok],
        out_specs=[tok, tok, tok],
        out_shape=[out, out, out],
        cost_estimate=pl.CostEstimate(
            flops=blocks * heads * 6 * 2 * block_len * DH * DH,
            transcendentals=0,
            bytes_accessed=rows * width * 18,
        ),
        name="state_part",
    )(k, v, g, kv_scaled, qg_scaled, *parts)


def make_shards(ctx_size, head_size):
    def shards(queries, keys, values, output_grad, out_weight):
        row_count = queries.shape[0]
        width = queries.shape[1]
        heads = width // DH
        block_len = min(row_count, 512)
        blocks = row_count // block_len
        scale_factor = DH ** (-0.5)
        shape = (blocks, block_len, heads, DH)
        q_blocks = queries.reshape(shape)
        k_blocks = keys.reshape(shape)
        v_blocks = values.reshape(shape)
        grad_heads, (k_tied, v_tied) = project(output_grad, out_weight, ctx_size, head_size, (keys, values))
        grad_heads = grad_heads.astype(jnp.bfloat16)
        kv_blocks = jnp.einsum(
            "nshd,nshe->nhde", k_tied.reshape(shape), v_tied.reshape(shape),
            preferred_element_type=jnp.float32,
        )
        kv_running = jnp.cumsum(kv_blocks, axis=0)
        g_blocks = grad_heads.reshape(shape)
        qg_blocks = jnp.einsum(
            "nthd,nthe->nhde", q_blocks, g_blocks, preferred_element_type=jnp.float32
        )
        qg_running = jnp.flip(jnp.cumsum(jnp.flip(qg_blocks, 0), axis=0), 0)
        kv_partner, kv_mine = exchange_prepare(kv_running[-1], ctx_size)
        qg_partner, qg_mine = exchange_prepare(qg_running[0], ctx_size)
        kv_mine, qg_mine, g_held = lax.optimization_barrier((kv_mine, qg_mine, grad_heads))
        kv_others = exchange_send(kv_mine, ctx_size, False)
        qg_others = exchange_send(qg_mine, ctx_size, True)
        parts = attention_part(queries, keys, values, g_held, blocks, block_len, heads, scale_factor)
        kv_others, qg_others, parts = lax.optimization_barrier((kv_others, qg_others, parts))
        kv_before = exchange_finish(kv_others, kv_partner, ctx_size, False)
        qg_after = exchange_finish(qg_others, qg_partner, ctx_size, True)
        kv_entry = kv_before[None] + kv_running - kv_blocks
        qg_entry = qg_after[None] + qg_running - qg_blocks
        return state_part(
            keys, values, grad_heads, scale_factor * kv_entry, scale_factor * qg_entry,
            parts, blocks, block_len, heads,
        )

    return shards


def solution(mesh):
    return jax.shard_map(
        make_shards(mesh.shape["ctx"], mesh.shape["head"]),
        mesh=mesh,
        in_specs=(
            P("ctx", "head"),
            P("ctx", "head"),
            P("ctx", "head"),
            P("ctx", "head"),
            P("head", None),
        ),
        out_specs=(P("ctx", "head"), P("ctx", "head"), P("ctx", "head")),
        check_vma=False,
    )
```

```python
import jax
import jax.numpy as jnp
from jax import lax
from jax.experimental import pallas as pl
from jax.sharding import PartitionSpec as P

DH = 128


def flip_pairs(n, bit):
    return [(a, a ^ bit) for a in range(n)]


def project(og, out_weight, ctx_size, head_size):
    cols = og.shape[1]

    def weight_cols(source, lo, width):
        return lax.dynamic_slice_in_dim(out_weight, source * cols + lo, width, axis=1)

    def mm(a, b):
        return lax.dot_general(
            a, b, (((1,), (1,)), ((), ())), preferred_element_type=jnp.float32
        )

    if head_size != 4:
        full = lax.all_gather(og, "head", axis=1, tiled=True)
        return mm(full, out_weight)
    me = lax.axis_index("head")
    core = lax.axis_index("ctx") % 2
    from_x = lax.ppermute(og, "head", flip_pairs(4, 1))
    from_y = lax.ppermute(og, "head", flip_pairs(4, 2))
    relayed = jnp.where(core == 0, from_x, from_y)
    devices = [(p, j) for p in range(ctx_size) for j in range(4)]
    route = [(p * 4 + j, p * 4 + (j ^ (2 if p % 2 == 0 else 1))) for p, j in devices]
    diag = lax.ppermute(relayed, ("ctx", "head"), route)
    acc = mm(og, weight_cols(me, 0, cols))
    acc = acc + mm(from_x, weight_cols(me ^ 1, 0, cols))
    acc = acc + mm(from_y, weight_cols(me ^ 2, 0, cols))
    acc = acc + mm(diag, weight_cols(me ^ 3, 0, cols))
    return acc


def ctx_states(kv, qg, ctx_size, cover):
    core = lax.axis_index("ctx") % 2
    chips = ctx_size // 2
    own = jnp.stack([kv, qg]).astype(jnp.bfloat16)
    partner = lax.ppermute(own, "ctx", flip_pairs(ctx_size, 1)).astype(jnp.float32)
    chip_sum = own.astype(jnp.float32) + partner
    mine = jnp.where(core == 0, chip_sum[0], chip_sum[1])

    def pairs(step):
        forward = [(2 * z, 2 * (z + step)) for z in range(chips - step)]
        backward = [(2 * (z + step) + 1, 2 * z + 1) for z in range(chips - step)]
        return forward + backward

    mine, held = lax.optimization_barrier((mine, cover.args))
    others = jnp.zeros_like(mine)
    if chips <= 4:
        sent = mine.astype(jnp.bfloat16)
        for step in range(1, chips):
            others = others + lax.ppermute(sent, "ctx", pairs(step)).astype(jnp.float32)
    else:
        run = mine
        step = 1
        while step < chips:
            got = lax.ppermute(run.astype(jnp.bfloat16), "ctx", pairs(step)).astype(jnp.float32)
            run = run + got
            others = others + got
            step *= 2
    covered = cover.fn(*held)
    others, covered = lax.optimization_barrier((others, covered))
    theirs = lax.ppermute(others, "ctx", flip_pairs(ctx_size, 1))
    kv_chips = jnp.where(core == 0, others, theirs)
    qg_chips = jnp.where(core == 0, theirs, others)
    kv_before = kv_chips + jnp.where(core == 1, partner[0], 0.0)
    qg_after = qg_chips + jnp.where(core == 0, partner[1], 0.0)
    return kv_before, qg_after, covered


class Cover:
    def __init__(self, fn, args):
        self.fn = fn
        self.args = args


NT = (((1,), (1,)), ((), ()))


def split_state(state):
    high = state.astype(jnp.bfloat16)
    low = (state - high.astype(jnp.float32)).astype(jnp.bfloat16)
    return high, low


def scores_kernel(scale, chunk, per_step, q_ref, k_ref, v_ref, g_ref, gq_ref, gk_ref, gv_ref):
    length = q_ref.shape[0]
    count = length // chunk
    row = lax.broadcasted_iota(jnp.int32, (chunk, chunk), 0)
    col = lax.broadcasted_iota(jnp.int32, (chunk, chunk), 1)

    def score(a, b, keep):
        s = lax.dot_general(a, b, NT, preferred_element_type=jnp.float32) * scale
        if keep is not None:
            s = jnp.where(keep, s, 0.0)
        return s.astype(jnp.bfloat16)

    for h in range(per_step):
        cols = pl.ds(h * DH, DH)

        def piece(ref, i):
            return ref[pl.ds(i * chunk, chunk), cols]

        for i in range(count):
            rows = pl.ds(i * chunk, chunk)
            g_i = piece(g_ref, i)
            gq = None
            for j in range(i + 1):
                sg = score(g_i, piece(v_ref, j), row >= col if j == i else None)
                term = jnp.dot(sg, piece(k_ref, j), preferred_element_type=jnp.float32)
                gq = term if gq is None else gq + term
            gq_ref[rows, cols] = gq.astype(gq_ref.dtype)
            v_i, k_i = piece(v_ref, i), piece(k_ref, i)
            gk = None
            gv = None
            for j in range(i, count):
                keep = row <= col if j == i else None
                sgt = score(v_i, piece(g_ref, j), keep)
                sft = score(k_i, piece(q_ref, j), keep)
                term_k = jnp.dot(sgt, piece(q_ref, j), preferred_element_type=jnp.float32)
                term_v = jnp.dot(sft, piece(g_ref, j), preferred_element_type=jnp.float32)
                gk = term_k if gk is None else gk + term_k
                gv = term_v if gv is None else gv + term_v
            gk_ref[rows, cols] = gk.astype(gk_ref.dtype)
            gv_ref[rows, cols] = gv.astype(gv_ref.dtype)


def state_kernel(scale, per_step, k_ref, v_ref, g_ref, kv_ref, qg_ref, gqp_ref, gkp_ref, gvp_ref,
                 gq_ref, gk_ref, gv_ref):
    for i in range(per_step):
        cols = pl.ds(i * DH, DH)
        k, v, g = k_ref[:, cols], v_ref[:, cols], g_ref[:, cols]
        kv_high, kv_low = split_state(kv_ref[0, i] * scale)
        qg_high, qg_low = split_state(qg_ref[0, i] * scale)
        gq = gqp_ref[:, cols] + lax.dot_general(g, kv_high, NT, preferred_element_type=jnp.float32)
        gq = gq + lax.dot_general(g, kv_low, NT, preferred_element_type=jnp.float32)
        gk = gkp_ref[:, cols] + lax.dot_general(v, qg_high, NT, preferred_element_type=jnp.float32)
        gk = gk + lax.dot_general(v, qg_low, NT, preferred_element_type=jnp.float32)
        gv = gvp_ref[:, cols] + jnp.dot(k, qg_high, preferred_element_type=jnp.float32)
        gv = gv + jnp.dot(k, qg_low, preferred_element_type=jnp.float32)
        gq_ref[:, cols] = gq.astype(jnp.bfloat16)
        gk_ref[:, cols] = gk.astype(jnp.bfloat16)
        gv_ref[:, cols] = gv.astype(jnp.bfloat16)


def attention_part(q, k, v, g, blocks, block_len, heads, scale, per_step=1):
    tok = pl.BlockSpec((block_len, DH * per_step), lambda n, h: (n, h))
    rows, width = q.shape
    part = jax.ShapeDtypeStruct((rows, width), jnp.bfloat16)
    chunk = 256 if block_len % 256 == 0 else block_len
    return pl.pallas_call(
        lambda *refs: scores_kernel(scale, chunk, per_step, *refs),
        grid=(blocks, heads // per_step),
        in_specs=[tok, tok, tok, tok],
        out_specs=[tok, tok, tok],
        out_shape=[part, part, part],
        cost_estimate=pl.CostEstimate(
            flops=blocks * heads * 6 * 2 * block_len * block_len * DH,
            transcendentals=0,
            bytes_accessed=rows * width * 14,
        ),
        name="attention_part",
    )(q, k, v, g)


def state_part(k, v, g, kv_state, qg_state, parts, blocks, block_len, heads, scale):
    per_step = 2 if heads % 2 == 0 else 1
    tok = pl.BlockSpec((block_len, DH * per_step), lambda n, h: (n, h))
    st = pl.BlockSpec((1, per_step, DH, DH), lambda n, h: (n, h, 0, 0))
    rows, width = k.shape
    out = jax.ShapeDtypeStruct((rows, width), jnp.bfloat16)
    return pl.pallas_call(
        lambda *refs: state_kernel(scale, per_step, *refs),
        grid=(blocks, heads // per_step),
        in_specs=[tok, tok, tok, st, st, tok, tok, tok],
        out_specs=[tok, tok, tok],
        out_shape=[out, out, out],
        cost_estimate=pl.CostEstimate(
            flops=blocks * heads * 6 * 2 * block_len * DH * DH,
            transcendentals=0,
            bytes_accessed=rows * width * 18,
        ),
        name="state_part",
    )(k, v, g, kv_state, qg_state, *parts)


def make_shards(ctx_size, head_size):
    def shards(queries, keys, values, output_grad, out_weight):
        row_count = queries.shape[0]
        width = queries.shape[1]
        heads = width // DH
        block_len = min(row_count, 512)
        blocks = row_count // block_len
        scale_factor = DH ** (-0.5)
        shape = (blocks, block_len, heads, DH)
        q_blocks = queries.reshape(shape)
        k_blocks = keys.reshape(shape)
        v_blocks = values.reshape(shape)
        grad_heads = project(output_grad, out_weight, ctx_size, head_size)
        grad_heads = grad_heads.astype(jnp.bfloat16)
        kv_blocks = jnp.einsum(
            "nshd,nshe->nhde", k_blocks, v_blocks,
            preferred_element_type=jnp.float32,
        )
        kv_running = jnp.cumsum(kv_blocks, axis=0)
        g_blocks = grad_heads.reshape(shape)
        qg_blocks = jnp.einsum(
            "nthd,nthe->nhde", q_blocks, g_blocks, preferred_element_type=jnp.float32
        )
        qg_running = jnp.flip(jnp.cumsum(jnp.flip(qg_blocks, 0), axis=0), 0)
        kv_before, qg_after, parts = ctx_states(
            kv_running[-1], qg_running[0], ctx_size,
            Cover(
                lambda g: attention_part(queries, keys, values, g, blocks, block_len, heads, scale_factor),
                (grad_heads,),
            ),
        )
        kv_entry = kv_before[None] + kv_running - kv_blocks
        qg_entry = qg_after[None] + qg_running - qg_blocks
        return state_part(
            keys, values, grad_heads, kv_entry, qg_entry, parts, blocks, block_len, heads, scale_factor
        )

    return shards


def solution(mesh):
    return jax.shard_map(
        make_shards(mesh.shape["ctx"], mesh.shape["head"]),
        mesh=mesh,
        in_specs=(
            P("ctx", "head"),
            P("ctx", "head"),
            P("ctx", "head"),
            P("ctx", "head"),
            P("head", None),
        ),
        out_specs=(P("ctx", "head"), P("ctx", "head"), P("ctx", "head")),
        check_vma=False,
    )
```

```python
import jax
import jax.numpy as jnp
from jax import lax
from jax.experimental import pallas as pl
from jax.sharding import PartitionSpec as P

DH = 128


def flip_pairs(n, bit):
    return [(a, a ^ bit) for a in range(n)]


def project(og, out_weight, ctx_size, head_size):
    cols = og.shape[1]

    def weight_cols(source, lo, width):
        return lax.dynamic_slice_in_dim(out_weight, source * cols + lo, width, axis=1)

    def mm(a, b):
        return lax.dot_general(
            a, b, (((1,), (1,)), ((), ())), preferred_element_type=jnp.float32
        )

    if head_size != 4:
        full = lax.all_gather(og, "head", axis=1, tiled=True)
        return mm(full, out_weight)
    me = lax.axis_index("head")
    core = lax.axis_index("ctx") % 2
    from_x = lax.ppermute(og, "head", flip_pairs(4, 1))
    from_y = lax.ppermute(og, "head", flip_pairs(4, 2))
    relayed = jnp.where(core == 0, from_x, from_y)
    devices = [(p, j) for p in range(ctx_size) for j in range(4)]
    route = [(p * 4 + j, p * 4 + (j ^ (2 if p % 2 == 0 else 1))) for p, j in devices]
    diag = lax.ppermute(relayed, ("ctx", "head"), route)
    acc = mm(og, weight_cols(me, 0, cols))
    acc = acc + mm(from_x, weight_cols(me ^ 1, 0, cols))
    acc = acc + mm(from_y, weight_cols(me ^ 2, 0, cols))
    acc = acc + mm(diag, weight_cols(me ^ 3, 0, cols))
    return acc


def ctx_exclusive(state, ctx_size, reverse, cover=None):
    core = lax.axis_index("ctx") % 2
    chips = ctx_size // 2
    rounded = state.astype(jnp.bfloat16)
    partner = lax.ppermute(rounded, "ctx", flip_pairs(ctx_size, 1)).astype(jnp.float32)
    chip_sum = rounded.astype(jnp.float32) + partner
    half = state.shape[1] // 2
    mine = lax.dynamic_slice_in_dim(chip_sum, core * half, half, axis=1)

    def pairs(step):
        if reverse:
            return [(2 * (z + step) + c, 2 * z + c) for z in range(chips - step) for c in range(2)]
        return [(2 * z + c, 2 * (z + step) + c) for z in range(chips - step) for c in range(2)]

    if cover is not None:
        mine, held = lax.optimization_barrier((mine, cover.args))
    others = jnp.zeros_like(mine)
    if chips <= 4:
        sent = mine.astype(jnp.bfloat16)
        for step in range(1, chips):
            others = others + lax.ppermute(sent, "ctx", pairs(step)).astype(jnp.float32)
    else:
        run = mine
        step = 1
        while step < chips:
            got = lax.ppermute(run.astype(jnp.bfloat16), "ctx", pairs(step)).astype(jnp.float32)
            run = run + got
            others = others + got
            step *= 2
    covered = None
    if cover is not None:
        covered = cover.fn(*held)
        others, covered = lax.optimization_barrier((others, covered))
    theirs = lax.ppermute(others, "ctx", flip_pairs(ctx_size, 1))
    lower = jnp.where(core == 0, others, theirs)
    upper = jnp.where(core == 0, theirs, others)
    chips_side = jnp.concatenate([lower, upper], axis=1)
    same_chip = (core == 0) if reverse else (core == 1)
    return chips_side + jnp.where(same_chip, partner, 0.0), covered


class Cover:
    def __init__(self, fn, args):
        self.fn = fn
        self.args = args


NT = (((1,), (1,)), ((), ()))


def split_state(state):
    high = state.astype(jnp.bfloat16)
    low = (state - high.astype(jnp.float32)).astype(jnp.bfloat16)
    return high, low


def scores_kernel(scale, chunk, per_step, q_ref, k_ref, v_ref, g_ref, kv_ref, gq_ref, gk_ref, gv_ref):
    length = q_ref.shape[0]
    count = length // chunk
    row = lax.broadcasted_iota(jnp.int32, (chunk, chunk), 0)
    col = lax.broadcasted_iota(jnp.int32, (chunk, chunk), 1)

    def score(a, b, keep):
        s = lax.dot_general(a, b, NT, preferred_element_type=jnp.float32) * scale
        if keep is not None:
            s = jnp.where(keep, s, 0.0)
        return s.astype(jnp.bfloat16)

    for h in range(per_step):
        cols = pl.ds(h * DH, DH)
        kv_high, kv_low = split_state(kv_ref[0, h] * scale)

        def piece(ref, i):
            return ref[pl.ds(i * chunk, chunk), cols]

        for i in range(count):
            rows = pl.ds(i * chunk, chunk)
            g_i = piece(g_ref, i)
            gq = lax.dot_general(g_i, kv_high, NT, preferred_element_type=jnp.float32)
            gq = gq + lax.dot_general(g_i, kv_low, NT, preferred_element_type=jnp.float32)
            for j in range(i + 1):
                sg = score(g_i, piece(v_ref, j), row >= col if j == i else None)
                term = jnp.dot(sg, piece(k_ref, j), preferred_element_type=jnp.float32)
                gq = gq + term
            gq_ref[rows, cols] = gq.astype(gq_ref.dtype)
            v_i, k_i = piece(v_ref, i), piece(k_ref, i)
            gk = None
            gv = None
            for j in range(i, count):
                keep = row <= col if j == i else None
                sgt = score(v_i, piece(g_ref, j), keep)
                sft = score(k_i, piece(q_ref, j), keep)
                term_k = jnp.dot(sgt, piece(q_ref, j), preferred_element_type=jnp.float32)
                term_v = jnp.dot(sft, piece(g_ref, j), preferred_element_type=jnp.float32)
                gk = term_k if gk is None else gk + term_k
                gv = term_v if gv is None else gv + term_v
            gk_ref[rows, cols] = gk.astype(gk_ref.dtype)
            gv_ref[rows, cols] = gv.astype(gv_ref.dtype)


def state_kernel(scale, per_step, k_ref, v_ref, qg_ref, gkp_ref, gvp_ref, gk_ref, gv_ref):
    for i in range(per_step):
        cols = pl.ds(i * DH, DH)
        k, v = k_ref[:, cols], v_ref[:, cols]
        qg_high, qg_low = split_state(qg_ref[0, i] * scale)
        gk = gkp_ref[:, cols].astype(jnp.float32)
        gk = gk + lax.dot_general(v, qg_high, NT, preferred_element_type=jnp.float32)
        gk = gk + lax.dot_general(v, qg_low, NT, preferred_element_type=jnp.float32)
        gv = gvp_ref[:, cols].astype(jnp.float32)
        gv = gv + jnp.dot(k, qg_high, preferred_element_type=jnp.float32)
        gv = gv + jnp.dot(k, qg_low, preferred_element_type=jnp.float32)
        gk_ref[:, cols] = gk.astype(jnp.bfloat16)
        gv_ref[:, cols] = gv.astype(jnp.bfloat16)


def attention_part(q, k, v, g, kv_state, blocks, block_len, heads, scale):
    per_step = 2 if heads % 2 == 0 else 1
    tok = pl.BlockSpec((block_len, DH * per_step), lambda n, h: (n, h))
    st = pl.BlockSpec((1, per_step, DH, DH), lambda n, h: (n, h, 0, 0))
    rows, width = q.shape
    out = jax.ShapeDtypeStruct((rows, width), jnp.bfloat16)
    chunk = 256 if block_len % 256 == 0 else block_len
    return pl.pallas_call(
        lambda *refs: scores_kernel(scale, chunk, per_step, *refs),
        grid=(blocks, heads // per_step),
        in_specs=[tok, tok, tok, tok, st],
        out_specs=[tok, tok, tok],
        out_shape=[out, out, out],
        cost_estimate=pl.CostEstimate(
            flops=blocks * heads * 6 * 2 * block_len * block_len * DH,
            transcendentals=0,
            bytes_accessed=rows * width * 14,
        ),
        name="attention_part",
    )(q, k, v, g, kv_state)


def state_part(k, v, qg_state, parts, blocks, block_len, heads, scale):
    per_step = 2 if heads % 2 == 0 else 1
    tok = pl.BlockSpec((block_len, DH * per_step), lambda n, h: (n, h))
    st = pl.BlockSpec((1, per_step, DH, DH), lambda n, h: (n, h, 0, 0))
    rows, width = k.shape
    out = jax.ShapeDtypeStruct((rows, width), jnp.bfloat16)
    return pl.pallas_call(
        lambda *refs: state_kernel(scale, per_step, *refs),
        grid=(blocks, heads // per_step),
        in_specs=[tok, tok, st, tok, tok],
        out_specs=[tok, tok],
        out_shape=[out, out],
        cost_estimate=pl.CostEstimate(
            flops=blocks * heads * 4 * 2 * block_len * DH * DH,
            transcendentals=0,
            bytes_accessed=rows * width * 12,
        ),
        name="state_part",
    )(k, v, qg_state, *parts)


def make_shards(ctx_size, head_size):
    def shards(queries, keys, values, output_grad, out_weight):
        row_count = queries.shape[0]
        width = queries.shape[1]
        heads = width // DH
        block_len = min(row_count, 512)
        blocks = row_count // block_len
        scale_factor = DH ** (-0.5)
        shape = (blocks, block_len, heads, DH)
        q_blocks = queries.reshape(shape)
        k_blocks = keys.reshape(shape)
        v_blocks = values.reshape(shape)
        grad_heads = project(output_grad, out_weight, ctx_size, head_size)
        grad_heads = grad_heads.astype(jnp.bfloat16)
        kv_blocks = jnp.einsum(
            "nshd,nshe->nhde", k_blocks, v_blocks,
            preferred_element_type=jnp.float32,
        )
        kv_running = jnp.cumsum(kv_blocks, axis=0)
        kv_before, _ = ctx_exclusive(kv_running[-1], ctx_size, False)
        if blocks == 1:
            kv_entry = kv_before[None]
        else:
            kv_entry = kv_before[None] + kv_running - kv_blocks
        g_blocks = grad_heads.reshape(shape)
        qg_blocks = jnp.einsum(
            "nthd,nthe->nhde", q_blocks, g_blocks, preferred_element_type=jnp.float32
        )
        qg_running = jnp.flip(jnp.cumsum(jnp.flip(qg_blocks, 0), axis=0), 0)
        qg_after, (gq, gk_part, gv_part) = ctx_exclusive(
            qg_running[0], ctx_size, True,
            Cover(
                lambda g, kv: attention_part(
                    queries, keys, values, g, kv, blocks, block_len, heads, scale_factor
                ),
                (grad_heads, kv_entry),
            ),
        )
        if blocks == 1:
            qg_entry = qg_after[None]
        else:
            qg_entry = qg_after[None] + qg_running - qg_blocks
        gk, gv = state_part(
            keys, values, qg_entry, (gk_part, gv_part), blocks, block_len, heads, scale_factor
        )
        return gq, gk, gv

    return shards


def solution(mesh):
    return jax.shard_map(
        make_shards(mesh.shape["ctx"], mesh.shape["head"]),
        mesh=mesh,
        in_specs=(
            P("ctx", "head"),
            P("ctx", "head"),
            P("ctx", "head"),
            P("ctx", "head"),
            P("head", None),
        ),
        out_specs=(P("ctx", "head"), P("ctx", "head"), P("ctx", "head")),
        check_vma=False,
    )
```

```python
import jax
import jax.numpy as jnp
from jax import lax
from jax.experimental import pallas as pl
from jax.sharding import PartitionSpec as P

DH = 128


def flip_pairs(n, bit):
    return [(a, a ^ bit) for a in range(n)]


def project(og, out_weight, ctx_size, head_size):
    cols = og.shape[1]

    def weight_cols(source, lo, width):
        return lax.dynamic_slice_in_dim(out_weight, source * cols + lo, width, axis=1)

    def mm(a, b):
        return lax.dot_general(
            a, b, (((1,), (1,)), ((), ())), preferred_element_type=jnp.float32
        )

    if head_size != 4:
        full = lax.all_gather(og, "head", axis=1, tiled=True)
        return mm(full, out_weight)
    me = lax.axis_index("head")
    core = lax.axis_index("ctx") % 2
    from_x = lax.ppermute(og, "head", flip_pairs(4, 1))
    from_y = lax.ppermute(og, "head", flip_pairs(4, 2))
    relayed = jnp.where(core == 0, from_x, from_y)
    devices = [(p, j) for p in range(ctx_size) for j in range(4)]
    route = [(p * 4 + j, p * 4 + (j ^ (2 if p % 2 == 0 else 1))) for p, j in devices]
    diag = lax.ppermute(relayed, ("ctx", "head"), route)
    acc = mm(og, weight_cols(me, 0, cols))
    acc = acc + mm(from_x, weight_cols(me ^ 1, 0, cols))
    acc = acc + mm(from_y, weight_cols(me ^ 2, 0, cols))
    acc = acc + mm(diag, weight_cols(me ^ 3, 0, cols))
    return acc


def ctx_exclusive(state, ctx_size, reverse, cover=None):
    core = lax.axis_index("ctx") % 2
    chips = ctx_size // 2
    rounded = state.astype(jnp.bfloat16)
    partner = lax.ppermute(rounded, "ctx", flip_pairs(ctx_size, 1)).astype(jnp.float32)
    chip_sum = rounded.astype(jnp.float32) + partner
    half = state.shape[1] // 2
    mine = lax.dynamic_slice_in_dim(chip_sum, core * half, half, axis=1)

    def pairs(step):
        if reverse:
            return [(2 * (z + step) + c, 2 * z + c) for z in range(chips - step) for c in range(2)]
        return [(2 * z + c, 2 * (z + step) + c) for z in range(chips - step) for c in range(2)]

    if cover is not None:
        mine, held = lax.optimization_barrier((mine, cover.args))
    others = jnp.zeros_like(mine)
    if chips <= 4:
        sent = mine.astype(jnp.bfloat16)
        for step in range(1, chips):
            others = others + lax.ppermute(sent, "ctx", pairs(step)).astype(jnp.float32)
    else:
        run = mine
        step = 1
        while step < chips:
            got = lax.ppermute(run.astype(jnp.bfloat16), "ctx", pairs(step)).astype(jnp.float32)
            run = run + got
            others = others + got
            step *= 2
    covered = None
    if cover is not None:
        covered = cover.fn(*held)
        others, covered = lax.optimization_barrier((others, covered))
    theirs = lax.ppermute(others, "ctx", flip_pairs(ctx_size, 1))
    lower = jnp.where(core == 0, others, theirs)
    upper = jnp.where(core == 0, theirs, others)
    chips_side = jnp.concatenate([lower, upper], axis=1)
    same_chip = (core == 0) if reverse else (core == 1)
    return chips_side + jnp.where(same_chip, partner, 0.0), covered


class Cover:
    def __init__(self, fn, args):
        self.fn = fn
        self.args = args


NT = (((1,), (1,)), ((), ()))


def split_state(state):
    high = state.astype(jnp.bfloat16)
    low = (state - high.astype(jnp.float32)).astype(jnp.bfloat16)
    return high, low


def score(a, b, keep, scale):
    s = lax.dot_general(a, b, NT, preferred_element_type=jnp.float32) * scale
    if keep is not None:
        s = jnp.where(keep, s, 0.0)
    return s.astype(jnp.bfloat16)


def query_kernel(scale, chunk, per_step, k_ref, v_ref, g_ref, kv_ref, gq_ref):
    count = k_ref.shape[0] // chunk
    row = lax.broadcasted_iota(jnp.int32, (chunk, chunk), 0)
    col = lax.broadcasted_iota(jnp.int32, (chunk, chunk), 1)
    for h in range(per_step):
        cols = pl.ds(h * DH, DH)
        kv_high, kv_low = split_state(kv_ref[0, h] * scale)

        def piece(ref, i):
            return ref[pl.ds(i * chunk, chunk), cols]

        for i in range(count):
            g_i = piece(g_ref, i)
            gq = lax.dot_general(g_i, kv_high, NT, preferred_element_type=jnp.float32)
            gq = gq + lax.dot_general(g_i, kv_low, NT, preferred_element_type=jnp.float32)
            for j in range(i + 1):
                sg = score(g_i, piece(v_ref, j), row >= col if j == i else None, scale)
                gq = gq + jnp.dot(sg, piece(k_ref, j), preferred_element_type=jnp.float32)
            gq_ref[pl.ds(i * chunk, chunk), cols] = gq.astype(gq_ref.dtype)


def key_value_kernel(scale, chunk, per_step, q_ref, k_ref, v_ref, g_ref, qg_ref, gk_ref, gv_ref):
    count = k_ref.shape[0] // chunk
    row = lax.broadcasted_iota(jnp.int32, (chunk, chunk), 0)
    col = lax.broadcasted_iota(jnp.int32, (chunk, chunk), 1)
    for h in range(per_step):
        cols = pl.ds(h * DH, DH)
        qg_high, qg_low = split_state(qg_ref[0, h] * scale)

        def piece(ref, i):
            return ref[pl.ds(i * chunk, chunk), cols]

        for i in range(count):
            v_i, k_i = piece(v_ref, i), piece(k_ref, i)
            gk = lax.dot_general(v_i, qg_high, NT, preferred_element_type=jnp.float32)
            gk = gk + lax.dot_general(v_i, qg_low, NT, preferred_element_type=jnp.float32)
            gv = jnp.dot(k_i, qg_high, preferred_element_type=jnp.float32)
            gv = gv + jnp.dot(k_i, qg_low, preferred_element_type=jnp.float32)
            for j in range(i, count):
                keep = row <= col if j == i else None
                sgt = score(v_i, piece(g_ref, j), keep, scale)
                sft = score(k_i, piece(q_ref, j), keep, scale)
                gk = gk + jnp.dot(sgt, piece(q_ref, j), preferred_element_type=jnp.float32)
                gv = gv + jnp.dot(sft, piece(g_ref, j), preferred_element_type=jnp.float32)
            rows = pl.ds(i * chunk, chunk)
            gk_ref[rows, cols] = gk.astype(gk_ref.dtype)
            gv_ref[rows, cols] = gv.astype(gv_ref.dtype)


def head_call(kernel, scale, inputs, state, outputs, blocks, block_len, heads, flops, name):
    per_step = 2 if heads % 2 == 0 else 1
    tok = pl.BlockSpec((block_len, DH * per_step), lambda n, h: (n, h))
    st = pl.BlockSpec((1, per_step, DH, DH), lambda n, h: (n, h, 0, 0))
    rows, width = inputs[0].shape
    out = jax.ShapeDtypeStruct((rows, width), jnp.bfloat16)
    chunk = 256 if block_len % 256 == 0 else block_len
    return pl.pallas_call(
        lambda *refs: kernel(scale, chunk, per_step, *refs),
        grid=(blocks, heads // per_step),
        in_specs=[tok] * len(inputs) + [st],
        out_specs=[tok] * outputs,
        out_shape=[out] * outputs,
        cost_estimate=pl.CostEstimate(
            flops=flops, transcendentals=0, bytes_accessed=rows * width * 2 * (len(inputs) + outputs)
        ),
        name=name,
    )(*inputs, state)


def make_shards(ctx_size, head_size):
    def shards(queries, keys, values, output_grad, out_weight):
        row_count = queries.shape[0]
        width = queries.shape[1]
        heads = width // DH
        block_len = min(row_count, 512)
        blocks = row_count // block_len
        scale_factor = DH ** (-0.5)
        shape = (blocks, block_len, heads, DH)
        q_blocks = queries.reshape(shape)
        k_blocks = keys.reshape(shape)
        v_blocks = values.reshape(shape)
        grad_heads = project(output_grad, out_weight, ctx_size, head_size)
        grad_heads = grad_heads.astype(jnp.bfloat16)
        kv_blocks = jnp.einsum(
            "nshd,nshe->nhde", k_blocks, v_blocks,
            preferred_element_type=jnp.float32,
        )
        kv_running = jnp.cumsum(kv_blocks, axis=0)
        kv_before, _ = ctx_exclusive(kv_running[-1], ctx_size, False)
        if blocks == 1:
            kv_entry = kv_before[None]
        else:
            kv_entry = kv_before[None] + kv_running - kv_blocks
        g_blocks = grad_heads.reshape(shape)
        qg_blocks = jnp.einsum(
            "nthd,nthe->nhde", q_blocks, g_blocks, preferred_element_type=jnp.float32
        )
        qg_running = jnp.flip(jnp.cumsum(jnp.flip(qg_blocks, 0), axis=0), 0)
        pair_flops = blocks * heads * 2 * 2 * block_len * block_len * DH
        qg_after, gq = ctx_exclusive(
            qg_running[0], ctx_size, True,
            Cover(
                lambda g, kv: head_call(
                    query_kernel, scale_factor, (keys, values, g), kv, 1,
                    blocks, block_len, heads, pair_flops, "grad_queries",
                )[0],
                (grad_heads, kv_entry),
            ),
        )
        if blocks == 1:
            qg_entry = qg_after[None]
        else:
            qg_entry = qg_after[None] + qg_running - qg_blocks
        gk, gv = head_call(
            key_value_kernel, scale_factor, (queries, keys, values, grad_heads), qg_entry, 2,
            blocks, block_len, heads, 2 * pair_flops, "grad_keys_values",
        )
        return gq, gk, gv

    return shards


def solution(mesh):
    return jax.shard_map(
        make_shards(mesh.shape["ctx"], mesh.shape["head"]),
        mesh=mesh,
        in_specs=(
            P("ctx", "head"),
            P("ctx", "head"),
            P("ctx", "head"),
            P("ctx", "head"),
            P("head", None),
        ),
        out_specs=(P("ctx", "head"), P("ctx", "head"), P("ctx", "head")),
        check_vma=False,
    )
```

```python
import jax
import jax.numpy as jnp
from jax import lax
from jax.experimental import pallas as pl
from jax.sharding import PartitionSpec as P

DH = 128


def flip_pairs(n, bit):
    return [(a, a ^ bit) for a in range(n)]


def project(og, out_weight, ctx_size, head_size, tied):
    cols = og.shape[1]

    def weight_cols(source, lo, width):
        return lax.dynamic_slice_in_dim(out_weight, source * cols + lo, width, axis=1)

    def mm(a, b):
        return lax.dot_general(
            a, b, (((1,), (1,)), ((), ())), preferred_element_type=jnp.float32
        )

    if head_size != 4:
        full = lax.all_gather(og, "head", axis=1, tiled=True)
        full, tied = lax.optimization_barrier((full, tied))
        return mm(full, out_weight), tied
    me = lax.axis_index("head")
    core = lax.axis_index("ctx") % 2
    from_x = lax.ppermute(og, "head", flip_pairs(4, 1))
    from_y = lax.ppermute(og, "head", flip_pairs(4, 2))
    relayed = jnp.where(core == 0, from_x, from_y)
    devices = [(p, j) for p in range(ctx_size) for j in range(4)]
    route = [(p * 4 + j, p * 4 + (j ^ (2 if p % 2 == 0 else 1))) for p, j in devices]
    diag = lax.ppermute(relayed, ("ctx", "head"), route)
    diag, tied = lax.optimization_barrier((diag, tied))
    acc = mm(og, weight_cols(me, 0, cols))
    acc = acc + mm(from_x, weight_cols(me ^ 1, 0, cols))
    acc = acc + mm(from_y, weight_cols(me ^ 2, 0, cols))
    acc = acc + mm(diag, weight_cols(me ^ 3, 0, cols))
    return acc, tied


def ctx_exclusive(state, ctx_size, reverse, cover=None):
    core = lax.axis_index("ctx") % 2
    chips = ctx_size // 2
    rounded = state.astype(jnp.bfloat16)
    partner = lax.ppermute(rounded, "ctx", flip_pairs(ctx_size, 1)).astype(jnp.float32)
    chip_sum = rounded.astype(jnp.float32) + partner
    half = state.shape[1] // 2
    mine = lax.dynamic_slice_in_dim(chip_sum, core * half, half, axis=1)

    def pairs(step):
        if reverse:
            return [(2 * (z + step) + c, 2 * z + c) for z in range(chips - step) for c in range(2)]
        return [(2 * z + c, 2 * (z + step) + c) for z in range(chips - step) for c in range(2)]

    if cover is not None:
        mine, held = lax.optimization_barrier((mine, cover.args))
    others = jnp.zeros_like(mine)
    if chips <= 4:
        sent = mine.astype(jnp.bfloat16)
        for step in range(1, chips):
            others = others + lax.ppermute(sent, "ctx", pairs(step)).astype(jnp.float32)
    else:
        run = mine
        step = 1
        while step < chips:
            got = lax.ppermute(run.astype(jnp.bfloat16), "ctx", pairs(step)).astype(jnp.float32)
            run = run + got
            others = others + got
            step *= 2
    covered = None
    if cover is not None:
        covered = cover.fn(*held)
        others, covered = lax.optimization_barrier((others, covered))
    theirs = lax.ppermute(others, "ctx", flip_pairs(ctx_size, 1))
    lower = jnp.where(core == 0, others, theirs)
    upper = jnp.where(core == 0, theirs, others)
    chips_side = jnp.concatenate([lower, upper], axis=1)
    same_chip = (core == 0) if reverse else (core == 1)
    return chips_side + jnp.where(same_chip, partner, 0.0), covered


class Cover:
    def __init__(self, fn, args):
        self.fn = fn
        self.args = args


NT = (((1,), (1,)), ((), ()))


def split_state(state):
    high = state.astype(jnp.bfloat16)
    low = (state - high.astype(jnp.float32)).astype(jnp.bfloat16)
    return high, low


def scores_kernel(scale, chunk, per_step, q_ref, k_ref, v_ref, g_ref, kv_ref, gq_ref, gk_ref, gv_ref):
    length = q_ref.shape[0]
    count = length // chunk
    row = lax.broadcasted_iota(jnp.int32, (chunk, chunk), 0)
    col = lax.broadcasted_iota(jnp.int32, (chunk, chunk), 1)

    def score(a, b, keep):
        s = lax.dot_general(a, b, NT, preferred_element_type=jnp.float32) * scale
        if keep is not None:
            s = jnp.where(keep, s, 0.0)
        return s.astype(jnp.bfloat16)

    for h in range(per_step):
        cols = pl.ds(h * DH, DH)
        kv_high, kv_low = split_state(kv_ref[0, h] * scale)

        def piece(ref, i):
            return ref[pl.ds(i * chunk, chunk), cols]

        for i in range(count):
            rows = pl.ds(i * chunk, chunk)
            g_i = piece(g_ref, i)
            gq = lax.dot_general(g_i, kv_high, NT, preferred_element_type=jnp.float32)
            gq = gq + lax.dot_general(g_i, kv_low, NT, preferred_element_type=jnp.float32)
            for j in range(i + 1):
                sg = score(g_i, piece(v_ref, j), row >= col if j == i else None)
                term = jnp.dot(sg, piece(k_ref, j), preferred_element_type=jnp.float32)
                gq = gq + term
            gq_ref[rows, cols] = gq.astype(gq_ref.dtype)
            v_i, k_i = piece(v_ref, i), piece(k_ref, i)
            gk = None
            gv = None
            for j in range(i, count):
                keep = row <= col if j == i else None
                sgt = score(v_i, piece(g_ref, j), keep)
                sft = score(k_i, piece(q_ref, j), keep)
                term_k = jnp.dot(sgt, piece(q_ref, j), preferred_element_type=jnp.float32)
                term_v = jnp.dot(sft, piece(g_ref, j), preferred_element_type=jnp.float32)
                gk = term_k if gk is None else gk + term_k
                gv = term_v if gv is None else gv + term_v
            gk_ref[rows, cols] = gk.astype(gk_ref.dtype)
            gv_ref[rows, cols] = gv.astype(gv_ref.dtype)


def state_kernel(scale, per_step, k_ref, v_ref, qg_ref, gkp_ref, gvp_ref, gk_ref, gv_ref):
    for i in range(per_step):
        cols = pl.ds(i * DH, DH)
        k, v = k_ref[:, cols], v_ref[:, cols]
        qg_high, qg_low = split_state(qg_ref[0, i] * scale)
        gk = gkp_ref[:, cols].astype(jnp.float32)
        gk = gk + lax.dot_general(v, qg_high, NT, preferred_element_type=jnp.float32)
        gk = gk + lax.dot_general(v, qg_low, NT, preferred_element_type=jnp.float32)
        gv = gvp_ref[:, cols].astype(jnp.float32)
        gv = gv + jnp.dot(k, qg_high, preferred_element_type=jnp.float32)
        gv = gv + jnp.dot(k, qg_low, preferred_element_type=jnp.float32)
        gk_ref[:, cols] = gk.astype(jnp.bfloat16)
        gv_ref[:, cols] = gv.astype(jnp.bfloat16)


def attention_part(q, k, v, g, kv_state, blocks, block_len, heads, scale):
    per_step = 2 if heads % 2 == 0 else 1
    tok = pl.BlockSpec((block_len, DH * per_step), lambda n, h: (n, h))
    st = pl.BlockSpec((1, per_step, DH, DH), lambda n, h: (n, h, 0, 0))
    rows, width = q.shape
    out = jax.ShapeDtypeStruct((rows, width), jnp.bfloat16)
    chunk = 256 if block_len % 256 == 0 else block_len
    return pl.pallas_call(
        lambda *refs: scores_kernel(scale, chunk, per_step, *refs),
        grid=(blocks, heads // per_step),
        in_specs=[tok, tok, tok, tok, st],
        out_specs=[tok, tok, tok],
        out_shape=[out, out, out],
        cost_estimate=pl.CostEstimate(
            flops=blocks * heads * 6 * 2 * block_len * block_len * DH,
            transcendentals=0,
            bytes_accessed=rows * width * 14,
        ),
        name="attention_part",
    )(q, k, v, g, kv_state)


def state_part(k, v, qg_state, parts, blocks, block_len, heads, scale):
    per_step = 2 if heads % 2 == 0 else 1
    tok = pl.BlockSpec((block_len, DH * per_step), lambda n, h: (n, h))
    st = pl.BlockSpec((1, per_step, DH, DH), lambda n, h: (n, h, 0, 0))
    rows, width = k.shape
    out = jax.ShapeDtypeStruct((rows, width), jnp.bfloat16)
    return pl.pallas_call(
        lambda *refs: state_kernel(scale, per_step, *refs),
        grid=(blocks, heads // per_step),
        in_specs=[tok, tok, st, tok, tok],
        out_specs=[tok, tok],
        out_shape=[out, out],
        cost_estimate=pl.CostEstimate(
            flops=blocks * heads * 4 * 2 * block_len * DH * DH,
            transcendentals=0,
            bytes_accessed=rows * width * 12,
        ),
        name="state_part",
    )(k, v, qg_state, *parts)


def make_shards(ctx_size, head_size):
    def shards(queries, keys, values, output_grad, out_weight):
        row_count = queries.shape[0]
        width = queries.shape[1]
        heads = width // DH
        block_len = min(row_count, 512)
        blocks = row_count // block_len
        scale_factor = DH ** (-0.5)
        shape = (blocks, block_len, heads, DH)
        q_blocks = queries.reshape(shape)
        k_blocks = keys.reshape(shape)
        v_blocks = values.reshape(shape)
        kv_blocks = jnp.einsum(
            "nshd,nshe->nhde", k_blocks, v_blocks,
            preferred_element_type=jnp.float32,
        )
        kv_running = jnp.cumsum(kv_blocks, axis=0)
        kv_before, _ = ctx_exclusive(kv_running[-1], ctx_size, False)
        if blocks == 1:
            kv_entry = kv_before[None]
        else:
            kv_entry = kv_before[None] + kv_running - kv_blocks
        grad_heads, kv_entry = project(output_grad, out_weight, ctx_size, head_size, kv_entry)
        grad_heads = grad_heads.astype(jnp.bfloat16)
        g_blocks = grad_heads.reshape(shape)
        qg_blocks = jnp.einsum(
            "nthd,nthe->nhde", q_blocks, g_blocks, preferred_element_type=jnp.float32
        )
        qg_running = jnp.flip(jnp.cumsum(jnp.flip(qg_blocks, 0), axis=0), 0)
        qg_after, (gq, gk_part, gv_part) = ctx_exclusive(
            qg_running[0], ctx_size, True,
            Cover(
                lambda g, kv: attention_part(
                    queries, keys, values, g, kv, blocks, block_len, heads, scale_factor
                ),
                (grad_heads, kv_entry),
            ),
        )
        if blocks == 1:
            qg_entry = qg_after[None]
        else:
            qg_entry = qg_after[None] + qg_running - qg_blocks
        gk, gv = state_part(
            keys, values, qg_entry, (gk_part, gv_part), blocks, block_len, heads, scale_factor
        )
        return gq, gk, gv

    return shards


def solution(mesh):
    return jax.shard_map(
        make_shards(mesh.shape["ctx"], mesh.shape["head"]),
        mesh=mesh,
        in_specs=(
            P("ctx", "head"),
            P("ctx", "head"),
            P("ctx", "head"),
            P("ctx", "head"),
            P("head", None),
        ),
        out_specs=(P("ctx", "head"), P("ctx", "head"), P("ctx", "head")),
        check_vma=False,
    )
```

```python
import jax
import jax.numpy as jnp
from jax import lax
from jax.experimental import pallas as pl
from jax.sharding import PartitionSpec as P

DH = 128


def flip_pairs(n, bit):
    return [(a, a ^ bit) for a in range(n)]


def project(og, out_weight, ctx_size, head_size, tied):
    cols = og.shape[1]

    def weight_cols(source, lo, width):
        return lax.dynamic_slice_in_dim(out_weight, source * cols + lo, width, axis=1)

    def mm(a, b):
        return lax.dot_general(
            a, b, (((1,), (1,)), ((), ())), preferred_element_type=jnp.float32
        )

    if head_size != 4:
        full = lax.all_gather(og, "head", axis=1, tiled=True)
        full, tied = lax.optimization_barrier((full, tied))
        return mm(full, out_weight), tied
    me = lax.axis_index("head")
    core = lax.axis_index("ctx") % 2
    devices = [(p, j) for p in range(ctx_size) for j in range(4)]

    def route(core_0_bit, core_1_bit):
        return [(p * 4 + j, p * 4 + (j ^ (core_0_bit if p % 2 == 0 else core_1_bit))) for p, j in devices]

    to_relay = lax.ppermute(og, ("ctx", "head"), route(1, 2))
    kept = lax.ppermute(og, ("ctx", "head"), route(2, 1))
    diag = lax.ppermute(to_relay, ("ctx", "head"), route(2, 1))
    diag, tied = lax.optimization_barrier((diag, tied))
    acc = mm(og, weight_cols(me, 0, cols))
    acc = acc + mm(to_relay, weight_cols(me ^ (1 + core), 0, cols))
    acc = acc + mm(kept, weight_cols(me ^ (2 - core), 0, cols))
    acc = acc + mm(diag, weight_cols(me ^ 3, 0, cols))
    return acc, tied


def ctx_exclusive(state, ctx_size, reverse, cover=None):
    core = lax.axis_index("ctx") % 2
    chips = ctx_size // 2
    rounded = state.astype(jnp.bfloat16)
    partner = lax.ppermute(rounded, "ctx", flip_pairs(ctx_size, 1)).astype(jnp.float32)
    chip_sum = rounded.astype(jnp.float32) + partner
    half = state.shape[1] // 2
    mine = lax.dynamic_slice_in_dim(chip_sum, core * half, half, axis=1)

    def pairs(step):
        if reverse:
            return [(2 * (z + step) + c, 2 * z + c) for z in range(chips - step) for c in range(2)]
        return [(2 * z + c, 2 * (z + step) + c) for z in range(chips - step) for c in range(2)]

    if cover is not None:
        mine, held = lax.optimization_barrier((mine, cover.args))
    others = jnp.zeros_like(mine)
    if chips <= 4:
        sent = mine.astype(jnp.bfloat16)
        for step in range(1, chips):
            others = others + lax.ppermute(sent, "ctx", pairs(step)).astype(jnp.float32)
    else:
        run = mine
        step = 1
        while step < chips:
            got = lax.ppermute(run.astype(jnp.bfloat16), "ctx", pairs(step)).astype(jnp.float32)
            run = run + got
            others = others + got
            step *= 2
    covered = None
    if cover is not None:
        covered = cover.fn(*held)
        others, covered = lax.optimization_barrier((others, covered))
    theirs = lax.ppermute(others, "ctx", flip_pairs(ctx_size, 1))
    lower = jnp.where(core == 0, others, theirs)
    upper = jnp.where(core == 0, theirs, others)
    chips_side = jnp.concatenate([lower, upper], axis=1)
    same_chip = (core == 0) if reverse else (core == 1)
    return chips_side + jnp.where(same_chip, partner, 0.0), covered


class Cover:
    def __init__(self, fn, args):
        self.fn = fn
        self.args = args


NT = (((1,), (1,)), ((), ()))


def split_state(state):
    high = state.astype(jnp.bfloat16)
    low = (state - high.astype(jnp.float32)).astype(jnp.bfloat16)
    return high, low


def scores_kernel(scale, chunk, per_step, q_ref, k_ref, v_ref, g_ref, kv_ref, gq_ref, gk_ref, gv_ref):
    length = q_ref.shape[0]
    count = length // chunk
    row = lax.broadcasted_iota(jnp.int32, (chunk, chunk), 0)
    col = lax.broadcasted_iota(jnp.int32, (chunk, chunk), 1)

    def score(a, b, keep):
        s = lax.dot_general(a, b, NT, preferred_element_type=jnp.float32) * scale
        if keep is not None:
            s = jnp.where(keep, s, 0.0)
        return s.astype(jnp.bfloat16)

    for h in range(per_step):
        cols = pl.ds(h * DH, DH)
        kv_high, kv_low = split_state(kv_ref[0, h] * scale)

        def piece(ref, i):
            return ref[pl.ds(i * chunk, chunk), cols]

        for i in range(count):
            rows = pl.ds(i * chunk, chunk)
            g_i = piece(g_ref, i)
            gq = lax.dot_general(g_i, kv_high, NT, preferred_element_type=jnp.float32)
            gq = gq + lax.dot_general(g_i, kv_low, NT, preferred_element_type=jnp.float32)
            for j in range(i + 1):
                sg = score(g_i, piece(v_ref, j), row >= col if j == i else None)
                term = jnp.dot(sg, piece(k_ref, j), preferred_element_type=jnp.float32)
                gq = gq + term
            gq_ref[rows, cols] = gq.astype(gq_ref.dtype)
            v_i, k_i = piece(v_ref, i), piece(k_ref, i)
            gk = None
            gv = None
            for j in range(i, count):
                keep = row <= col if j == i else None
                sgt = score(v_i, piece(g_ref, j), keep)
                sft = score(k_i, piece(q_ref, j), keep)
                term_k = jnp.dot(sgt, piece(q_ref, j), preferred_element_type=jnp.float32)
                term_v = jnp.dot(sft, piece(g_ref, j), preferred_element_type=jnp.float32)
                gk = term_k if gk is None else gk + term_k
                gv = term_v if gv is None else gv + term_v
            gk_ref[rows, cols] = gk.astype(gk_ref.dtype)
            gv_ref[rows, cols] = gv.astype(gv_ref.dtype)


def state_kernel(scale, per_step, k_ref, v_ref, qg_ref, gkp_ref, gvp_ref, gk_ref, gv_ref):
    for i in range(per_step):
        cols = pl.ds(i * DH, DH)
        k, v = k_ref[:, cols], v_ref[:, cols]
        qg_high, qg_low = split_state(qg_ref[0, i] * scale)
        gk = gkp_ref[:, cols].astype(jnp.float32)
        gk = gk + lax.dot_general(v, qg_high, NT, preferred_element_type=jnp.float32)
        gk = gk + lax.dot_general(v, qg_low, NT, preferred_element_type=jnp.float32)
        gv = gvp_ref[:, cols].astype(jnp.float32)
        gv = gv + jnp.dot(k, qg_high, preferred_element_type=jnp.float32)
        gv = gv + jnp.dot(k, qg_low, preferred_element_type=jnp.float32)
        gk_ref[:, cols] = gk.astype(jnp.bfloat16)
        gv_ref[:, cols] = gv.astype(jnp.bfloat16)


def attention_part(q, k, v, g, kv_state, blocks, block_len, heads, scale):
    per_step = 2 if heads % 2 == 0 else 1
    tok = pl.BlockSpec((block_len, DH * per_step), lambda n, h: (n, h))
    st = pl.BlockSpec((1, per_step, DH, DH), lambda n, h: (n, h, 0, 0))
    rows, width = q.shape
    out = jax.ShapeDtypeStruct((rows, width), jnp.bfloat16)
    chunk = block_len
    return pl.pallas_call(
        lambda *refs: scores_kernel(scale, chunk, per_step, *refs),
        grid=(blocks, heads // per_step),
        in_specs=[tok, tok, tok, tok, st],
        out_specs=[tok, tok, tok],
        out_shape=[out, out, out],
        cost_estimate=pl.CostEstimate(
            flops=blocks * heads * 6 * 2 * block_len * block_len * DH,
            transcendentals=0,
            bytes_accessed=rows * width * 14,
        ),
        name="attention_part",
    )(q, k, v, g, kv_state)


def state_part(k, v, qg_state, parts, blocks, block_len, heads, scale):
    per_step = 2 if heads % 2 == 0 else 1
    tok = pl.BlockSpec((block_len, DH * per_step), lambda n, h: (n, h))
    st = pl.BlockSpec((1, per_step, DH, DH), lambda n, h: (n, h, 0, 0))
    rows, width = k.shape
    out = jax.ShapeDtypeStruct((rows, width), jnp.bfloat16)
    return pl.pallas_call(
        lambda *refs: state_kernel(scale, per_step, *refs),
        grid=(blocks, heads // per_step),
        in_specs=[tok, tok, st, tok, tok],
        out_specs=[tok, tok],
        out_shape=[out, out],
        cost_estimate=pl.CostEstimate(
            flops=blocks * heads * 4 * 2 * block_len * DH * DH,
            transcendentals=0,
            bytes_accessed=rows * width * 12,
        ),
        name="state_part",
    )(k, v, qg_state, *parts)


def make_shards(ctx_size, head_size):
    def shards(queries, keys, values, output_grad, out_weight):
        row_count = queries.shape[0]
        width = queries.shape[1]
        heads = width // DH
        block_len = min(row_count, 512)
        blocks = row_count // block_len
        scale_factor = DH ** (-0.5)
        shape = (blocks, block_len, heads, DH)
        q_blocks = queries.reshape(shape)
        k_blocks = keys.reshape(shape)
        v_blocks = values.reshape(shape)
        kv_blocks = jnp.einsum(
            "nshd,nshe->nhde", k_blocks, v_blocks,
            preferred_element_type=jnp.float32,
        )
        kv_running = jnp.cumsum(kv_blocks, axis=0)
        kv_before, _ = ctx_exclusive(kv_running[-1], ctx_size, False)
        if blocks == 1:
            kv_entry = kv_before[None]
        else:
            kv_entry = kv_before[None] + kv_running - kv_blocks
        grad_heads, kv_entry = project(output_grad, out_weight, ctx_size, head_size, kv_entry)
        grad_heads = grad_heads.astype(jnp.bfloat16)
        g_blocks = grad_heads.reshape(shape)
        qg_blocks = jnp.einsum(
            "nthd,nthe->nhde", q_blocks, g_blocks, preferred_element_type=jnp.float32
        )
        qg_running = jnp.flip(jnp.cumsum(jnp.flip(qg_blocks, 0), axis=0), 0)
        qg_after, (gq, gk_part, gv_part) = ctx_exclusive(
            qg_running[0], ctx_size, True,
            Cover(
                lambda g, kv: attention_part(
                    queries, keys, values, g, kv, blocks, block_len, heads, scale_factor
                ),
                (grad_heads, kv_entry),
            ),
        )
        if blocks == 1:
            qg_entry = qg_after[None]
        else:
            qg_entry = qg_after[None] + qg_running - qg_blocks
        gk, gv = state_part(
            keys, values, qg_entry, (gk_part, gv_part), blocks, block_len, heads, scale_factor
        )
        return gq, gk, gv

    return shards


def solution(mesh):
    return jax.shard_map(
        make_shards(mesh.shape["ctx"], mesh.shape["head"]),
        mesh=mesh,
        in_specs=(
            P("ctx", "head"),
            P("ctx", "head"),
            P("ctx", "head"),
            P("ctx", "head"),
            P("head", None),
        ),
        out_specs=(P("ctx", "head"), P("ctx", "head"), P("ctx", "head")),
        check_vma=False,
    )
```

```python
import jax
import jax.numpy as jnp
from jax import lax
from jax.experimental import pallas as pl
from jax.sharding import PartitionSpec as P

DH = 128


def flip_pairs(n, bit):
    return [(a, a ^ bit) for a in range(n)]


def project(og, out_weight, ctx_size, head_size, tied, early):
    cols = og.shape[1]

    def weight_cols(source, lo, width):
        return lax.dynamic_slice_in_dim(out_weight, source * cols + lo, width, axis=1)

    def mm(a, b):
        return lax.dot_general(
            a, b, (((1,), (1,)), ((), ())), preferred_element_type=jnp.float32
        )

    if head_size != 4:
        full = lax.all_gather(og, "head", axis=1, tiled=True)
        early = early[0](*early[1:])
        full, tied = lax.optimization_barrier((full, tied))
        return mm(full, out_weight), tied, early
    me = lax.axis_index("head")
    core = lax.axis_index("ctx") % 2
    devices = [(p, j) for p in range(ctx_size) for j in range(4)]

    def route(core_0_bit, core_1_bit):
        return [(p * 4 + j, p * 4 + (j ^ (core_0_bit if p % 2 == 0 else core_1_bit))) for p, j in devices]

    to_relay = lax.ppermute(og, ("ctx", "head"), route(1, 2))
    kept = lax.ppermute(og, ("ctx", "head"), route(2, 1))
    to_relay, early_args = lax.optimization_barrier((to_relay, early[1:]))
    early = early[0](*early_args)
    diag = lax.ppermute(to_relay, ("ctx", "head"), route(2, 1))
    diag, tied, early = lax.optimization_barrier((diag, tied, early))
    acc = mm(og, weight_cols(me, 0, cols))
    acc = acc + mm(to_relay, weight_cols(me ^ (1 + core), 0, cols))
    acc = acc + mm(kept, weight_cols(me ^ (2 - core), 0, cols))
    acc = acc + mm(diag, weight_cols(me ^ 3, 0, cols))
    return acc, tied, early


def ctx_exclusive(state, ctx_size, reverse, cover=None):
    core = lax.axis_index("ctx") % 2
    chips = ctx_size // 2
    rounded = state.astype(jnp.bfloat16)
    partner = lax.ppermute(rounded, "ctx", flip_pairs(ctx_size, 1)).astype(jnp.float32)
    chip_sum = rounded.astype(jnp.float32) + partner
    half = state.shape[1] // 2
    mine = lax.dynamic_slice_in_dim(chip_sum, core * half, half, axis=1)

    def pairs(step):
        if reverse:
            return [(2 * (z + step) + c, 2 * z + c) for z in range(chips - step) for c in range(2)]
        return [(2 * z + c, 2 * (z + step) + c) for z in range(chips - step) for c in range(2)]

    if cover is not None:
        mine, held = lax.optimization_barrier((mine, cover.args))
    others = jnp.zeros_like(mine)
    if chips <= 4:
        sent = mine.astype(jnp.bfloat16)
        for step in range(1, chips):
            others = others + lax.ppermute(sent, "ctx", pairs(step)).astype(jnp.float32)
    else:
        run = mine
        step = 1
        while step < chips:
            got = lax.ppermute(run.astype(jnp.bfloat16), "ctx", pairs(step)).astype(jnp.float32)
            run = run + got
            others = others + got
            step *= 2
    covered = None
    if cover is not None:
        covered = cover.fn(*held)
        others, covered = lax.optimization_barrier((others, covered))
    theirs = lax.ppermute(others, "ctx", flip_pairs(ctx_size, 1))
    lower = jnp.where(core == 0, others, theirs)
    upper = jnp.where(core == 0, theirs, others)
    chips_side = jnp.concatenate([lower, upper], axis=1)
    same_chip = (core == 0) if reverse else (core == 1)
    return chips_side + jnp.where(same_chip, partner, 0.0), covered


class Cover:
    def __init__(self, fn, args):
        self.fn = fn
        self.args = args


NT = (((1,), (1,)), ((), ()))


def split_state(state):
    high = state.astype(jnp.bfloat16)
    low = (state - high.astype(jnp.float32)).astype(jnp.bfloat16)
    return high, low


def scores_kernel(scale, chunk, per_step, q_ref, k_ref, v_ref, g_ref, kv_ref, gq_ref, gk_ref, gv_ref):
    length = q_ref.shape[0]
    count = length // chunk
    row = lax.broadcasted_iota(jnp.int32, (chunk, chunk), 0)
    col = lax.broadcasted_iota(jnp.int32, (chunk, chunk), 1)

    def score(a, b, keep):
        s = lax.dot_general(a, b, NT, preferred_element_type=jnp.float32) * scale
        if keep is not None:
            s = jnp.where(keep, s, 0.0)
        return s.astype(jnp.bfloat16)

    for h in range(per_step):
        cols = pl.ds(h * DH, DH)
        kv_high, kv_low = split_state(kv_ref[0, h] * scale)

        def piece(ref, i):
            return ref[pl.ds(i * chunk, chunk), cols]

        for i in range(count):
            rows = pl.ds(i * chunk, chunk)
            g_i = piece(g_ref, i)
            gq = lax.dot_general(g_i, kv_high, NT, preferred_element_type=jnp.float32)
            gq = gq + lax.dot_general(g_i, kv_low, NT, preferred_element_type=jnp.float32)
            for j in range(i + 1):
                sg = score(g_i, piece(v_ref, j), row >= col if j == i else None)
                term = jnp.dot(sg, piece(k_ref, j), preferred_element_type=jnp.float32)
                gq = gq + term
            gq_ref[rows, cols] = gq.astype(gq_ref.dtype)
            v_i, k_i = piece(v_ref, i), piece(k_ref, i)
            gk = None
            gv = None
            for j in range(i, count):
                keep = row <= col if j == i else None
                sgt = score(v_i, piece(g_ref, j), keep)
                sft = score(k_i, piece(q_ref, j), keep)
                term_k = jnp.dot(sgt, piece(q_ref, j), preferred_element_type=jnp.float32)
                term_v = jnp.dot(sft, piece(g_ref, j), preferred_element_type=jnp.float32)
                gk = term_k if gk is None else gk + term_k
                gv = term_v if gv is None else gv + term_v
            gk_ref[rows, cols] = gk.astype(gk_ref.dtype)
            gv_ref[rows, cols] = gv.astype(gv_ref.dtype)


def state_kernel(scale, per_step, k_ref, v_ref, qg_ref, gkp_ref, gvp_ref, gk_ref, gv_ref):
    for i in range(per_step):
        cols = pl.ds(i * DH, DH)
        k, v = k_ref[:, cols], v_ref[:, cols]
        qg_high, qg_low = split_state(qg_ref[0, i] * scale)
        gk = gkp_ref[:, cols].astype(jnp.float32)
        gk = gk + lax.dot_general(v, qg_high, NT, preferred_element_type=jnp.float32)
        gk = gk + lax.dot_general(v, qg_low, NT, preferred_element_type=jnp.float32)
        gv = gvp_ref[:, cols].astype(jnp.float32)
        gv = gv + jnp.dot(k, qg_high, preferred_element_type=jnp.float32)
        gv = gv + jnp.dot(k, qg_low, preferred_element_type=jnp.float32)
        gk_ref[:, cols] = gk.astype(jnp.bfloat16)
        gv_ref[:, cols] = gv.astype(jnp.bfloat16)


def attention_part(q, k, v, g, kv_state, blocks, block_len, heads, scale):
    per_step = 2 if heads % 2 == 0 else 1
    tok = pl.BlockSpec((block_len, DH * per_step), lambda n, h: (n, h))
    st = pl.BlockSpec((1, per_step, DH, DH), lambda n, h: (n, h, 0, 0))
    rows, width = q.shape
    out = jax.ShapeDtypeStruct((rows, width), jnp.bfloat16)
    chunk = block_len
    return pl.pallas_call(
        lambda *refs: scores_kernel(scale, chunk, per_step, *refs),
        grid=(blocks, heads // per_step),
        in_specs=[tok, tok, tok, tok, st],
        out_specs=[tok, tok, tok],
        out_shape=[out, out, out],
        cost_estimate=pl.CostEstimate(
            flops=blocks * heads * 6 * 2 * block_len * block_len * DH,
            transcendentals=0,
            bytes_accessed=rows * width * 14,
        ),
        name="attention_part",
    )(q, k, v, g, kv_state)


def state_part(k, v, qg_state, parts, blocks, block_len, heads, scale):
    per_step = 2 if heads % 2 == 0 else 1
    tok = pl.BlockSpec((block_len, DH * per_step), lambda n, h: (n, h))
    st = pl.BlockSpec((1, per_step, DH, DH), lambda n, h: (n, h, 0, 0))
    rows, width = k.shape
    out = jax.ShapeDtypeStruct((rows, width), jnp.bfloat16)
    return pl.pallas_call(
        lambda *refs: state_kernel(scale, per_step, *refs),
        grid=(blocks, heads // per_step),
        in_specs=[tok, tok, st, tok, tok],
        out_specs=[tok, tok],
        out_shape=[out, out],
        cost_estimate=pl.CostEstimate(
            flops=blocks * heads * 4 * 2 * block_len * DH * DH,
            transcendentals=0,
            bytes_accessed=rows * width * 12,
        ),
        name="state_part",
    )(k, v, qg_state, *parts)


def make_shards(ctx_size, head_size):
    def shards(queries, keys, values, output_grad, out_weight):
        row_count = queries.shape[0]
        width = queries.shape[1]
        heads = width // DH
        block_len = min(row_count, 512)
        blocks = row_count // block_len
        scale_factor = DH ** (-0.5)
        shape = (blocks, block_len, heads, DH)
        q_blocks = queries.reshape(shape)
        k_blocks = keys.reshape(shape)
        v_blocks = values.reshape(shape)
        def kv_state(k, v):
            kv_blocks = jnp.einsum(
                "nshd,nshe->nhde", k.reshape(shape), v.reshape(shape),
                preferred_element_type=jnp.float32,
            )
            kv_running = jnp.cumsum(kv_blocks, axis=0)
            kv_before, _ = ctx_exclusive(kv_running[-1], ctx_size, False)
            if blocks == 1:
                return kv_before[None]
            return kv_before[None] + kv_running - kv_blocks

        grad_heads, _, kv_entry = project(
            output_grad, out_weight, ctx_size, head_size, (), (kv_state, keys, values)
        )
        grad_heads = grad_heads.astype(jnp.bfloat16)
        g_blocks = grad_heads.reshape(shape)
        qg_blocks = jnp.einsum(
            "nthd,nthe->nhde", q_blocks, g_blocks, preferred_element_type=jnp.float32
        )
        qg_running = jnp.flip(jnp.cumsum(jnp.flip(qg_blocks, 0), axis=0), 0)
        qg_after, (gq, gk_part, gv_part) = ctx_exclusive(
            qg_running[0], ctx_size, True,
            Cover(
                lambda g, kv: attention_part(
                    queries, keys, values, g, kv, blocks, block_len, heads, scale_factor
                ),
                (grad_heads, kv_entry),
            ),
        )
        if blocks == 1:
            qg_entry = qg_after[None]
        else:
            qg_entry = qg_after[None] + qg_running - qg_blocks
        gk, gv = state_part(
            keys, values, qg_entry, (gk_part, gv_part), blocks, block_len, heads, scale_factor
        )
        return gq, gk, gv

    return shards


def solution(mesh):
    return jax.shard_map(
        make_shards(mesh.shape["ctx"], mesh.shape["head"]),
        mesh=mesh,
        in_specs=(
            P("ctx", "head"),
            P("ctx", "head"),
            P("ctx", "head"),
            P("ctx", "head"),
            P("head", None),
        ),
        out_specs=(P("ctx", "head"), P("ctx", "head"), P("ctx", "head")),
        check_vma=False,
    )
```

```python
import jax
import jax.numpy as jnp
from jax import lax
from jax.experimental import pallas as pl
from jax.sharding import PartitionSpec as P

DH = 128


def flip_pairs(n, bit):
    return [(a, a ^ bit) for a in range(n)]


def project(og, out_weight, ctx_size, head_size, tied):
    cols = og.shape[1]

    def weight_cols(source, lo, width):
        return lax.dynamic_slice_in_dim(out_weight, source * cols + lo, width, axis=1)

    def mm(a, b):
        return lax.dot_general(
            a, b, (((1,), (1,)), ((), ())), preferred_element_type=jnp.float32
        )

    if head_size != 4:
        full = lax.all_gather(og, "head", axis=1, tiled=True)
        full, tied = lax.optimization_barrier((full, tied))
        return mm(full, out_weight), tied
    me = lax.axis_index("head")
    core = lax.axis_index("ctx") % 2
    devices = [(p, j) for p in range(ctx_size) for j in range(4)]

    def route(core_0_bit, core_1_bit):
        return [(p * 4 + j, p * 4 + (j ^ (core_0_bit if p % 2 == 0 else core_1_bit))) for p, j in devices]

    to_relay = lax.ppermute(og, ("ctx", "head"), route(1, 2))
    kept = lax.ppermute(og, ("ctx", "head"), route(2, 1))
    diag = lax.ppermute(to_relay, ("ctx", "head"), route(2, 1))
    diag, tied = lax.optimization_barrier((diag, tied))
    acc = mm(og, weight_cols(me, 0, cols))
    acc = acc + mm(to_relay, weight_cols(me ^ (1 + core), 0, cols))
    acc = acc + mm(kept, weight_cols(me ^ (2 - core), 0, cols))
    acc = acc + mm(diag, weight_cols(me ^ 3, 0, cols))
    return acc, tied


def ctx_exclusive(state, ctx_size, reverse, cover=None):
    core = lax.axis_index("ctx") % 2
    chips = ctx_size // 2
    rounded = state.astype(jnp.bfloat16)
    partner = lax.ppermute(rounded, "ctx", flip_pairs(ctx_size, 1)).astype(jnp.float32)
    chip_sum = rounded.astype(jnp.float32) + partner
    half = state.shape[1] // 2
    mine = lax.dynamic_slice_in_dim(chip_sum, core * half, half, axis=1)

    def pairs(step):
        if reverse:
            return [(2 * (z + step) + c, 2 * z + c) for z in range(chips - step) for c in range(2)]
        return [(2 * z + c, 2 * (z + step) + c) for z in range(chips - step) for c in range(2)]

    if cover is not None:
        mine, held = lax.optimization_barrier((mine, cover.args))
    others = jnp.zeros_like(mine)
    if chips <= 4:
        sent = mine.astype(jnp.bfloat16)
        for step in range(1, chips):
            others = others + lax.ppermute(sent, "ctx", pairs(step)).astype(jnp.float32)
    else:
        run = mine
        step = 1
        while step < chips:
            got = lax.ppermute(run.astype(jnp.bfloat16), "ctx", pairs(step)).astype(jnp.float32)
            run = run + got
            others = others + got
            step *= 2
    covered = None
    if cover is not None:
        covered = cover.fn(*held)
        others, covered = lax.optimization_barrier((others, covered))
    theirs = lax.ppermute(others, "ctx", flip_pairs(ctx_size, 1))
    lower = jnp.where(core == 0, others, theirs)
    upper = jnp.where(core == 0, theirs, others)
    chips_side = jnp.concatenate([lower, upper], axis=1)
    same_chip = (core == 0) if reverse else (core == 1)
    return chips_side + jnp.where(same_chip, partner, 0.0), covered


class Cover:
    def __init__(self, fn, args):
        self.fn = fn
        self.args = args


NT = (((1,), (1,)), ((), ()))
TN = (((0,), (0,)), ((), ()))


def split_state(state):
    high = state.astype(jnp.bfloat16)
    low = (state - high.astype(jnp.float32)).astype(jnp.bfloat16)
    return high, low


def scores_kernel(scale, per_step, q_ref, k_ref, v_ref, g_ref, kv_ref, gq_ref, gk_ref, gv_ref):
    length = q_ref.shape[0]
    row = lax.broadcasted_iota(jnp.int32, (length, length), 0)
    col = lax.broadcasted_iota(jnp.int32, (length, length), 1)
    lower = row >= col
    for h in range(per_step):
        cols = pl.ds(h * DH, DH)
        q, k, v, g = q_ref[:, cols], k_ref[:, cols], v_ref[:, cols], g_ref[:, cols]
        kv_high, kv_low = split_state(kv_ref[0, h] * scale)
        score_grad = lax.dot_general(g, v, NT, preferred_element_type=jnp.float32) * scale
        score_grad = jnp.where(lower, score_grad, 0.0).astype(jnp.bfloat16)
        score_fwd = lax.dot_general(q, k, NT, preferred_element_type=jnp.float32) * scale
        score_fwd = jnp.where(lower, score_fwd, 0.0).astype(jnp.bfloat16)
        gq = lax.dot_general(g, kv_high, NT, preferred_element_type=jnp.float32)
        gq = gq + lax.dot_general(g, kv_low, NT, preferred_element_type=jnp.float32)
        gq = gq + jnp.dot(score_grad, k, preferred_element_type=jnp.float32)
        gq_ref[:, cols] = gq.astype(gq_ref.dtype)
        gk_t = lax.dot_general(q, score_grad, TN, preferred_element_type=jnp.float32)
        gv_t = lax.dot_general(g, score_fwd, TN, preferred_element_type=jnp.float32)
        gk_ref[:, cols] = gk_t.T.astype(gk_ref.dtype)
        gv_ref[:, cols] = gv_t.T.astype(gv_ref.dtype)


def state_kernel(scale, per_step, k_ref, v_ref, qg_ref, gkp_ref, gvp_ref, gk_ref, gv_ref):
    for i in range(per_step):
        cols = pl.ds(i * DH, DH)
        k, v = k_ref[:, cols], v_ref[:, cols]
        qg_high, qg_low = split_state(qg_ref[0, i] * scale)
        gk = gkp_ref[:, cols].astype(jnp.float32)
        gk = gk + lax.dot_general(v, qg_high, NT, preferred_element_type=jnp.float32)
        gk = gk + lax.dot_general(v, qg_low, NT, preferred_element_type=jnp.float32)
        gv = gvp_ref[:, cols].astype(jnp.float32)
        gv = gv + jnp.dot(k, qg_high, preferred_element_type=jnp.float32)
        gv = gv + jnp.dot(k, qg_low, preferred_element_type=jnp.float32)
        gk_ref[:, cols] = gk.astype(jnp.bfloat16)
        gv_ref[:, cols] = gv.astype(jnp.bfloat16)


def attention_part(q, k, v, g, kv_state, blocks, block_len, heads, scale):
    per_step = 2 if heads % 2 == 0 else 1
    tok = pl.BlockSpec((block_len, DH * per_step), lambda n, h: (n, h))
    st = pl.BlockSpec((1, per_step, DH, DH), lambda n, h: (n, h, 0, 0))
    rows, width = q.shape
    out = jax.ShapeDtypeStruct((rows, width), jnp.bfloat16)
    return pl.pallas_call(
        lambda *refs: scores_kernel(scale, per_step, *refs),
        grid=(blocks, heads // per_step),
        in_specs=[tok, tok, tok, tok, st],
        out_specs=[tok, tok, tok],
        out_shape=[out, out, out],
        cost_estimate=pl.CostEstimate(
            flops=blocks * heads * 6 * 2 * block_len * block_len * DH,
            transcendentals=0,
            bytes_accessed=rows * width * 14,
        ),
        name="attention_part",
    )(q, k, v, g, kv_state)


def state_part(k, v, qg_state, parts, blocks, block_len, heads, scale):
    per_step = 2 if heads % 2 == 0 else 1
    tok = pl.BlockSpec((block_len, DH * per_step), lambda n, h: (n, h))
    st = pl.BlockSpec((1, per_step, DH, DH), lambda n, h: (n, h, 0, 0))
    rows, width = k.shape
    out = jax.ShapeDtypeStruct((rows, width), jnp.bfloat16)
    return pl.pallas_call(
        lambda *refs: state_kernel(scale, per_step, *refs),
        grid=(blocks, heads // per_step),
        in_specs=[tok, tok, st, tok, tok],
        out_specs=[tok, tok],
        out_shape=[out, out],
        cost_estimate=pl.CostEstimate(
            flops=blocks * heads * 4 * 2 * block_len * DH * DH,
            transcendentals=0,
            bytes_accessed=rows * width * 12,
        ),
        name="state_part",
    )(k, v, qg_state, *parts)


def make_shards(ctx_size, head_size):
    def shards(queries, keys, values, output_grad, out_weight):
        row_count = queries.shape[0]
        width = queries.shape[1]
        heads = width // DH
        block_len = min(row_count, 512)
        blocks = row_count // block_len
        scale_factor = DH ** (-0.5)
        shape = (blocks, block_len, heads, DH)
        q_blocks = queries.reshape(shape)
        k_blocks = keys.reshape(shape)
        v_blocks = values.reshape(shape)
        kv_blocks = jnp.einsum(
            "nshd,nshe->nhde", k_blocks, v_blocks,
            preferred_element_type=jnp.float32,
        )
        kv_running = jnp.cumsum(kv_blocks, axis=0)
        kv_before, _ = ctx_exclusive(kv_running[-1], ctx_size, False)
        if blocks == 1:
            kv_entry = kv_before[None]
        else:
            kv_entry = kv_before[None] + kv_running - kv_blocks
        grad_heads, kv_entry = project(output_grad, out_weight, ctx_size, head_size, kv_entry)
        grad_heads = grad_heads.astype(jnp.bfloat16)
        g_blocks = grad_heads.reshape(shape)
        qg_blocks = jnp.einsum(
            "nthd,nthe->nhde", q_blocks, g_blocks, preferred_element_type=jnp.float32
        )
        qg_running = jnp.flip(jnp.cumsum(jnp.flip(qg_blocks, 0), axis=0), 0)
        qg_after, (gq, gk_part, gv_part) = ctx_exclusive(
            qg_running[0], ctx_size, True,
            Cover(
                lambda g, kv: attention_part(
                    queries, keys, values, g, kv, blocks, block_len, heads, scale_factor
                ),
                (grad_heads, kv_entry),
            ),
        )
        if blocks == 1:
            qg_entry = qg_after[None]
        else:
            qg_entry = qg_after[None] + qg_running - qg_blocks
        gk, gv = state_part(
            keys, values, qg_entry, (gk_part, gv_part), blocks, block_len, heads, scale_factor
        )
        return gq, gk, gv

    return shards


def solution(mesh):
    return jax.shard_map(
        make_shards(mesh.shape["ctx"], mesh.shape["head"]),
        mesh=mesh,
        in_specs=(
            P("ctx", "head"),
            P("ctx", "head"),
            P("ctx", "head"),
            P("ctx", "head"),
            P("head", None),
        ),
        out_specs=(P("ctx", "head"), P("ctx", "head"), P("ctx", "head")),
        check_vma=False,
    )
```

```python
import jax
import jax.numpy as jnp
from jax import lax
from jax.experimental import pallas as pl
from jax.sharding import PartitionSpec as P

DH = 128


def flip_pairs(n, bit):
    return [(a, a ^ bit) for a in range(n)]


def project(og, out_weight, ctx_size, head_size, tied):
    cols = og.shape[1]

    def weight_cols(source, lo, width):
        return lax.dynamic_slice_in_dim(out_weight, source * cols + lo, width, axis=1)

    def mm(a, b):
        return lax.dot_general(
            a, b, (((1,), (1,)), ((), ())), preferred_element_type=jnp.float32
        )

    if head_size != 4:
        full = lax.all_gather(og, "head", axis=1, tiled=True)
        full, tied = lax.optimization_barrier((full, tied))
        return mm(full, out_weight), tied
    me = lax.axis_index("head")
    core = lax.axis_index("ctx") % 2
    devices = [(p, j) for p in range(ctx_size) for j in range(4)]

    def route(core_0_bit, core_1_bit):
        return [(p * 4 + j, p * 4 + (j ^ (core_0_bit if p % 2 == 0 else core_1_bit))) for p, j in devices]

    to_relay = lax.ppermute(og, ("ctx", "head"), route(1, 2))
    kept = lax.ppermute(og, ("ctx", "head"), route(2, 1))
    diag = lax.ppermute(to_relay, ("ctx", "head"), route(2, 1))
    diag, tied = lax.optimization_barrier((diag, tied))
    acc = mm(og, weight_cols(me, 0, cols))
    acc = acc + mm(to_relay, weight_cols(me ^ (1 + core), 0, cols))
    acc = acc + mm(kept, weight_cols(me ^ (2 - core), 0, cols))
    acc = acc + mm(diag, weight_cols(me ^ 3, 0, cols))
    return acc, tied


def ctx_exclusive(state, ctx_size, reverse, cover=None):
    core = lax.axis_index("ctx") % 2
    chips = ctx_size // 2
    rounded = state.astype(jnp.bfloat16)
    partner = lax.ppermute(rounded, "ctx", flip_pairs(ctx_size, 1)).astype(jnp.float32)
    chip_sum = rounded.astype(jnp.float32) + partner
    half = state.shape[1] // 2
    mine = lax.dynamic_slice_in_dim(chip_sum, core * half, half, axis=1)

    def pairs(step):
        if reverse:
            return [(2 * (z + step) + c, 2 * z + c) for z in range(chips - step) for c in range(2)]
        return [(2 * z + c, 2 * (z + step) + c) for z in range(chips - step) for c in range(2)]

    others = jnp.zeros_like(mine)
    if cover is None and chips <= 4:
        sent = mine.astype(jnp.bfloat16)
        for step in range(1, chips):
            others = others + lax.ppermute(sent, "ctx", pairs(step)).astype(jnp.float32)
        covered = None
    else:
        run = mine
        step = 1
        held = cover.args if cover is not None else None
        while step < chips:
            last = 2 * step >= chips
            if last and cover is not None:
                run, others, held = lax.optimization_barrier((run, others, held))
            got = lax.ppermute(run.astype(jnp.bfloat16), "ctx", pairs(step)).astype(jnp.float32)
            if last and cover is not None:
                covered = cover.fn(*held)
            run = run + got
            others = others + got
            step *= 2
        covered = None if cover is None else covered
        if cover is not None:
            others, covered = lax.optimization_barrier((others, covered))
    theirs = lax.ppermute(others, "ctx", flip_pairs(ctx_size, 1))
    lower = jnp.where(core == 0, others, theirs)
    upper = jnp.where(core == 0, theirs, others)
    chips_side = jnp.concatenate([lower, upper], axis=1)
    same_chip = (core == 0) if reverse else (core == 1)
    return chips_side + jnp.where(same_chip, partner, 0.0), covered


class Cover:
    def __init__(self, fn, args):
        self.fn = fn
        self.args = args


NT = (((1,), (1,)), ((), ()))
TN = (((0,), (0,)), ((), ()))


def split_state(state):
    high = state.astype(jnp.bfloat16)
    low = (state - high.astype(jnp.float32)).astype(jnp.bfloat16)
    return high, low


def scores_kernel(scale, per_step, q_ref, k_ref, v_ref, g_ref, kv_ref, gq_ref, gk_ref, gv_ref):
    length = q_ref.shape[0]
    row = lax.broadcasted_iota(jnp.int32, (length, length), 0)
    col = lax.broadcasted_iota(jnp.int32, (length, length), 1)
    lower = row >= col
    for h in range(per_step):
        cols = pl.ds(h * DH, DH)
        q, k, v, g = q_ref[:, cols], k_ref[:, cols], v_ref[:, cols], g_ref[:, cols]
        kv_high, kv_low = split_state(kv_ref[0, h] * scale)
        score_grad = lax.dot_general(g, v, NT, preferred_element_type=jnp.float32) * scale
        score_grad = jnp.where(lower, score_grad, 0.0).astype(jnp.bfloat16)
        score_fwd = lax.dot_general(q, k, NT, preferred_element_type=jnp.float32) * scale
        score_fwd = jnp.where(lower, score_fwd, 0.0).astype(jnp.bfloat16)
        gq = lax.dot_general(g, kv_high, NT, preferred_element_type=jnp.float32)
        gq = gq + lax.dot_general(g, kv_low, NT, preferred_element_type=jnp.float32)
        gq = gq + jnp.dot(score_grad, k, preferred_element_type=jnp.float32)
        gq_ref[:, cols] = gq.astype(gq_ref.dtype)
        gk_t = lax.dot_general(q, score_grad, TN, preferred_element_type=jnp.float32)
        gv_t = lax.dot_general(g, score_fwd, TN, preferred_element_type=jnp.float32)
        gk_ref[:, cols] = gk_t.T.astype(gk_ref.dtype)
        gv_ref[:, cols] = gv_t.T.astype(gv_ref.dtype)


def state_kernel(scale, per_step, k_ref, v_ref, qg_ref, gkp_ref, gvp_ref, gk_ref, gv_ref):
    for i in range(per_step):
        cols = pl.ds(i * DH, DH)
        k, v = k_ref[:, cols], v_ref[:, cols]
        qg_high, qg_low = split_state(qg_ref[0, i] * scale)
        gk = gkp_ref[:, cols].astype(jnp.float32)
        gk = gk + lax.dot_general(v, qg_high, NT, preferred_element_type=jnp.float32)
        gk = gk + lax.dot_general(v, qg_low, NT, preferred_element_type=jnp.float32)
        gv = gvp_ref[:, cols].astype(jnp.float32)
        gv = gv + jnp.dot(k, qg_high, preferred_element_type=jnp.float32)
        gv = gv + jnp.dot(k, qg_low, preferred_element_type=jnp.float32)
        gk_ref[:, cols] = gk.astype(jnp.bfloat16)
        gv_ref[:, cols] = gv.astype(jnp.bfloat16)


def attention_part(q, k, v, g, kv_state, blocks, block_len, heads, scale):
    per_step = 2 if heads % 2 == 0 else 1
    tok = pl.BlockSpec((block_len, DH * per_step), lambda n, h: (n, h))
    st = pl.BlockSpec((1, per_step, DH, DH), lambda n, h: (n, h, 0, 0))
    rows, width = q.shape
    out = jax.ShapeDtypeStruct((rows, width), jnp.bfloat16)
    return pl.pallas_call(
        lambda *refs: scores_kernel(scale, per_step, *refs),
        grid=(blocks, heads // per_step),
        in_specs=[tok, tok, tok, tok, st],
        out_specs=[tok, tok, tok],
        out_shape=[out, out, out],
        cost_estimate=pl.CostEstimate(
            flops=blocks * heads * 6 * 2 * block_len * block_len * DH,
            transcendentals=0,
            bytes_accessed=rows * width * 14,
        ),
        name="attention_part",
    )(q, k, v, g, kv_state)


def state_part(k, v, qg_state, parts, blocks, block_len, heads, scale):
    per_step = 2 if heads % 2 == 0 else 1
    tok = pl.BlockSpec((block_len, DH * per_step), lambda n, h: (n, h))
    st = pl.BlockSpec((1, per_step, DH, DH), lambda n, h: (n, h, 0, 0))
    rows, width = k.shape
    out = jax.ShapeDtypeStruct((rows, width), jnp.bfloat16)
    return pl.pallas_call(
        lambda *refs: state_kernel(scale, per_step, *refs),
        grid=(blocks, heads // per_step),
        in_specs=[tok, tok, st, tok, tok],
        out_specs=[tok, tok],
        out_shape=[out, out],
        cost_estimate=pl.CostEstimate(
            flops=blocks * heads * 4 * 2 * block_len * DH * DH,
            transcendentals=0,
            bytes_accessed=rows * width * 12,
        ),
        name="state_part",
    )(k, v, qg_state, *parts)


def make_shards(ctx_size, head_size):
    def shards(queries, keys, values, output_grad, out_weight):
        row_count = queries.shape[0]
        width = queries.shape[1]
        heads = width // DH
        block_len = min(row_count, 512)
        blocks = row_count // block_len
        scale_factor = DH ** (-0.5)
        shape = (blocks, block_len, heads, DH)
        q_blocks = queries.reshape(shape)
        k_blocks = keys.reshape(shape)
        v_blocks = values.reshape(shape)
        kv_blocks = jnp.einsum(
            "nshd,nshe->nhde", k_blocks, v_blocks,
            preferred_element_type=jnp.float32,
        )
        kv_running = jnp.cumsum(kv_blocks, axis=0)
        kv_before, _ = ctx_exclusive(kv_running[-1], ctx_size, False)
        if blocks == 1:
            kv_entry = kv_before[None]
        else:
            kv_entry = kv_before[None] + kv_running - kv_blocks
        grad_heads, kv_entry = project(output_grad, out_weight, ctx_size, head_size, kv_entry)
        grad_heads = grad_heads.astype(jnp.bfloat16)
        g_blocks = grad_heads.reshape(shape)
        qg_blocks = jnp.einsum(
            "nthd,nthe->nhde", q_blocks, g_blocks, preferred_element_type=jnp.float32
        )
        qg_running = jnp.flip(jnp.cumsum(jnp.flip(qg_blocks, 0), axis=0), 0)
        qg_after, (gq, gk_part, gv_part) = ctx_exclusive(
            qg_running[0], ctx_size, True,
            Cover(
                lambda g, kv: attention_part(
                    queries, keys, values, g, kv, blocks, block_len, heads, scale_factor
                ),
                (grad_heads, kv_entry),
            ),
        )
        if blocks == 1:
            qg_entry = qg_after[None]
        else:
            qg_entry = qg_after[None] + qg_running - qg_blocks
        gk, gv = state_part(
            keys, values, qg_entry, (gk_part, gv_part), blocks, block_len, heads, scale_factor
        )
        return gq, gk, gv

    return shards


def solution(mesh):
    return jax.shard_map(
        make_shards(mesh.shape["ctx"], mesh.shape["head"]),
        mesh=mesh,
        in_specs=(
            P("ctx", "head"),
            P("ctx", "head"),
            P("ctx", "head"),
            P("ctx", "head"),
            P("head", None),
        ),
        out_specs=(P("ctx", "head"), P("ctx", "head"), P("ctx", "head")),
        check_vma=False,
    )
```

```python
import jax
import jax.numpy as jnp
from jax import lax
from jax.experimental import pallas as pl
from jax.sharding import PartitionSpec as P

DH = 128


def flip_pairs(n, bit):
    return [(a, a ^ bit) for a in range(n)]


def project(og, out_weight, ctx_size, head_size, tied):
    cols = og.shape[1]

    def weight_cols(source, lo, width):
        return lax.dynamic_slice_in_dim(out_weight, source * cols + lo, width, axis=1)

    def mm(a, b):
        return lax.dot_general(
            a, b, (((1,), (1,)), ((), ())), preferred_element_type=jnp.float32
        )

    if head_size != 4:
        full = lax.all_gather(og, "head", axis=1, tiled=True)
        full, tied = lax.optimization_barrier((full, tied))
        return mm(full, out_weight), tied
    me = lax.axis_index("head")
    core = lax.axis_index("ctx") % 2
    devices = [(p, j) for p in range(ctx_size) for j in range(4)]

    def route(core_0_bit, core_1_bit):
        return [(p * 4 + j, p * 4 + (j ^ (core_0_bit if p % 2 == 0 else core_1_bit))) for p, j in devices]

    to_relay = lax.ppermute(og, ("ctx", "head"), route(1, 2))
    kept = lax.ppermute(og, ("ctx", "head"), route(2, 1))
    diag = lax.ppermute(to_relay, ("ctx", "head"), route(2, 1))
    diag, tied = lax.optimization_barrier((diag, tied))
    acc = mm(og, weight_cols(me, 0, cols))
    acc = acc + mm(to_relay, weight_cols(me ^ (1 + core), 0, cols))
    acc = acc + mm(kept, weight_cols(me ^ (2 - core), 0, cols))
    acc = acc + mm(diag, weight_cols(me ^ 3, 0, cols))
    return acc, tied


def ctx_exclusive(state, ctx_size, reverse, cover=None):
    core = lax.axis_index("ctx") % 2
    chips = ctx_size // 2
    rounded = state.astype(jnp.bfloat16)
    partner = lax.ppermute(rounded, "ctx", flip_pairs(ctx_size, 1)).astype(jnp.float32)
    chip_sum = rounded.astype(jnp.float32) + partner
    half = state.shape[1] // 2
    mine = lax.dynamic_slice_in_dim(chip_sum, core * half, half, axis=1)

    def pairs(step):
        if reverse:
            return [(2 * (z + step) + c, 2 * z + c) for z in range(chips - step) for c in range(2)]
        return [(2 * z + c, 2 * (z + step) + c) for z in range(chips - step) for c in range(2)]

    if cover is not None:
        mine, held = lax.optimization_barrier((mine, cover.args))
    others = jnp.zeros_like(mine)
    if chips <= 4:
        sent = mine.astype(jnp.bfloat16)
        for step in range(1, chips):
            others = others + lax.ppermute(sent, "ctx", pairs(step)).astype(jnp.float32)
    else:
        run = mine
        step = 1
        while step < chips:
            got = lax.ppermute(run.astype(jnp.bfloat16), "ctx", pairs(step)).astype(jnp.float32)
            run = run + got
            others = others + got
            step *= 2
    covered = None
    if cover is not None:
        covered = cover.fn(*held)
        others, covered = lax.optimization_barrier((others, covered))
    theirs = lax.ppermute(others, "ctx", flip_pairs(ctx_size, 1))
    lower = jnp.where(core == 0, others, theirs)
    upper = jnp.where(core == 0, theirs, others)
    chips_side = jnp.concatenate([lower, upper], axis=1)
    same_chip = (core == 0) if reverse else (core == 1)
    return chips_side + jnp.where(same_chip, partner, 0.0), covered


class Cover:
    def __init__(self, fn, args):
        self.fn = fn
        self.args = args


NT = (((1,), (1,)), ((), ()))
TN = (((0,), (0,)), ((), ()))


def split_state(state):
    high = state.astype(jnp.bfloat16)
    low = (state - high.astype(jnp.float32)).astype(jnp.bfloat16)
    return high, low


def scores_kernel(scale, per_step, q_ref, k_ref, v_ref, g_ref, kv_ref, gq_ref, gk_ref, gv_ref):
    length = q_ref.shape[0]
    row = lax.broadcasted_iota(jnp.int32, (length, length), 0)
    col = lax.broadcasted_iota(jnp.int32, (length, length), 1)
    lower = row >= col
    for h in range(per_step):
        cols = pl.ds(h * DH, DH)
        q, k, v, g = q_ref[:, cols], k_ref[:, cols], v_ref[:, cols], g_ref[:, cols]
        kv_high, kv_low = split_state(kv_ref[0, h] * scale)
        score_grad = lax.dot_general(g, v, NT, preferred_element_type=jnp.float32) * scale
        score_grad = jnp.where(lower, score_grad, 0.0).astype(jnp.bfloat16)
        score_fwd = lax.dot_general(q, k, NT, preferred_element_type=jnp.float32) * scale
        score_fwd = jnp.where(lower, score_fwd, 0.0).astype(jnp.bfloat16)
        gq = lax.dot_general(g, kv_high, NT, preferred_element_type=jnp.float32)
        gq = gq + lax.dot_general(g, kv_low, NT, preferred_element_type=jnp.float32)
        gq = gq + jnp.dot(score_grad, k, preferred_element_type=jnp.float32)
        gq_ref[:, cols] = gq.astype(gq_ref.dtype)
        gk_t = lax.dot_general(q, score_grad, TN, preferred_element_type=jnp.float32)
        gv_t = lax.dot_general(g, score_fwd, TN, preferred_element_type=jnp.float32)
        gk_ref[:, cols] = gk_t.T.astype(gk_ref.dtype)
        gv_ref[:, cols] = gv_t.T.astype(gv_ref.dtype)


def state_kernel(scale, per_step, k_ref, v_ref, qg_ref, gkp_ref, gvp_ref, gk_ref, gv_ref):
    for i in range(per_step):
        cols = pl.ds(i * DH, DH)
        k, v = k_ref[:, cols], v_ref[:, cols]
        qg_high, qg_low = split_state(qg_ref[0, i] * scale)
        gk = gkp_ref[:, cols].astype(jnp.float32)
        gk = gk + lax.dot_general(v, qg_high, NT, preferred_element_type=jnp.float32)
        gk = gk + lax.dot_general(v, qg_low, NT, preferred_element_type=jnp.float32)
        gv = gvp_ref[:, cols].astype(jnp.float32)
        gv = gv + jnp.dot(k, qg_high, preferred_element_type=jnp.float32)
        gv = gv + jnp.dot(k, qg_low, preferred_element_type=jnp.float32)
        gk_ref[:, cols] = gk.astype(jnp.bfloat16)
        gv_ref[:, cols] = gv.astype(jnp.bfloat16)


def attention_part(q, k, v, g, kv_state, blocks, block_len, heads, scale):
    per_step = 2 if heads % 2 == 0 else 1
    tok = pl.BlockSpec((block_len, DH * per_step), lambda n, h: (n, h))
    st = pl.BlockSpec((1, per_step, DH, DH), lambda n, h: (n, h, 0, 0))
    rows, width = q.shape
    out = jax.ShapeDtypeStruct((rows, width), jnp.bfloat16)
    return pl.pallas_call(
        lambda *refs: scores_kernel(scale, per_step, *refs),
        grid=(blocks, heads // per_step),
        in_specs=[tok, tok, tok, tok, st],
        out_specs=[tok, tok, tok],
        out_shape=[out, out, out],
        cost_estimate=pl.CostEstimate(
            flops=blocks * heads * 6 * 2 * block_len * block_len * DH,
            transcendentals=0,
            bytes_accessed=rows * width * 14,
        ),
        name="attention_part",
    )(q, k, v, g, kv_state)


def state_part(k, v, qg_state, parts, blocks, block_len, heads, scale):
    per_step = 4 if heads % 4 == 0 else (2 if heads % 2 == 0 else 1)
    tok = pl.BlockSpec((block_len, DH * per_step), lambda n, h: (n, h))
    st = pl.BlockSpec((1, per_step, DH, DH), lambda n, h: (n, h, 0, 0))
    rows, width = k.shape
    out = jax.ShapeDtypeStruct((rows, width), jnp.bfloat16)
    return pl.pallas_call(
        lambda *refs: state_kernel(scale, per_step, *refs),
        grid=(blocks, heads // per_step),
        in_specs=[tok, tok, st, tok, tok],
        out_specs=[tok, tok],
        out_shape=[out, out],
        cost_estimate=pl.CostEstimate(
            flops=blocks * heads * 4 * 2 * block_len * DH * DH,
            transcendentals=0,
            bytes_accessed=rows * width * 12,
        ),
        name="state_part",
    )(k, v, qg_state, *parts)


def make_shards(ctx_size, head_size):
    def shards(queries, keys, values, output_grad, out_weight):
        row_count = queries.shape[0]
        width = queries.shape[1]
        heads = width // DH
        block_len = min(row_count, 512)
        blocks = row_count // block_len
        scale_factor = DH ** (-0.5)
        shape = (blocks, block_len, heads, DH)
        q_blocks = queries.reshape(shape)
        k_blocks = keys.reshape(shape)
        v_blocks = values.reshape(shape)
        kv_blocks = jnp.einsum(
            "nshd,nshe->nhde", k_blocks, v_blocks,
            preferred_element_type=jnp.float32,
        )
        kv_running = jnp.cumsum(kv_blocks, axis=0)
        kv_before, _ = ctx_exclusive(kv_running[-1], ctx_size, False)
        if blocks == 1:
            kv_entry = kv_before[None]
        else:
            kv_entry = kv_before[None] + kv_running - kv_blocks
        grad_heads, kv_entry = project(output_grad, out_weight, ctx_size, head_size, kv_entry)
        grad_heads = grad_heads.astype(jnp.bfloat16)
        g_blocks = grad_heads.reshape(shape)
        qg_blocks = jnp.einsum(
            "nthd,nthe->nhde", q_blocks, g_blocks, preferred_element_type=jnp.float32
        )
        qg_running = jnp.flip(jnp.cumsum(jnp.flip(qg_blocks, 0), axis=0), 0)
        qg_after, (gq, gk_part, gv_part) = ctx_exclusive(
            qg_running[0], ctx_size, True,
            Cover(
                lambda g, kv: attention_part(
                    queries, keys, values, g, kv, blocks, block_len, heads, scale_factor
                ),
                (grad_heads, kv_entry),
            ),
        )
        if blocks == 1:
            qg_entry = qg_after[None]
        else:
            qg_entry = qg_after[None] + qg_running - qg_blocks
        gk, gv = state_part(
            keys, values, qg_entry, (gk_part, gv_part), blocks, block_len, heads, scale_factor
        )
        return gq, gk, gv

    return shards


def solution(mesh):
    return jax.shard_map(
        make_shards(mesh.shape["ctx"], mesh.shape["head"]),
        mesh=mesh,
        in_specs=(
            P("ctx", "head"),
            P("ctx", "head"),
            P("ctx", "head"),
            P("ctx", "head"),
            P("head", None),
        ),
        out_specs=(P("ctx", "head"), P("ctx", "head"), P("ctx", "head")),
        check_vma=False,
    )
```

```python
import jax
import jax.numpy as jnp
from jax import lax
from jax.experimental import pallas as pl
from jax.sharding import PartitionSpec as P

DH = 128


def flip_pairs(n, bit):
    return [(a, a ^ bit) for a in range(n)]


def project(og, out_weight, ctx_size, head_size, tied):
    cols = og.shape[1]

    def weight_cols(source, lo, width):
        return lax.dynamic_slice_in_dim(out_weight, source * cols + lo, width, axis=1)

    def mm(a, b):
        return lax.dot_general(
            a, b, (((1,), (1,)), ((), ())), preferred_element_type=jnp.float32
        )

    if head_size != 4:
        full = lax.all_gather(og, "head", axis=1, tiled=True)
        full, tied = lax.optimization_barrier((full, tied))
        return mm(full, out_weight), tied
    me = lax.axis_index("head")
    core = lax.axis_index("ctx") % 2
    devices = [(p, j) for p in range(ctx_size) for j in range(4)]

    def route(core_0_bit, core_1_bit):
        return [(p * 4 + j, p * 4 + (j ^ (core_0_bit if p % 2 == 0 else core_1_bit))) for p, j in devices]

    to_relay = lax.ppermute(og, ("ctx", "head"), route(1, 2))
    kept = lax.ppermute(og, ("ctx", "head"), route(2, 1))
    diag = lax.ppermute(to_relay, ("ctx", "head"), route(2, 1))
    diag, tied = lax.optimization_barrier((diag, tied))
    acc = mm(og, weight_cols(me, 0, cols))
    acc = acc + mm(to_relay, weight_cols(me ^ (1 + core), 0, cols))
    acc = acc + mm(kept, weight_cols(me ^ (2 - core), 0, cols))
    acc = acc + mm(diag, weight_cols(me ^ 3, 0, cols))
    return acc, tied


def ctx_exclusive(state, ctx_size, reverse, cover=None, direct=True):
    core = lax.axis_index("ctx") % 2
    chips = ctx_size // 2
    rounded = state.astype(jnp.bfloat16)
    partner = lax.ppermute(rounded, "ctx", flip_pairs(ctx_size, 1)).astype(jnp.float32)
    chip_sum = rounded.astype(jnp.float32) + partner
    half = state.shape[1] // 2
    mine = lax.dynamic_slice_in_dim(chip_sum, core * half, half, axis=1)

    def pairs(step):
        if reverse:
            return [(2 * (z + step) + c, 2 * z + c) for z in range(chips - step) for c in range(2)]
        return [(2 * z + c, 2 * (z + step) + c) for z in range(chips - step) for c in range(2)]

    if cover is not None:
        mine, held = lax.optimization_barrier((mine, cover.args))
    others = jnp.zeros_like(mine)
    if chips <= 4 and direct:
        sent = mine.astype(jnp.bfloat16)
        for step in range(1, chips):
            others = others + lax.ppermute(sent, "ctx", pairs(step)).astype(jnp.float32)
    else:
        run = mine
        step = 1
        while step < chips:
            got = lax.ppermute(run.astype(jnp.bfloat16), "ctx", pairs(step)).astype(jnp.float32)
            run = run + got
            others = others + got
            step *= 2
    covered = None
    if cover is not None:
        covered = cover.fn(*held)
        others, covered = lax.optimization_barrier((others, covered))
    theirs = lax.ppermute(others, "ctx", flip_pairs(ctx_size, 1))
    lower = jnp.where(core == 0, others, theirs)
    upper = jnp.where(core == 0, theirs, others)
    chips_side = jnp.concatenate([lower, upper], axis=1)
    same_chip = (core == 0) if reverse else (core == 1)
    return chips_side + jnp.where(same_chip, partner, 0.0), covered


class Cover:
    def __init__(self, fn, args):
        self.fn = fn
        self.args = args


NT = (((1,), (1,)), ((), ()))
TN = (((0,), (0,)), ((), ()))


def split_state(state):
    high = state.astype(jnp.bfloat16)
    low = (state - high.astype(jnp.float32)).astype(jnp.bfloat16)
    return high, low


def scores_kernel(scale, per_step, q_ref, k_ref, v_ref, g_ref, kv_ref, gq_ref, gk_ref, gv_ref):
    length = q_ref.shape[0]
    row = lax.broadcasted_iota(jnp.int32, (length, length), 0)
    col = lax.broadcasted_iota(jnp.int32, (length, length), 1)
    lower = row >= col
    for h in range(per_step):
        cols = pl.ds(h * DH, DH)
        q, k, v, g = q_ref[:, cols], k_ref[:, cols], v_ref[:, cols], g_ref[:, cols]
        kv_high, kv_low = split_state(kv_ref[0, h] * scale)
        score_grad = lax.dot_general(g, v, NT, preferred_element_type=jnp.float32) * scale
        score_grad = jnp.where(lower, score_grad, 0.0).astype(jnp.bfloat16)
        score_fwd = lax.dot_general(q, k, NT, preferred_element_type=jnp.float32) * scale
        score_fwd = jnp.where(lower, score_fwd, 0.0).astype(jnp.bfloat16)
        gq = lax.dot_general(g, kv_high, NT, preferred_element_type=jnp.float32)
        gq = gq + lax.dot_general(g, kv_low, NT, preferred_element_type=jnp.float32)
        gq = gq + jnp.dot(score_grad, k, preferred_element_type=jnp.float32)
        gq_ref[:, cols] = gq.astype(gq_ref.dtype)
        gk_t = lax.dot_general(q, score_grad, TN, preferred_element_type=jnp.float32)
        gv_t = lax.dot_general(g, score_fwd, TN, preferred_element_type=jnp.float32)
        gk_ref[:, cols] = gk_t.T.astype(gk_ref.dtype)
        gv_ref[:, cols] = gv_t.T.astype(gv_ref.dtype)


def state_kernel(scale, per_step, k_ref, v_ref, qg_ref, gkp_ref, gvp_ref, gk_ref, gv_ref):
    for i in range(per_step):
        cols = pl.ds(i * DH, DH)
        k, v = k_ref[:, cols], v_ref[:, cols]
        qg_high, qg_low = split_state(qg_ref[0, i] * scale)
        gk = gkp_ref[:, cols].astype(jnp.float32)
        gk = gk + lax.dot_general(v, qg_high, NT, preferred_element_type=jnp.float32)
        gk = gk + lax.dot_general(v, qg_low, NT, preferred_element_type=jnp.float32)
        gv = gvp_ref[:, cols].astype(jnp.float32)
        gv = gv + jnp.dot(k, qg_high, preferred_element_type=jnp.float32)
        gv = gv + jnp.dot(k, qg_low, preferred_element_type=jnp.float32)
        gk_ref[:, cols] = gk.astype(jnp.bfloat16)
        gv_ref[:, cols] = gv.astype(jnp.bfloat16)


def attention_part(q, k, v, g, kv_state, blocks, block_len, heads, scale):
    per_step = 2 if heads % 2 == 0 else 1
    tok = pl.BlockSpec((block_len, DH * per_step), lambda n, h: (n, h))
    st = pl.BlockSpec((1, per_step, DH, DH), lambda n, h: (n, h, 0, 0))
    rows, width = q.shape
    out = jax.ShapeDtypeStruct((rows, width), jnp.bfloat16)
    return pl.pallas_call(
        lambda *refs: scores_kernel(scale, per_step, *refs),
        grid=(blocks, heads // per_step),
        in_specs=[tok, tok, tok, tok, st],
        out_specs=[tok, tok, tok],
        out_shape=[out, out, out],
        cost_estimate=pl.CostEstimate(
            flops=blocks * heads * 6 * 2 * block_len * block_len * DH,
            transcendentals=0,
            bytes_accessed=rows * width * 14,
        ),
        name="attention_part",
    )(q, k, v, g, kv_state)


def state_part(k, v, qg_state, parts, blocks, block_len, heads, scale):
    per_step = 4 if heads % 4 == 0 else (2 if heads % 2 == 0 else 1)
    tok = pl.BlockSpec((block_len, DH * per_step), lambda n, h: (n, h))
    st = pl.BlockSpec((1, per_step, DH, DH), lambda n, h: (n, h, 0, 0))
    rows, width = k.shape
    out = jax.ShapeDtypeStruct((rows, width), jnp.bfloat16)
    return pl.pallas_call(
        lambda *refs: state_kernel(scale, per_step, *refs),
        grid=(blocks, heads // per_step),
        in_specs=[tok, tok, st, tok, tok],
        out_specs=[tok, tok],
        out_shape=[out, out],
        cost_estimate=pl.CostEstimate(
            flops=blocks * heads * 4 * 2 * block_len * DH * DH,
            transcendentals=0,
            bytes_accessed=rows * width * 12,
        ),
        name="state_part",
    )(k, v, qg_state, *parts)


def make_shards(ctx_size, head_size):
    def shards(queries, keys, values, output_grad, out_weight):
        row_count = queries.shape[0]
        width = queries.shape[1]
        heads = width // DH
        block_len = min(row_count, 512)
        blocks = row_count // block_len
        scale_factor = DH ** (-0.5)
        shape = (blocks, block_len, heads, DH)
        q_blocks = queries.reshape(shape)
        k_blocks = keys.reshape(shape)
        v_blocks = values.reshape(shape)
        kv_blocks = jnp.einsum(
            "nshd,nshe->nhde", k_blocks, v_blocks,
            preferred_element_type=jnp.float32,
        )
        kv_running = jnp.cumsum(kv_blocks, axis=0)
        kv_before, _ = ctx_exclusive(kv_running[-1], ctx_size, False, direct=False)
        if blocks == 1:
            kv_entry = kv_before[None]
        else:
            kv_entry = kv_before[None] + kv_running - kv_blocks
        grad_heads, kv_entry = project(output_grad, out_weight, ctx_size, head_size, kv_entry)
        grad_heads = grad_heads.astype(jnp.bfloat16)
        g_blocks = grad_heads.reshape(shape)
        qg_blocks = jnp.einsum(
            "nthd,nthe->nhde", q_blocks, g_blocks, preferred_element_type=jnp.float32
        )
        qg_running = jnp.flip(jnp.cumsum(jnp.flip(qg_blocks, 0), axis=0), 0)
        qg_after, (gq, gk_part, gv_part) = ctx_exclusive(
            qg_running[0], ctx_size, True,
            Cover(
                lambda g, kv: attention_part(
                    queries, keys, values, g, kv, blocks, block_len, heads, scale_factor
                ),
                (grad_heads, kv_entry),
            ),
        )
        if blocks == 1:
            qg_entry = qg_after[None]
        else:
            qg_entry = qg_after[None] + qg_running - qg_blocks
        gk, gv = state_part(
            keys, values, qg_entry, (gk_part, gv_part), blocks, block_len, heads, scale_factor
        )
        return gq, gk, gv

    return shards


def solution(mesh):
    return jax.shard_map(
        make_shards(mesh.shape["ctx"], mesh.shape["head"]),
        mesh=mesh,
        in_specs=(
            P("ctx", "head"),
            P("ctx", "head"),
            P("ctx", "head"),
            P("ctx", "head"),
            P("head", None),
        ),
        out_specs=(P("ctx", "head"), P("ctx", "head"), P("ctx", "head")),
        check_vma=False,
    )
```

```python
import jax
import jax.numpy as jnp
from jax import lax
from jax.experimental import pallas as pl
from jax.experimental.pallas import tpu as pltpu
from jax.sharding import PartitionSpec as P

DH = 128


def flip_pairs(n, bit):
    return [(a, a ^ bit) for a in range(n)]


def project(og, out_weight, ctx_size, head_size, tied):
    cols = og.shape[1]

    def weight_cols(source, lo, width):
        return lax.dynamic_slice_in_dim(out_weight, source * cols + lo, width, axis=1)

    def mm(a, b):
        return lax.dot_general(
            a, b, (((1,), (1,)), ((), ())), preferred_element_type=jnp.float32
        )

    if head_size != 4:
        full = lax.all_gather(og, "head", axis=1, tiled=True)
        full, tied = lax.optimization_barrier((full, tied))
        return mm(full, out_weight), tied
    me = lax.axis_index("head")
    core = lax.axis_index("ctx") % 2
    devices = [(p, j) for p in range(ctx_size) for j in range(4)]

    def route(core_0_bit, core_1_bit):
        return [(p * 4 + j, p * 4 + (j ^ (core_0_bit if p % 2 == 0 else core_1_bit))) for p, j in devices]

    to_relay = lax.ppermute(og, ("ctx", "head"), route(1, 2))
    kept = lax.ppermute(og, ("ctx", "head"), route(2, 1))
    diag = lax.ppermute(to_relay, ("ctx", "head"), route(2, 1))
    diag, tied = lax.optimization_barrier((diag, tied))
    acc = mm(og, weight_cols(me, 0, cols))
    acc = acc + mm(to_relay, weight_cols(me ^ (1 + core), 0, cols))
    acc = acc + mm(kept, weight_cols(me ^ (2 - core), 0, cols))
    acc = acc + mm(diag, weight_cols(me ^ 3, 0, cols))
    return acc, tied


def ctx_exclusive(state, ctx_size, reverse, cover=None, by_heads=False):
    core = lax.axis_index("ctx") % 2
    chips = ctx_size // 2
    rounded = state.astype(jnp.bfloat16)
    partner = lax.ppermute(rounded, "ctx", flip_pairs(ctx_size, 1)).astype(jnp.float32)
    chip_sum = rounded.astype(jnp.float32) + partner
    axis = 0 if by_heads else 1
    half = state.shape[axis] // 2
    mine = lax.dynamic_slice_in_dim(chip_sum, core * half, half, axis=axis)

    def pairs(step):
        if reverse:
            return [(2 * (z + step) + c, 2 * z + c) for z in range(chips - step) for c in range(2)]
        return [(2 * z + c, 2 * (z + step) + c) for z in range(chips - step) for c in range(2)]

    if cover is not None:
        mine, held = lax.optimization_barrier((mine, cover.args))
    others = jnp.zeros_like(mine)
    if chips <= 4:
        sent = mine.astype(jnp.bfloat16)
        for step in range(1, chips):
            others = others + lax.ppermute(sent, "ctx", pairs(step)).astype(jnp.float32)
    else:
        run = mine
        step = 1
        while step < chips:
            got = lax.ppermute(run.astype(jnp.bfloat16), "ctx", pairs(step)).astype(jnp.float32)
            run = run + got
            others = others + got
            step *= 2
    covered = None
    if cover is not None:
        covered = cover.fn(*held)
        others, covered = lax.optimization_barrier((others, covered))
    theirs = lax.ppermute(others, "ctx", flip_pairs(ctx_size, 1))
    if by_heads:
        same_chip = (core == 0) if reverse else (core == 1)
        partner_kept = jnp.where(same_chip, partner, 0.0)
        own = others + lax.dynamic_slice_in_dim(partner_kept, core * half, half, axis=0)
        other_partner = lax.dynamic_slice_in_dim(partner_kept, (1 - core) * half, half, axis=0)
        return (own, theirs, other_partner), covered
    lower = jnp.where(core == 0, others, theirs)
    upper = jnp.where(core == 0, theirs, others)
    chips_side = jnp.concatenate([lower, upper], axis=1)
    same_chip = (core == 0) if reverse else (core == 1)
    return chips_side + jnp.where(same_chip, partner, 0.0), covered


class Cover:
    def __init__(self, fn, args):
        self.fn = fn
        self.args = args


NT = (((1,), (1,)), ((), ()))
TN = (((0,), (0,)), ((), ()))


def split_state(state):
    high = state.astype(jnp.bfloat16)
    low = (state - high.astype(jnp.float32)).astype(jnp.bfloat16)
    return high, low


def scores_kernel(scale, per_step, q_ref, k_ref, v_ref, g_ref, kv_ref, gq_ref, gk_ref, gv_ref):
    length = q_ref.shape[0]
    row = lax.broadcasted_iota(jnp.int32, (length, length), 0)
    col = lax.broadcasted_iota(jnp.int32, (length, length), 1)
    lower = row >= col
    for h in range(per_step):
        cols = pl.ds(h * DH, DH)
        q, k, v, g = q_ref[:, cols], k_ref[:, cols], v_ref[:, cols], g_ref[:, cols]
        kv_high, kv_low = split_state(kv_ref[0, h] * scale)
        score_grad = lax.dot_general(g, v, NT, preferred_element_type=jnp.float32) * scale
        score_grad = jnp.where(lower, score_grad, 0.0).astype(jnp.bfloat16)
        score_fwd = lax.dot_general(q, k, NT, preferred_element_type=jnp.float32) * scale
        score_fwd = jnp.where(lower, score_fwd, 0.0).astype(jnp.bfloat16)
        gq = lax.dot_general(g, kv_high, NT, preferred_element_type=jnp.float32)
        gq = gq + lax.dot_general(g, kv_low, NT, preferred_element_type=jnp.float32)
        gq = gq + jnp.dot(score_grad, k, preferred_element_type=jnp.float32)
        gq_ref[:, cols] = gq.astype(gq_ref.dtype)
        gk_t = lax.dot_general(q, score_grad, TN, preferred_element_type=jnp.float32)
        gv_t = lax.dot_general(g, score_fwd, TN, preferred_element_type=jnp.float32)
        gk_ref[:, cols] = gk_t.T.astype(gk_ref.dtype)
        gv_ref[:, cols] = gv_t.T.astype(gv_ref.dtype)


def state_kernel(scale, per_step, k_ref, v_ref, qg_ref, gkp_ref, gvp_ref, gk_ref, gv_ref):
    for i in range(per_step):
        cols = pl.ds(i * DH, DH)
        k, v = k_ref[:, cols], v_ref[:, cols]
        qg_high, qg_low = split_state(qg_ref[0, i] * scale)
        gk = gkp_ref[:, cols].astype(jnp.float32)
        gk = gk + lax.dot_general(v, qg_high, NT, preferred_element_type=jnp.float32)
        gk = gk + lax.dot_general(v, qg_low, NT, preferred_element_type=jnp.float32)
        gv = gvp_ref[:, cols].astype(jnp.float32)
        gv = gv + jnp.dot(k, qg_high, preferred_element_type=jnp.float32)
        gv = gv + jnp.dot(k, qg_low, preferred_element_type=jnp.float32)
        gk_ref[:, cols] = gk.astype(jnp.bfloat16)
        gv_ref[:, cols] = gv.astype(jnp.bfloat16)


def attention_part(q, k, v, g, kv_state, blocks, block_len, heads, scale):
    per_step = 2 if heads % 2 == 0 else 1
    tok = pl.BlockSpec((block_len, DH * per_step), lambda n, h: (n, h))
    st = pl.BlockSpec((1, per_step, DH, DH), lambda n, h: (n, h, 0, 0))
    rows, width = q.shape
    out = jax.ShapeDtypeStruct((rows, width), jnp.bfloat16)
    return pl.pallas_call(
        lambda *refs: scores_kernel(scale, per_step, *refs),
        grid=(blocks, heads // per_step),
        in_specs=[tok, tok, tok, tok, st],
        out_specs=[tok, tok, tok],
        out_shape=[out, out, out],
        cost_estimate=pl.CostEstimate(
            flops=blocks * heads * 6 * 2 * block_len * block_len * DH,
            transcendentals=0,
            bytes_accessed=rows * width * 14,
        ),
        name="attention_part",
    )(q, k, v, g, kv_state)


def state_part(k, v, qg_state, parts, blocks, block_len, heads, scale, first=None, into=None):
    count = qg_state.shape[1]
    per_step = 4 if count % 4 == 0 else (2 if count % 2 == 0 else 1)
    rows, width = k.shape
    if first is None:
        first = jnp.zeros((), jnp.int32)
    offset = jnp.reshape(first // per_step, (1,)).astype(jnp.int32)
    tok = pl.BlockSpec((block_len, DH * per_step), lambda n, h, o: (n, h + o[0]))
    st = pl.BlockSpec((1, per_step, DH, DH), lambda n, h, o: (n, h, 0, 0))
    out = jax.ShapeDtypeStruct((rows, width), jnp.bfloat16)
    operands = [offset, k, v, qg_state, *parts]
    in_specs = [tok, tok, st, tok, tok]
    aliases = {}
    kernel = lambda o, *refs: state_kernel(scale, per_step, *refs)
    if into is not None:
        operands += list(into)
        in_specs += [pl.BlockSpec(memory_space=pl.ANY)] * 2
        aliases = {6: 0, 7: 1}
        kernel = lambda o, *refs: state_kernel(scale, per_step, *refs[:5], *refs[7:])
    return pl.pallas_call(
        kernel,
        grid_spec=pltpu.PrefetchScalarGridSpec(
            num_scalar_prefetch=1,
            grid=(blocks, count // per_step),
            in_specs=in_specs,
            out_specs=[tok, tok],
        ),
        out_shape=[out, out],
        input_output_aliases=aliases,
        cost_estimate=pl.CostEstimate(
            flops=blocks * count * 4 * 2 * block_len * DH * DH,
            transcendentals=0,
            bytes_accessed=rows * DH * count * 12,
        ),
        name="state_part",
    )(*operands)


def make_shards(ctx_size, head_size):
    def shards(queries, keys, values, output_grad, out_weight):
        row_count = queries.shape[0]
        width = queries.shape[1]
        heads = width // DH
        block_len = min(row_count, 512)
        blocks = row_count // block_len
        scale_factor = DH ** (-0.5)
        shape = (blocks, block_len, heads, DH)
        q_blocks = queries.reshape(shape)
        k_blocks = keys.reshape(shape)
        v_blocks = values.reshape(shape)
        kv_blocks = jnp.einsum(
            "nshd,nshe->nhde", k_blocks, v_blocks,
            preferred_element_type=jnp.float32,
        )
        kv_running = jnp.cumsum(kv_blocks, axis=0)
        kv_before, _ = ctx_exclusive(kv_running[-1], ctx_size, False)
        if blocks == 1:
            kv_entry = kv_before[None]
        else:
            kv_entry = kv_before[None] + kv_running - kv_blocks
        grad_heads, kv_entry = project(output_grad, out_weight, ctx_size, head_size, kv_entry)
        grad_heads = grad_heads.astype(jnp.bfloat16)
        g_blocks = grad_heads.reshape(shape)
        qg_blocks = jnp.einsum(
            "nthd,nthe->nhde", q_blocks, g_blocks, preferred_element_type=jnp.float32
        )
        qg_running = jnp.flip(jnp.cumsum(jnp.flip(qg_blocks, 0), axis=0), 0)
        split = blocks == 1 and heads % 2 == 0
        qg_after, (gq, gk_part, gv_part) = ctx_exclusive(
            qg_running[0], ctx_size, True,
            Cover(
                lambda g, kv: attention_part(
                    queries, keys, values, g, kv, blocks, block_len, heads, scale_factor
                ),
                (grad_heads, kv_entry),
            ),
            by_heads=split,
        )
        if split:
            own, theirs, other_partner = qg_after
            half = heads // 2
            core = lax.axis_index("ctx") % 2
            gk, gv = state_part(
                keys, values, own[None], (gk_part, gv_part), blocks, block_len, heads,
                scale_factor, first=core * half,
            )
            theirs, gk, gv = lax.optimization_barrier((theirs, gk, gv))
            other = theirs + other_partner
            gk, gv = state_part(
                keys, values, other[None], (gk_part, gv_part), blocks, block_len, heads,
                scale_factor, first=(1 - core) * half, into=(gk, gv),
            )
            return gq, gk, gv
        if blocks == 1:
            qg_entry = qg_after[None]
        else:
            qg_entry = qg_after[None] + qg_running - qg_blocks
        gk, gv = state_part(
            keys, values, qg_entry, (gk_part, gv_part), blocks, block_len, heads, scale_factor
        )
        return gq, gk, gv

    return shards


def solution(mesh):
    return jax.shard_map(
        make_shards(mesh.shape["ctx"], mesh.shape["head"]),
        mesh=mesh,
        in_specs=(
            P("ctx", "head"),
            P("ctx", "head"),
            P("ctx", "head"),
            P("ctx", "head"),
            P("head", None),
        ),
        out_specs=(P("ctx", "head"), P("ctx", "head"), P("ctx", "head")),
        check_vma=False,
    )
```

```python
import jax
import jax.numpy as jnp
from jax import lax
from jax.experimental import pallas as pl
from jax.experimental.pallas import tpu as pltpu
from jax.sharding import PartitionSpec as P

DH = 128


def flip_pairs(n, bit):
    return [(a, a ^ bit) for a in range(n)]


def project(og, out_weight, ctx_size, head_size, tied):
    cols = og.shape[1]

    def weight_cols(source, lo, width):
        return lax.dynamic_slice_in_dim(out_weight, source * cols + lo, width, axis=1)

    def mm(a, b):
        return lax.dot_general(
            a, b, (((1,), (1,)), ((), ())), preferred_element_type=jnp.float32
        )

    if head_size != 4:
        full = lax.all_gather(og, "head", axis=1, tiled=True)
        full, tied = lax.optimization_barrier((full, tied))
        return mm(full, out_weight), tied
    me = lax.axis_index("head")
    core = lax.axis_index("ctx") % 2
    devices = [(p, j) for p in range(ctx_size) for j in range(4)]

    def route(core_0_bit, core_1_bit):
        return [(p * 4 + j, p * 4 + (j ^ (core_0_bit if p % 2 == 0 else core_1_bit))) for p, j in devices]

    to_relay = lax.ppermute(og, ("ctx", "head"), route(1, 2))
    kept = lax.ppermute(og, ("ctx", "head"), route(2, 1))
    diag = lax.ppermute(to_relay, ("ctx", "head"), route(2, 1))
    diag, tied = lax.optimization_barrier((diag, tied))
    acc = mm(og, weight_cols(me, 0, cols))
    acc = acc + mm(to_relay, weight_cols(me ^ (1 + core), 0, cols))
    acc = acc + mm(kept, weight_cols(me ^ (2 - core), 0, cols))
    acc = acc + mm(diag, weight_cols(me ^ 3, 0, cols))
    return acc, tied


def ctx_exclusive(state, ctx_size, reverse, cover=None, by_heads=False):
    core = lax.axis_index("ctx") % 2
    chips = ctx_size // 2
    rounded = state.astype(jnp.bfloat16)
    partner = lax.ppermute(rounded, "ctx", flip_pairs(ctx_size, 1)).astype(jnp.float32)
    chip_sum = rounded.astype(jnp.float32) + partner
    axis = 0 if by_heads else 1
    half = state.shape[axis] // 2
    mine = lax.dynamic_slice_in_dim(chip_sum, core * half, half, axis=axis)

    def pairs(step):
        if reverse:
            return [(2 * (z + step) + c, 2 * z + c) for z in range(chips - step) for c in range(2)]
        return [(2 * z + c, 2 * (z + step) + c) for z in range(chips - step) for c in range(2)]

    if cover is not None:
        mine, held = lax.optimization_barrier((mine, cover.args))
    others = jnp.zeros_like(mine)
    if chips <= 4:
        sent = mine.astype(jnp.bfloat16)
        for step in range(1, chips):
            others = others + lax.ppermute(sent, "ctx", pairs(step)).astype(jnp.float32)
    else:
        run = mine
        step = 1
        while step < chips:
            got = lax.ppermute(run.astype(jnp.bfloat16), "ctx", pairs(step)).astype(jnp.float32)
            run = run + got
            others = others + got
            step *= 2
    covered = None
    if cover is not None:
        covered = cover.fn(*held)
        others, covered = lax.optimization_barrier((others, covered))
    theirs = lax.ppermute(others, "ctx", flip_pairs(ctx_size, 1))
    if by_heads:
        same_chip = (core == 0) if reverse else (core == 1)
        partner_kept = jnp.where(same_chip, partner, 0.0)
        own = others + lax.dynamic_slice_in_dim(partner_kept, core * half, half, axis=0)
        other_partner = lax.dynamic_slice_in_dim(partner_kept, (1 - core) * half, half, axis=0)
        return (own, theirs, other_partner), covered
    lower = jnp.where(core == 0, others, theirs)
    upper = jnp.where(core == 0, theirs, others)
    chips_side = jnp.concatenate([lower, upper], axis=1)
    same_chip = (core == 0) if reverse else (core == 1)
    return chips_side + jnp.where(same_chip, partner, 0.0), covered


class Cover:
    def __init__(self, fn, args):
        self.fn = fn
        self.args = args


NT = (((1,), (1,)), ((), ()))
TN = (((0,), (0,)), ((), ()))


def split_state(state):
    high = state.astype(jnp.bfloat16)
    low = (state - high.astype(jnp.float32)).astype(jnp.bfloat16)
    return high, low


def scores_kernel(scale, per_step, q_ref, k_ref, v_ref, g_ref, kv_ref, gq_ref, gk_ref, gv_ref):
    length = q_ref.shape[0]
    row = lax.broadcasted_iota(jnp.int32, (length, length), 0)
    col = lax.broadcasted_iota(jnp.int32, (length, length), 1)
    lower = row >= col
    for h in range(per_step):
        cols = pl.ds(h * DH, DH)
        q, k, v, g = q_ref[:, cols], k_ref[:, cols], v_ref[:, cols], g_ref[:, cols]
        kv_high, kv_low = split_state(kv_ref[0, h] * scale)
        score_grad = lax.dot_general(g, v, NT, preferred_element_type=jnp.float32) * scale
        score_grad = jnp.where(lower, score_grad, 0.0).astype(jnp.bfloat16)
        score_fwd = lax.dot_general(q, k, NT, preferred_element_type=jnp.float32) * scale
        score_fwd = jnp.where(lower, score_fwd, 0.0).astype(jnp.bfloat16)
        gq = lax.dot_general(g, kv_high, NT, preferred_element_type=jnp.float32)
        gq = gq + lax.dot_general(g, kv_low, NT, preferred_element_type=jnp.float32)
        gq = gq + jnp.dot(score_grad, k, preferred_element_type=jnp.float32)
        gq_ref[:, cols] = gq.astype(gq_ref.dtype)
        gk_t = lax.dot_general(q, score_grad, TN, preferred_element_type=jnp.float32)
        gv_t = lax.dot_general(g, score_fwd, TN, preferred_element_type=jnp.float32)
        gk_ref[:, cols] = gk_t.T.astype(gk_ref.dtype)
        gv_ref[:, cols] = gv_t.T.astype(gv_ref.dtype)


def state_kernel(scale, per_step, k_ref, v_ref, qg_ref, gkp_ref, gvp_ref, gk_ref, gv_ref):
    for i in range(per_step):
        cols = pl.ds(i * DH, DH)
        k, v = k_ref[:, cols], v_ref[:, cols]
        qg_high, qg_low = split_state(qg_ref[0, i] * scale)
        gk = gkp_ref[:, cols].astype(jnp.float32)
        gk = gk + lax.dot_general(v, qg_high, NT, preferred_element_type=jnp.float32)
        gk = gk + lax.dot_general(v, qg_low, NT, preferred_element_type=jnp.float32)
        gv = gvp_ref[:, cols].astype(jnp.float32)
        gv = gv + jnp.dot(k, qg_high, preferred_element_type=jnp.float32)
        gv = gv + jnp.dot(k, qg_low, preferred_element_type=jnp.float32)
        gk_ref[:, cols] = gk.astype(jnp.bfloat16)
        gv_ref[:, cols] = gv.astype(jnp.bfloat16)


def attention_part(q, k, v, g, kv_state, blocks, block_len, heads, scale):
    per_step = 2 if heads % 2 == 0 else 1
    tok = pl.BlockSpec((block_len, DH * per_step), lambda n, h: (n, h))
    st = pl.BlockSpec((1, per_step, DH, DH), lambda n, h: (n, h, 0, 0))
    rows, width = q.shape
    out = jax.ShapeDtypeStruct((rows, width), jnp.bfloat16)
    return pl.pallas_call(
        lambda *refs: scores_kernel(scale, per_step, *refs),
        grid=(blocks, heads // per_step),
        in_specs=[tok, tok, tok, tok, st],
        out_specs=[tok, tok, tok],
        out_shape=[out, out, out],
        cost_estimate=pl.CostEstimate(
            flops=blocks * heads * 6 * 2 * block_len * block_len * DH,
            transcendentals=0,
            bytes_accessed=rows * width * 14,
        ),
        name="attention_part",
    )(q, k, v, g, kv_state)


def state_part(k, v, qg_state, parts, blocks, block_len, heads, scale, first=None, into=None):
    count = qg_state.shape[1]
    per_step = 4 if count % 4 == 0 and count > 4 else (2 if count % 2 == 0 else 1)
    rows, width = k.shape
    if first is None:
        first = jnp.zeros((), jnp.int32)
    offset = jnp.reshape(first // per_step, (1,)).astype(jnp.int32)
    tok = pl.BlockSpec((block_len, DH * per_step), lambda n, h, o: (n, h + o[0]))
    st = pl.BlockSpec((1, per_step, DH, DH), lambda n, h, o: (n, h, 0, 0))
    out = jax.ShapeDtypeStruct((rows, width), jnp.bfloat16)
    operands = [offset, k, v, qg_state, *parts]
    in_specs = [tok, tok, st, tok, tok]
    aliases = {}
    kernel = lambda o, *refs: state_kernel(scale, per_step, *refs)
    if into is not None:
        operands += list(into)
        in_specs += [pl.BlockSpec(memory_space=pl.ANY)] * 2
        aliases = {6: 0, 7: 1}
        kernel = lambda o, *refs: state_kernel(scale, per_step, *refs[:5], *refs[7:])
    return pl.pallas_call(
        kernel,
        grid_spec=pltpu.PrefetchScalarGridSpec(
            num_scalar_prefetch=1,
            grid=(blocks, count // per_step),
            in_specs=in_specs,
            out_specs=[tok, tok],
        ),
        out_shape=[out, out],
        input_output_aliases=aliases,
        cost_estimate=pl.CostEstimate(
            flops=blocks * count * 4 * 2 * block_len * DH * DH,
            transcendentals=0,
            bytes_accessed=rows * DH * count * 12,
        ),
        name="state_part",
    )(*operands)


def make_shards(ctx_size, head_size):
    def shards(queries, keys, values, output_grad, out_weight):
        row_count = queries.shape[0]
        width = queries.shape[1]
        heads = width // DH
        block_len = min(row_count, 512)
        blocks = row_count // block_len
        scale_factor = DH ** (-0.5)
        shape = (blocks, block_len, heads, DH)
        q_blocks = queries.reshape(shape)
        k_blocks = keys.reshape(shape)
        v_blocks = values.reshape(shape)
        kv_blocks = jnp.einsum(
            "nshd,nshe->nhde", k_blocks, v_blocks,
            preferred_element_type=jnp.float32,
        )
        kv_running = jnp.cumsum(kv_blocks, axis=0)
        kv_before, _ = ctx_exclusive(kv_running[-1], ctx_size, False)
        if blocks == 1:
            kv_entry = kv_before[None]
        else:
            kv_entry = kv_before[None] + kv_running - kv_blocks
        grad_heads, kv_entry = project(output_grad, out_weight, ctx_size, head_size, kv_entry)
        grad_heads = grad_heads.astype(jnp.bfloat16)
        g_blocks = grad_heads.reshape(shape)
        qg_blocks = jnp.einsum(
            "nthd,nthe->nhde", q_blocks, g_blocks, preferred_element_type=jnp.float32
        )
        qg_running = jnp.flip(jnp.cumsum(jnp.flip(qg_blocks, 0), axis=0), 0)
        split = blocks == 1 and heads % 2 == 0
        qg_after, (gq, gk_part, gv_part) = ctx_exclusive(
            qg_running[0], ctx_size, True,
            Cover(
                lambda g, kv: attention_part(
                    queries, keys, values, g, kv, blocks, block_len, heads, scale_factor
                ),
                (grad_heads, kv_entry),
            ),
            by_heads=split,
        )
        if split:
            own, theirs, other_partner = qg_after
            half = heads // 2
            core = lax.axis_index("ctx") % 2
            gk, gv = state_part(
                keys, values, own[None], (gk_part, gv_part), blocks, block_len, heads,
                scale_factor, first=core * half,
            )
            theirs, gk, gv = lax.optimization_barrier((theirs, gk, gv))
            other = theirs + other_partner
            gk, gv = state_part(
                keys, values, other[None], (gk_part, gv_part), blocks, block_len, heads,
                scale_factor, first=(1 - core) * half, into=(gk, gv),
            )
            return gq, gk, gv
        if blocks == 1:
            qg_entry = qg_after[None]
        else:
            qg_entry = qg_after[None] + qg_running - qg_blocks
        gk, gv = state_part(
            keys, values, qg_entry, (gk_part, gv_part), blocks, block_len, heads, scale_factor
        )
        return gq, gk, gv

    return shards


def solution(mesh):
    return jax.shard_map(
        make_shards(mesh.shape["ctx"], mesh.shape["head"]),
        mesh=mesh,
        in_specs=(
            P("ctx", "head"),
            P("ctx", "head"),
            P("ctx", "head"),
            P("ctx", "head"),
            P("head", None),
        ),
        out_specs=(P("ctx", "head"), P("ctx", "head"), P("ctx", "head")),
        check_vma=False,
    )
```

```python
import jax
import jax.numpy as jnp
from jax import lax
from jax.experimental import pallas as pl
from jax.sharding import PartitionSpec as P

DH = 128


def flip_pairs(n, bit):
    return [(a, a ^ bit) for a in range(n)]


def project(og, out_weight, ctx_size, head_size, tied):
    cols = og.shape[1]

    def weight_cols(source, lo, width):
        return lax.dynamic_slice_in_dim(out_weight, source * cols + lo, width, axis=1)

    def mm(a, b):
        return lax.dot_general(
            a, b, (((1,), (1,)), ((), ())), preferred_element_type=jnp.float32
        )

    if head_size != 4:
        full = lax.all_gather(og, "head", axis=1, tiled=True)
        full, tied = lax.optimization_barrier((full, tied))
        return mm(full, out_weight), tied
    me = lax.axis_index("head")
    core = lax.axis_index("ctx") % 2
    devices = [(p, j) for p in range(ctx_size) for j in range(4)]

    def route(core_0_bit, core_1_bit):
        return [(p * 4 + j, p * 4 + (j ^ (core_0_bit if p % 2 == 0 else core_1_bit))) for p, j in devices]

    to_relay = lax.ppermute(og, ("ctx", "head"), route(1, 2))
    kept = lax.ppermute(og, ("ctx", "head"), route(2, 1))
    diag = lax.ppermute(to_relay, ("ctx", "head"), route(2, 1))
    diag, tied = lax.optimization_barrier((diag, tied))
    acc = mm(og, weight_cols(me, 0, cols))
    acc = acc + mm(to_relay, weight_cols(me ^ (1 + core), 0, cols))
    acc = acc + mm(kept, weight_cols(me ^ (2 - core), 0, cols))
    acc = acc + mm(diag, weight_cols(me ^ 3, 0, cols))
    return acc, tied


def ctx_exclusive(state, ctx_size, reverse, cover=None):
    core = lax.axis_index("ctx") % 2
    chips = ctx_size // 2
    rounded = state.astype(jnp.bfloat16)
    partner = lax.ppermute(rounded, "ctx", flip_pairs(ctx_size, 1)).astype(jnp.float32)
    chip_sum = rounded.astype(jnp.float32) + partner
    half = state.shape[1] // 2
    mine = lax.dynamic_slice_in_dim(chip_sum, core * half, half, axis=1)

    def pairs(step):
        if reverse:
            return [(2 * (z + step) + c, 2 * z + c) for z in range(chips - step) for c in range(2)]
        return [(2 * z + c, 2 * (z + step) + c) for z in range(chips - step) for c in range(2)]

    if cover is not None:
        mine, held = lax.optimization_barrier((mine, cover.args))
    others = jnp.zeros_like(mine)
    if chips <= 4:
        sent = mine.astype(jnp.bfloat16)
        for step in range(1, chips):
            others = others + lax.ppermute(sent, "ctx", pairs(step)).astype(jnp.float32)
    else:
        run = mine
        step = 1
        while step < chips:
            got = lax.ppermute(run.astype(jnp.bfloat16), "ctx", pairs(step)).astype(jnp.float32)
            run = run + got
            others = others + got
            step *= 2
    covered = None
    if cover is not None:
        covered = cover.fn(*held)
        others, covered = lax.optimization_barrier((others, covered))
    theirs = lax.ppermute(others.astype(jnp.bfloat16), "ctx", flip_pairs(ctx_size, 1))
    theirs = theirs.astype(jnp.float32)
    lower = jnp.where(core == 0, others, theirs)
    upper = jnp.where(core == 0, theirs, others)
    chips_side = jnp.concatenate([lower, upper], axis=1)
    same_chip = (core == 0) if reverse else (core == 1)
    return chips_side + jnp.where(same_chip, partner, 0.0), covered


class Cover:
    def __init__(self, fn, args):
        self.fn = fn
        self.args = args


NT = (((1,), (1,)), ((), ()))
TN = (((0,), (0,)), ((), ()))


def split_state(state):
    high = state.astype(jnp.bfloat16)
    low = (state - high.astype(jnp.float32)).astype(jnp.bfloat16)
    return high, low


def scores_kernel(scale, per_step, q_ref, k_ref, v_ref, g_ref, kv_ref, gq_ref, gk_ref, gv_ref):
    length = q_ref.shape[0]
    row = lax.broadcasted_iota(jnp.int32, (length, length), 0)
    col = lax.broadcasted_iota(jnp.int32, (length, length), 1)
    lower = row >= col
    for h in range(per_step):
        cols = pl.ds(h * DH, DH)
        q, k, v, g = q_ref[:, cols], k_ref[:, cols], v_ref[:, cols], g_ref[:, cols]
        kv_high, kv_low = split_state(kv_ref[0, h] * scale)
        score_grad = lax.dot_general(g, v, NT, preferred_element_type=jnp.float32) * scale
        score_grad = jnp.where(lower, score_grad, 0.0).astype(jnp.bfloat16)
        score_fwd = lax.dot_general(q, k, NT, preferred_element_type=jnp.float32) * scale
        score_fwd = jnp.where(lower, score_fwd, 0.0).astype(jnp.bfloat16)
        gq = lax.dot_general(g, kv_high, NT, preferred_element_type=jnp.float32)
        gq = gq + lax.dot_general(g, kv_low, NT, preferred_element_type=jnp.float32)
        gq = gq + jnp.dot(score_grad, k, preferred_element_type=jnp.float32)
        gq_ref[:, cols] = gq.astype(gq_ref.dtype)
        gk_t = lax.dot_general(q, score_grad, TN, preferred_element_type=jnp.float32)
        gv_t = lax.dot_general(g, score_fwd, TN, preferred_element_type=jnp.float32)
        gk_ref[:, cols] = gk_t.T.astype(gk_ref.dtype)
        gv_ref[:, cols] = gv_t.T.astype(gv_ref.dtype)


def state_kernel(scale, per_step, k_ref, v_ref, qg_ref, gkp_ref, gvp_ref, gk_ref, gv_ref):
    for i in range(per_step):
        cols = pl.ds(i * DH, DH)
        k, v = k_ref[:, cols], v_ref[:, cols]
        qg_high, qg_low = split_state(qg_ref[0, i] * scale)
        gk = gkp_ref[:, cols].astype(jnp.float32)
        gk = gk + lax.dot_general(v, qg_high, NT, preferred_element_type=jnp.float32)
        gk = gk + lax.dot_general(v, qg_low, NT, preferred_element_type=jnp.float32)
        gv = gvp_ref[:, cols].astype(jnp.float32)
        gv = gv + jnp.dot(k, qg_high, preferred_element_type=jnp.float32)
        gv = gv + jnp.dot(k, qg_low, preferred_element_type=jnp.float32)
        gk_ref[:, cols] = gk.astype(jnp.bfloat16)
        gv_ref[:, cols] = gv.astype(jnp.bfloat16)


def attention_part(q, k, v, g, kv_state, blocks, block_len, heads, scale):
    per_step = 2 if heads % 2 == 0 else 1
    tok = pl.BlockSpec((block_len, DH * per_step), lambda n, h: (n, h))
    st = pl.BlockSpec((1, per_step, DH, DH), lambda n, h: (n, h, 0, 0))
    rows, width = q.shape
    out = jax.ShapeDtypeStruct((rows, width), jnp.bfloat16)
    return pl.pallas_call(
        lambda *refs: scores_kernel(scale, per_step, *refs),
        grid=(blocks, heads // per_step),
        in_specs=[tok, tok, tok, tok, st],
        out_specs=[tok, tok, tok],
        out_shape=[out, out, out],
        cost_estimate=pl.CostEstimate(
            flops=blocks * heads * 6 * 2 * block_len * block_len * DH,
            transcendentals=0,
            bytes_accessed=rows * width * 14,
        ),
        name="attention_part",
    )(q, k, v, g, kv_state)


def state_part(k, v, qg_state, parts, blocks, block_len, heads, scale):
    per_step = 4 if heads % 4 == 0 else (2 if heads % 2 == 0 else 1)
    tok = pl.BlockSpec((block_len, DH * per_step), lambda n, h: (n, h))
    st = pl.BlockSpec((1, per_step, DH, DH), lambda n, h: (n, h, 0, 0))
    rows, width = k.shape
    out = jax.ShapeDtypeStruct((rows, width), jnp.bfloat16)
    return pl.pallas_call(
        lambda *refs: state_kernel(scale, per_step, *refs),
        grid=(blocks, heads // per_step),
        in_specs=[tok, tok, st, tok, tok],
        out_specs=[tok, tok],
        out_shape=[out, out],
        cost_estimate=pl.CostEstimate(
            flops=blocks * heads * 4 * 2 * block_len * DH * DH,
            transcendentals=0,
            bytes_accessed=rows * width * 12,
        ),
        name="state_part",
    )(k, v, qg_state, *parts)


def make_shards(ctx_size, head_size):
    def shards(queries, keys, values, output_grad, out_weight):
        row_count = queries.shape[0]
        width = queries.shape[1]
        heads = width // DH
        block_len = min(row_count, 512)
        blocks = row_count // block_len
        scale_factor = DH ** (-0.5)
        shape = (blocks, block_len, heads, DH)
        q_blocks = queries.reshape(shape)
        k_blocks = keys.reshape(shape)
        v_blocks = values.reshape(shape)
        kv_blocks = jnp.einsum(
            "nshd,nshe->nhde", k_blocks, v_blocks,
            preferred_element_type=jnp.float32,
        )
        kv_running = jnp.cumsum(kv_blocks, axis=0)
        kv_before, _ = ctx_exclusive(kv_running[-1], ctx_size, False)
        if blocks == 1:
            kv_entry = kv_before[None]
        else:
            kv_entry = kv_before[None] + kv_running - kv_blocks
        grad_heads, kv_entry = project(output_grad, out_weight, ctx_size, head_size, kv_entry)
        grad_heads = grad_heads.astype(jnp.bfloat16)
        g_blocks = grad_heads.reshape(shape)
        qg_blocks = jnp.einsum(
            "nthd,nthe->nhde", q_blocks, g_blocks, preferred_element_type=jnp.float32
        )
        qg_running = jnp.flip(jnp.cumsum(jnp.flip(qg_blocks, 0), axis=0), 0)
        qg_after, (gq, gk_part, gv_part) = ctx_exclusive(
            qg_running[0], ctx_size, True,
            Cover(
                lambda g, kv: attention_part(
                    queries, keys, values, g, kv, blocks, block_len, heads, scale_factor
                ),
                (grad_heads, kv_entry),
            ),
        )
        if blocks == 1:
            qg_entry = qg_after[None]
        else:
            qg_entry = qg_after[None] + qg_running - qg_blocks
        gk, gv = state_part(
            keys, values, qg_entry, (gk_part, gv_part), blocks, block_len, heads, scale_factor
        )
        return gq, gk, gv

    return shards


def solution(mesh):
    return jax.shard_map(
        make_shards(mesh.shape["ctx"], mesh.shape["head"]),
        mesh=mesh,
        in_specs=(
            P("ctx", "head"),
            P("ctx", "head"),
            P("ctx", "head"),
            P("ctx", "head"),
            P("head", None),
        ),
        out_specs=(P("ctx", "head"), P("ctx", "head"), P("ctx", "head")),
        check_vma=False,
    )
```

```python
import jax
import jax.numpy as jnp
from jax import lax
from jax.experimental import pallas as pl
from jax.experimental.pallas import tpu as pltpu
from jax.sharding import PartitionSpec as P

DH = 128


def flip_pairs(n, bit):
    return [(a, a ^ bit) for a in range(n)]


def project(og, out_weight, ctx_size, head_size, tied):
    cols = og.shape[1]

    def weight_cols(source, lo, width):
        return lax.dynamic_slice_in_dim(out_weight, source * cols + lo, width, axis=1)

    def mm(a, b):
        return lax.dot_general(
            a, b, (((1,), (1,)), ((), ())), preferred_element_type=jnp.float32
        )

    if head_size != 4:
        full = lax.all_gather(og, "head", axis=1, tiled=True)
        full, tied = lax.optimization_barrier((full, tied))
        return mm(full, out_weight), tied
    me = lax.axis_index("head")
    core = lax.axis_index("ctx") % 2
    devices = [(p, j) for p in range(ctx_size) for j in range(4)]

    def route(core_0_bit, core_1_bit):
        return [(p * 4 + j, p * 4 + (j ^ (core_0_bit if p % 2 == 0 else core_1_bit))) for p, j in devices]

    to_relay = lax.ppermute(og, ("ctx", "head"), route(1, 2))
    kept = lax.ppermute(og, ("ctx", "head"), route(2, 1))
    diag = lax.ppermute(to_relay, ("ctx", "head"), route(2, 1))
    diag, tied = lax.optimization_barrier((diag, tied))
    acc = mm(og, weight_cols(me, 0, cols))
    acc = acc + mm(to_relay, weight_cols(me ^ (1 + core), 0, cols))
    acc = acc + mm(kept, weight_cols(me ^ (2 - core), 0, cols))
    acc = acc + mm(diag, weight_cols(me ^ 3, 0, cols))
    return acc, tied


def ctx_exclusive(state, ctx_size, reverse, cover=None, unassembled=False):
    core = lax.axis_index("ctx") % 2
    chips = ctx_size // 2
    rounded = state.astype(jnp.bfloat16)
    partner = lax.ppermute(rounded, "ctx", flip_pairs(ctx_size, 1)).astype(jnp.float32)
    chip_sum = rounded.astype(jnp.float32) + partner
    half = state.shape[1] // 2
    mine = lax.dynamic_slice_in_dim(chip_sum, core * half, half, axis=1)

    def pairs(step):
        if reverse:
            return [(2 * (z + step) + c, 2 * z + c) for z in range(chips - step) for c in range(2)]
        return [(2 * z + c, 2 * (z + step) + c) for z in range(chips - step) for c in range(2)]

    if cover is not None:
        mine, held = lax.optimization_barrier((mine, cover.args))
    others = jnp.zeros_like(mine)
    if chips <= 4:
        sent = mine.astype(jnp.bfloat16)
        for step in range(1, chips):
            others = others + lax.ppermute(sent, "ctx", pairs(step)).astype(jnp.float32)
    else:
        run = mine
        step = 1
        while step < chips:
            got = lax.ppermute(run.astype(jnp.bfloat16), "ctx", pairs(step)).astype(jnp.float32)
            run = run + got
            others = others + got
            step *= 2
    covered = None
    if cover is not None:
        covered = cover.fn(*held)
        others, covered = lax.optimization_barrier((others, covered))
    theirs = lax.ppermute(others.astype(jnp.bfloat16), "ctx", flip_pairs(ctx_size, 1))
    same_chip = (core == 0) if reverse else (core == 1)
    if unassembled:
        base = jnp.where(same_chip, partner, 0.0)
        base = lax.dynamic_update_slice_in_dim(
            base, lax.dynamic_slice_in_dim(base, core * half, half, axis=1) + others, core * half, axis=1
        )
        return (base, theirs), covered
    theirs = theirs.astype(jnp.float32)
    lower = jnp.where(core == 0, others, theirs)
    upper = jnp.where(core == 0, theirs, others)
    chips_side = jnp.concatenate([lower, upper], axis=1)
    same_chip = (core == 0) if reverse else (core == 1)
    return chips_side + jnp.where(same_chip, partner, 0.0), covered


class Cover:
    def __init__(self, fn, args):
        self.fn = fn
        self.args = args


NT = (((1,), (1,)), ((), ()))
TN = (((0,), (0,)), ((), ()))


def split_state(state):
    high = state.astype(jnp.bfloat16)
    low = (state - high.astype(jnp.float32)).astype(jnp.bfloat16)
    return high, low


def scores_kernel(scale, per_step, q_ref, k_ref, v_ref, g_ref, kv_ref, gq_ref, gk_ref, gv_ref):
    length = q_ref.shape[0]
    row = lax.broadcasted_iota(jnp.int32, (length, length), 0)
    col = lax.broadcasted_iota(jnp.int32, (length, length), 1)
    lower = row >= col
    for h in range(per_step):
        cols = pl.ds(h * DH, DH)
        q, k, v, g = q_ref[:, cols], k_ref[:, cols], v_ref[:, cols], g_ref[:, cols]
        kv_high, kv_low = split_state(kv_ref[0, h] * scale)
        score_grad = lax.dot_general(g, v, NT, preferred_element_type=jnp.float32) * scale
        score_grad = jnp.where(lower, score_grad, 0.0).astype(jnp.bfloat16)
        score_fwd = lax.dot_general(q, k, NT, preferred_element_type=jnp.float32) * scale
        score_fwd = jnp.where(lower, score_fwd, 0.0).astype(jnp.bfloat16)
        gq = lax.dot_general(g, kv_high, NT, preferred_element_type=jnp.float32)
        gq = gq + lax.dot_general(g, kv_low, NT, preferred_element_type=jnp.float32)
        gq = gq + jnp.dot(score_grad, k, preferred_element_type=jnp.float32)
        gq_ref[:, cols] = gq.astype(gq_ref.dtype)
        gk_t = lax.dot_general(q, score_grad, TN, preferred_element_type=jnp.float32)
        gv_t = lax.dot_general(g, score_fwd, TN, preferred_element_type=jnp.float32)
        gk_ref[:, cols] = gk_t.T.astype(gk_ref.dtype)
        gv_ref[:, cols] = gv_t.T.astype(gv_ref.dtype)


def state_kernel(scale, per_step, k_ref, v_ref, qg_ref, gkp_ref, gvp_ref, gk_ref, gv_ref,
                 core_ref=None, theirs_ref=None):
    for i in range(per_step):
        cols = pl.ds(i * DH, DH)
        k, v = k_ref[:, cols], v_ref[:, cols]
        qg = qg_ref[0, i]
        if theirs_ref is not None:
            part = theirs_ref[0, i].astype(jnp.float32)
            part = jnp.concatenate([part, part], axis=0)
            row = lax.broadcasted_iota(jnp.int32, qg.shape, 0)
            qg = qg + jnp.where((row * 2) // qg.shape[0] != core_ref[0], part, 0.0)
        qg_high, qg_low = split_state(qg * scale)
        gk = gkp_ref[:, cols].astype(jnp.float32)
        gk = gk + lax.dot_general(v, qg_high, NT, preferred_element_type=jnp.float32)
        gk = gk + lax.dot_general(v, qg_low, NT, preferred_element_type=jnp.float32)
        gv = gvp_ref[:, cols].astype(jnp.float32)
        gv = gv + jnp.dot(k, qg_high, preferred_element_type=jnp.float32)
        gv = gv + jnp.dot(k, qg_low, preferred_element_type=jnp.float32)
        gk_ref[:, cols] = gk.astype(jnp.bfloat16)
        gv_ref[:, cols] = gv.astype(jnp.bfloat16)


def attention_part(q, k, v, g, kv_state, blocks, block_len, heads, scale):
    per_step = 2 if heads % 2 == 0 else 1
    tok = pl.BlockSpec((block_len, DH * per_step), lambda n, h: (n, h))
    st = pl.BlockSpec((1, per_step, DH, DH), lambda n, h: (n, h, 0, 0))
    rows, width = q.shape
    out = jax.ShapeDtypeStruct((rows, width), jnp.bfloat16)
    return pl.pallas_call(
        lambda *refs: scores_kernel(scale, per_step, *refs),
        grid=(blocks, heads // per_step),
        in_specs=[tok, tok, tok, tok, st],
        out_specs=[tok, tok, tok],
        out_shape=[out, out, out],
        cost_estimate=pl.CostEstimate(
            flops=blocks * heads * 6 * 2 * block_len * block_len * DH,
            transcendentals=0,
            bytes_accessed=rows * width * 14,
        ),
        name="attention_part",
    )(q, k, v, g, kv_state)


def state_part(k, v, qg_state, parts, blocks, block_len, heads, scale, theirs=None):
    per_step = 4 if heads % 4 == 0 else (2 if heads % 2 == 0 else 1)
    rows, width = k.shape
    out = jax.ShapeDtypeStruct((rows, width), jnp.bfloat16)
    cost = pl.CostEstimate(
        flops=blocks * heads * 4 * 2 * block_len * DH * DH,
        transcendentals=0,
        bytes_accessed=rows * width * 12,
    )
    if theirs is None:
        tok = pl.BlockSpec((block_len, DH * per_step), lambda n, h: (n, h))
        st = pl.BlockSpec((1, per_step, DH, DH), lambda n, h: (n, h, 0, 0))
        return pl.pallas_call(
            lambda *refs: state_kernel(scale, per_step, *refs),
            grid=(blocks, heads // per_step),
            in_specs=[tok, tok, st, tok, tok],
            out_specs=[tok, tok],
            out_shape=[out, out],
            cost_estimate=cost,
            name="state_part",
        )(k, v, qg_state, *parts)
    tok = pl.BlockSpec((block_len, DH * per_step), lambda n, h, c: (n, h))
    st = pl.BlockSpec((1, per_step, DH, DH), lambda n, h, c: (n, h, 0, 0))
    half = pl.BlockSpec((1, per_step, DH // 2, DH), lambda n, h, c: (n, h, 0, 0))
    core = jnp.reshape(lax.axis_index("ctx") % 2, (1,)).astype(jnp.int32)

    def kernel(core_ref, k_ref, v_ref, qg_ref, gkp_ref, gvp_ref, theirs_ref, gk_ref, gv_ref):
        state_kernel(scale, per_step, k_ref, v_ref, qg_ref, gkp_ref, gvp_ref, gk_ref, gv_ref,
                     core_ref=core_ref, theirs_ref=theirs_ref)

    return pl.pallas_call(
        kernel,
        grid_spec=pltpu.PrefetchScalarGridSpec(
            num_scalar_prefetch=1,
            grid=(blocks, heads // per_step),
            in_specs=[tok, tok, st, tok, tok, half],
            out_specs=[tok, tok],
        ),
        out_shape=[out, out],
        cost_estimate=cost,
        name="state_part",
    )(core, k, v, qg_state, *parts, theirs)


def make_shards(ctx_size, head_size):
    def shards(queries, keys, values, output_grad, out_weight):
        row_count = queries.shape[0]
        width = queries.shape[1]
        heads = width // DH
        block_len = min(row_count, 512)
        blocks = row_count // block_len
        scale_factor = DH ** (-0.5)
        shape = (blocks, block_len, heads, DH)
        q_blocks = queries.reshape(shape)
        k_blocks = keys.reshape(shape)
        v_blocks = values.reshape(shape)
        kv_blocks = jnp.einsum(
            "nshd,nshe->nhde", k_blocks, v_blocks,
            preferred_element_type=jnp.float32,
        )
        kv_running = jnp.cumsum(kv_blocks, axis=0)
        kv_before, _ = ctx_exclusive(kv_running[-1], ctx_size, False)
        if blocks == 1:
            kv_entry = kv_before[None]
        else:
            kv_entry = kv_before[None] + kv_running - kv_blocks
        grad_heads, kv_entry = project(output_grad, out_weight, ctx_size, head_size, kv_entry)
        grad_heads = grad_heads.astype(jnp.bfloat16)
        g_blocks = grad_heads.reshape(shape)
        qg_blocks = jnp.einsum(
            "nthd,nthe->nhde", q_blocks, g_blocks, preferred_element_type=jnp.float32
        )
        qg_running = jnp.flip(jnp.cumsum(jnp.flip(qg_blocks, 0), axis=0), 0)
        qg_after, (gq, gk_part, gv_part) = ctx_exclusive(
            qg_running[0], ctx_size, True,
            Cover(
                lambda g, kv: attention_part(
                    queries, keys, values, g, kv, blocks, block_len, heads, scale_factor
                ),
                (grad_heads, kv_entry),
            ),
            unassembled=blocks == 1,
        )
        if blocks == 1:
            base, theirs = qg_after
            gk, gv = state_part(
                keys, values, base[None], (gk_part, gv_part), blocks, block_len, heads,
                scale_factor, theirs=theirs[None],
            )
            return gq, gk, gv
        qg_entry = qg_after[None] + qg_running - qg_blocks
        gk, gv = state_part(
            keys, values, qg_entry, (gk_part, gv_part), blocks, block_len, heads, scale_factor
        )
        return gq, gk, gv

    return shards


def solution(mesh):
    return jax.shard_map(
        make_shards(mesh.shape["ctx"], mesh.shape["head"]),
        mesh=mesh,
        in_specs=(
            P("ctx", "head"),
            P("ctx", "head"),
            P("ctx", "head"),
            P("ctx", "head"),
            P("head", None),
        ),
        out_specs=(P("ctx", "head"), P("ctx", "head"), P("ctx", "head")),
        check_vma=False,
    )
```

```python
import jax
import jax.numpy as jnp
from jax import lax
from jax.experimental import pallas as pl
from jax.sharding import PartitionSpec as P

DH = 128


def flip_pairs(n, bit):
    return [(a, a ^ bit) for a in range(n)]


def project(og, out_weight, ctx_size, head_size, tied):
    cols = og.shape[1]

    def weight_cols(source, lo, width):
        return lax.dynamic_slice_in_dim(out_weight, source * cols + lo, width, axis=1)

    def mm(a, b):
        return lax.dot_general(
            a, b, (((1,), (1,)), ((), ())), preferred_element_type=jnp.float32
        )

    if head_size != 4:
        full = lax.all_gather(og, "head", axis=1, tiled=True)
        full, tied = lax.optimization_barrier((full, tied))
        return mm(full, out_weight), tied
    me = lax.axis_index("head")
    core = lax.axis_index("ctx") % 2
    devices = [(p, j) for p in range(ctx_size) for j in range(4)]

    def route(core_0_bit, core_1_bit):
        return [(p * 4 + j, p * 4 + (j ^ (core_0_bit if p % 2 == 0 else core_1_bit))) for p, j in devices]

    to_relay = lax.ppermute(og, ("ctx", "head"), route(1, 2))
    kept = lax.ppermute(og, ("ctx", "head"), route(2, 1))
    diag = lax.ppermute(to_relay, ("ctx", "head"), route(2, 1))
    diag, tied = lax.optimization_barrier((diag, tied))
    acc = mm(og, weight_cols(me, 0, cols))
    acc = acc + mm(to_relay, weight_cols(me ^ (1 + core), 0, cols))
    acc = acc + mm(kept, weight_cols(me ^ (2 - core), 0, cols))
    acc = acc + mm(diag, weight_cols(me ^ 3, 0, cols))
    return acc, tied


def ctx_exclusive(state, ctx_size, reverse, cover=None):
    core = lax.axis_index("ctx") % 2
    chips = ctx_size // 2
    rounded = state.astype(jnp.bfloat16)
    half = state.shape[1] // 2
    swap = flip_pairs(ctx_size, 1)
    near = lax.ppermute(
        lax.dynamic_slice_in_dim(rounded, (1 - core) * half, half, axis=1), "ctx", swap
    ).astype(jnp.float32)
    mine = lax.dynamic_slice_in_dim(rounded, core * half, half, axis=1).astype(jnp.float32) + near
    far = lax.ppermute(
        lax.dynamic_slice_in_dim(rounded, core * half, half, axis=1), "ctx", swap
    ).astype(jnp.float32)
    partner = jnp.where(
        core == 0, jnp.concatenate([near, far], axis=1), jnp.concatenate([far, near], axis=1)
    )

    def pairs(step):
        if reverse:
            return [(2 * (z + step) + c, 2 * z + c) for z in range(chips - step) for c in range(2)]
        return [(2 * z + c, 2 * (z + step) + c) for z in range(chips - step) for c in range(2)]

    if cover is not None:
        mine, held = lax.optimization_barrier((mine, cover.args))
    others = jnp.zeros_like(mine)
    if chips <= 4:
        sent = mine.astype(jnp.bfloat16)
        for step in range(1, chips):
            others = others + lax.ppermute(sent, "ctx", pairs(step)).astype(jnp.float32)
    else:
        run = mine
        step = 1
        while step < chips:
            got = lax.ppermute(run.astype(jnp.bfloat16), "ctx", pairs(step)).astype(jnp.float32)
            run = run + got
            others = others + got
            step *= 2
    covered = None
    if cover is not None:
        covered = cover.fn(*held)
        others, covered = lax.optimization_barrier((others, covered))
    theirs = lax.ppermute(others.astype(jnp.bfloat16), "ctx", flip_pairs(ctx_size, 1))
    theirs = theirs.astype(jnp.float32)
    lower = jnp.where(core == 0, others, theirs)
    upper = jnp.where(core == 0, theirs, others)
    chips_side = jnp.concatenate([lower, upper], axis=1)
    same_chip = (core == 0) if reverse else (core == 1)
    return chips_side + jnp.where(same_chip, partner, 0.0), covered


class Cover:
    def __init__(self, fn, args):
        self.fn = fn
        self.args = args


NT = (((1,), (1,)), ((), ()))
TN = (((0,), (0,)), ((), ()))


def split_state(state):
    high = state.astype(jnp.bfloat16)
    low = (state - high.astype(jnp.float32)).astype(jnp.bfloat16)
    return high, low


def scores_kernel(scale, per_step, q_ref, k_ref, v_ref, g_ref, kv_ref, gq_ref, gk_ref, gv_ref):
    length = q_ref.shape[0]
    row = lax.broadcasted_iota(jnp.int32, (length, length), 0)
    col = lax.broadcasted_iota(jnp.int32, (length, length), 1)
    lower = row >= col
    for h in range(per_step):
        cols = pl.ds(h * DH, DH)
        q, k, v, g = q_ref[:, cols], k_ref[:, cols], v_ref[:, cols], g_ref[:, cols]
        kv_high, kv_low = split_state(kv_ref[0, h] * scale)
        score_grad = lax.dot_general(g, v, NT, preferred_element_type=jnp.float32) * scale
        score_grad = jnp.where(lower, score_grad, 0.0).astype(jnp.bfloat16)
        score_fwd = lax.dot_general(q, k, NT, preferred_element_type=jnp.float32) * scale
        score_fwd = jnp.where(lower, score_fwd, 0.0).astype(jnp.bfloat16)
        gq = lax.dot_general(g, kv_high, NT, preferred_element_type=jnp.float32)
        gq = gq + lax.dot_general(g, kv_low, NT, preferred_element_type=jnp.float32)
        gq = gq + jnp.dot(score_grad, k, preferred_element_type=jnp.float32)
        gq_ref[:, cols] = gq.astype(gq_ref.dtype)
        gk_t = lax.dot_general(q, score_grad, TN, preferred_element_type=jnp.float32)
        gv_t = lax.dot_general(g, score_fwd, TN, preferred_element_type=jnp.float32)
        gk_ref[:, cols] = gk_t.T.astype(gk_ref.dtype)
        gv_ref[:, cols] = gv_t.T.astype(gv_ref.dtype)


def state_kernel(scale, per_step, k_ref, v_ref, qg_ref, gkp_ref, gvp_ref, gk_ref, gv_ref):
    for i in range(per_step):
        cols = pl.ds(i * DH, DH)
        k, v = k_ref[:, cols], v_ref[:, cols]
        qg_high, qg_low = split_state(qg_ref[0, i] * scale)
        gk = gkp_ref[:, cols].astype(jnp.float32)
        gk = gk + lax.dot_general(v, qg_high, NT, preferred_element_type=jnp.float32)
        gk = gk + lax.dot_general(v, qg_low, NT, preferred_element_type=jnp.float32)
        gv = gvp_ref[:, cols].astype(jnp.float32)
        gv = gv + jnp.dot(k, qg_high, preferred_element_type=jnp.float32)
        gv = gv + jnp.dot(k, qg_low, preferred_element_type=jnp.float32)
        gk_ref[:, cols] = gk.astype(jnp.bfloat16)
        gv_ref[:, cols] = gv.astype(jnp.bfloat16)


def attention_part(q, k, v, g, kv_state, blocks, block_len, heads, scale):
    per_step = 2 if heads % 2 == 0 else 1
    tok = pl.BlockSpec((block_len, DH * per_step), lambda n, h: (n, h))
    st = pl.BlockSpec((1, per_step, DH, DH), lambda n, h: (n, h, 0, 0))
    rows, width = q.shape
    out = jax.ShapeDtypeStruct((rows, width), jnp.bfloat16)
    return pl.pallas_call(
        lambda *refs: scores_kernel(scale, per_step, *refs),
        grid=(blocks, heads // per_step),
        in_specs=[tok, tok, tok, tok, st],
        out_specs=[tok, tok, tok],
        out_shape=[out, out, out],
        cost_estimate=pl.CostEstimate(
            flops=blocks * heads * 6 * 2 * block_len * block_len * DH,
            transcendentals=0,
            bytes_accessed=rows * width * 14,
        ),
        name="attention_part",
    )(q, k, v, g, kv_state)


def state_part(k, v, qg_state, parts, blocks, block_len, heads, scale):
    per_step = 4 if heads % 4 == 0 else (2 if heads % 2 == 0 else 1)
    tok = pl.BlockSpec((block_len, DH * per_step), lambda n, h: (n, h))
    st = pl.BlockSpec((1, per_step, DH, DH), lambda n, h: (n, h, 0, 0))
    rows, width = k.shape
    out = jax.ShapeDtypeStruct((rows, width), jnp.bfloat16)
    return pl.pallas_call(
        lambda *refs: state_kernel(scale, per_step, *refs),
        grid=(blocks, heads // per_step),
        in_specs=[tok, tok, st, tok, tok],
        out_specs=[tok, tok],
        out_shape=[out, out],
        cost_estimate=pl.CostEstimate(
            flops=blocks * heads * 4 * 2 * block_len * DH * DH,
            transcendentals=0,
            bytes_accessed=rows * width * 12,
        ),
        name="state_part",
    )(k, v, qg_state, *parts)


def make_shards(ctx_size, head_size):
    def shards(queries, keys, values, output_grad, out_weight):
        row_count = queries.shape[0]
        width = queries.shape[1]
        heads = width // DH
        block_len = min(row_count, 512)
        blocks = row_count // block_len
        scale_factor = DH ** (-0.5)
        shape = (blocks, block_len, heads, DH)
        q_blocks = queries.reshape(shape)
        k_blocks = keys.reshape(shape)
        v_blocks = values.reshape(shape)
        kv_blocks = jnp.einsum(
            "nshd,nshe->nhde", k_blocks, v_blocks,
            preferred_element_type=jnp.float32,
        )
        kv_running = jnp.cumsum(kv_blocks, axis=0)
        kv_before, _ = ctx_exclusive(kv_running[-1], ctx_size, False)
        if blocks == 1:
            kv_entry = kv_before[None]
        else:
            kv_entry = kv_before[None] + kv_running - kv_blocks
        grad_heads, kv_entry = project(output_grad, out_weight, ctx_size, head_size, kv_entry)
        grad_heads = grad_heads.astype(jnp.bfloat16)
        g_blocks = grad_heads.reshape(shape)
        qg_blocks = jnp.einsum(
            "nthd,nthe->nhde", q_blocks, g_blocks, preferred_element_type=jnp.float32
        )
        qg_running = jnp.flip(jnp.cumsum(jnp.flip(qg_blocks, 0), axis=0), 0)
        qg_after, (gq, gk_part, gv_part) = ctx_exclusive(
            qg_running[0], ctx_size, True,
            Cover(
                lambda g, kv: attention_part(
                    queries, keys, values, g, kv, blocks, block_len, heads, scale_factor
                ),
                (grad_heads, kv_entry),
            ),
        )
        if blocks == 1:
            qg_entry = qg_after[None]
        else:
            qg_entry = qg_after[None] + qg_running - qg_blocks
        gk, gv = state_part(
            keys, values, qg_entry, (gk_part, gv_part), blocks, block_len, heads, scale_factor
        )
        return gq, gk, gv

    return shards


def solution(mesh):
    return jax.shard_map(
        make_shards(mesh.shape["ctx"], mesh.shape["head"]),
        mesh=mesh,
        in_specs=(
            P("ctx", "head"),
            P("ctx", "head"),
            P("ctx", "head"),
            P("ctx", "head"),
            P("head", None),
        ),
        out_specs=(P("ctx", "head"), P("ctx", "head"), P("ctx", "head")),
        check_vma=False,
    )
```
